128 devices in a mesh: seq: 32 (over y, x, core), mp: 4 (over z).
Axes of the slice: x: 4, y: 4, z: 4, core: 2. Of those that a mesh axis runs over, the one named last changes fastest.
Arguments:
- states: bfloat16 [4, 16, 2048], P(None, None, 'mp'), may hold values from -4 to 4
- query_weight: bfloat16 [2048, 2048], P('seq', 'mp'), may hold values from -5 to 5
- key_weight: bfloat16 [2048, 2048], P('seq', 'mp'), may hold values from -5 to 5
- value_weight: bfloat16 [2048, 2048], P('seq', 'mp'), may hold values from -5 to 5
- output_weight: bfloat16 [2048, 2048], P('seq', 'mp'), may hold values from -5 to 5
- gate_weight: bfloat16 [2048, 8192], P('seq', 'mp'), may hold values from -5 to 5
- up_weight: bfloat16 [2048, 8192], P('seq', 'mp'), may hold values from -5 to 5
- down_weight: bfloat16 [8192, 2048], P('seq', 'mp'), may hold values from -5 to 5
- query_gain: float32 [2048], P('mp'), may hold values from 0.5 to 2
- key_gain: float32 [2048], P('mp'), may hold values from 0.5 to 2
- attention_gain: float32 [2048], P('mp'), may hold values from 0.1 to 1.9
- feedforward_gain: float32 [2048], P('mp'), may hold values from 0.1 to 1.9
- key_cache: bfloat16 [512, 256, 2048], P('seq', None, 'mp'), may hold values from -500 to 500
- value_cache: bfloat16 [512, 256, 2048], P('seq', None, 'mp'), may hold values from -6 to 6
- lengths: int32 [16], replicated, may hold values from 1 to 32768, as said below
- page_owner: int32 [512], P('seq'), may hold values from -1 to 15, as said below
- page_index: int32 [512], P('seq'), may hold values from 0 to 127, as said below
Outputs:
- decoded: bfloat16 [4, 16, 2048], P(None, None, 'mp')
The draws below stay inside these ranges and needn't reach their ends.
Inputs may be any that keep to these rules, and one draw needn't show every extreme that they name: Request r owns exactly ceil(lengths[r] / 256) pages. `page_owner`: on each device of seq the used pages come before the unused ones. `page_index`: the pages of one request carry the numbers 0, 1, 2 and so on, once each; unused pages carry 0.
All inputs are finite; a program needn't handle non-finite values.
Results may differ from the reference program's by a relative error of at most 0.015.
Values may be sent and summed in bfloat16 or wider, within the bound.
No kernel may reach another device: no remote copies, remote signals or barrier semaphores. Data moves between devices by JAX's collectives and lax.ppermute only.
A program may use at most 64 MiB of HBM per device.

```python
import math
import jax
import jax.numpy as jnp
from jax import lax

D = 2048
HEADS = 16
HD = 128
FF = 8192
R = 16
STEPS = 4
PAGE = 256
PAGES_DEV = 16
PAGES = 512
MAXPAGES = 128


def rising_weight(key, salt, rows, cols, spread_cols):
    first_key, second_key = jax.random.split(jax.random.fold_in(key, salt))
    base = jax.random.truncated_normal(first_key, -4.0, 4.0, (rows, cols), jnp.float32) / math.sqrt(rows)
    row_place = jnp.arange(rows, dtype=jnp.float32)[:, None] / rows
    rise_log = math.log(3.0)
    rise = jnp.exp(row_place * rise_log)
    mean_square = (math.exp(2.0 * rise_log) - 1.0) / (2.0 * rise_log)
    rise = rise / math.sqrt(mean_square)
    if spread_cols:
        spread = jnp.exp(jax.random.uniform(second_key, (1, cols), jnp.float32, -0.5 * math.log(10.0), 0.5 * math.log(10.0)))
        return base * rise * spread / 1.5
    return base * rise


def draw_query_weight(key, part):
    return rising_weight(key, 101, D, D, True).astype(jnp.bfloat16)


def draw_key_weight(key, part):
    return rising_weight(key, 102, D, D, True).astype(jnp.bfloat16)


def draw_output_weight(key, part):
    return rising_weight(key, 103, D, D, True).astype(jnp.bfloat16)


def draw_down_weight(key, part):
    return rising_weight(key, 104, FF, D, True).astype(jnp.bfloat16)


def draw_value_weight(key, part):
    return rising_weight(key, 108, D, D, False).astype(jnp.bfloat16)


def draw_gate_weight(key, part):
    return rising_weight(key, 109, D, FF, False).astype(jnp.bfloat16)


def draw_up_weight(key, part):
    return rising_weight(key, 110, D, FF, False).astype(jnp.bfloat16)


def draw_states(key, part):
    first_key, second_key = jax.random.split(jax.random.fold_in(key, 105))
    row_scale = jnp.exp(jax.random.uniform(second_key, (STEPS, R, 1), jnp.float32, math.log(0.1), math.log(1.0)))
    base = jax.random.truncated_normal(first_key, -4.0, 4.0, (STEPS, R, D), jnp.float32)
    return (base * row_scale).astype(jnp.bfloat16)


def draw_key_cache(key, part):
    base = jax.random.truncated_normal(jax.random.fold_in(key, 106), -6.0, 6.0, (PAGES, PAGE, D), jnp.float32)
    return base.astype(jnp.bfloat16)


def page_table(key):
    seq_count = PAGES // PAGES_DEV
    first_key, second_key, third_key = jax.random.split(jax.random.fold_in(key, 107), 3)
    spare_pages = (PAGES * 3 // 4 - MAXPAGES) // (R - 1)
    requests = jnp.arange(R, dtype=jnp.int32)
    counts = jax.random.randint(first_key, (R,), 1, spare_pages + 1, dtype=jnp.int32)
    longest = jax.random.randint(second_key, (), 0, R, dtype=jnp.int32)
    counts = jnp.where(requests == longest, MAXPAGES, counts)
    tails = jax.random.randint(third_key, (R,), 1, PAGE + 1, dtype=jnp.int32)
    tails = jnp.where(requests == longest, PAGE, tails)
    lengths = (counts - 1) * PAGE + tails
    ends = jnp.cumsum(counts)
    starts = ends - counts
    slots = jnp.arange(PAGES, dtype=jnp.int32)
    order = slots % PAGES_DEV * seq_count + slots // PAGES_DEV
    owners = jnp.sum((starts[None, :] <= order[:, None]).astype(jnp.int32), axis=1) - 1
    used = order < ends[R - 1]
    owners = jnp.where(used, owners, -1)
    own_start = jnp.sum(jnp.where(requests[None, :] == owners[:, None], starts[None, :], 0), axis=1)
    indices = jnp.where(used, order - own_start, 0)
    return (lengths.astype(jnp.int32), owners.astype(jnp.int32), indices.astype(jnp.int32))


def draw_lengths(key, part):
    return page_table(key)[0]


def draw_page_owner(key, part):
    return page_table(key)[1]


def draw_page_index(key, part):
    return page_table(key)[2]


def steps_of(key, dims, cuts, low, top_value):
    loudness, own = 1.0, jax.random.fold_in(key, 6)
    for dim, blocks in cuts:
        steps = jnp.exp(jax.random.uniform(jax.random.fold_in(own, dim), (blocks,), jnp.float32, low / len(cuts), top_value / len(cuts)))
        loudness = loudness * jnp.repeat(steps, dims[dim] // blocks).reshape([-1 if axis == dim else 1 for axis in range(len(dims))])
    return loudness


def gaussian(own_key, dims, width, reach, pieces=(), kind=jnp.bfloat16):
    entries = jax.random.normal(own_key, dims, jnp.float32) * width
    if len(pieces) > 0:
        entries = steps_of(own_key, dims, pieces, -0.22, 0.18) * entries
    return jnp.clip(entries, min=-reach, max=reach).astype(kind)


def setup_inputs(seed: int = 0) -> dict:
    arg_keys = jax.random.split(jax.random.key(seed), 18)
    return {
        "states": draw_states(jax.random.fold_in(arg_keys[17], 71), 0),
        "query_weight": draw_query_weight(jax.random.fold_in(arg_keys[17], 71), 0),
        "key_weight": draw_key_weight(jax.random.fold_in(arg_keys[17], 71), 0),
        "value_weight": draw_value_weight(jax.random.fold_in(arg_keys[17], 71), 0),
        "output_weight": draw_output_weight(jax.random.fold_in(arg_keys[17], 71), 0),
        "gate_weight": draw_gate_weight(jax.random.fold_in(arg_keys[17], 71), 0),
        "up_weight": draw_up_weight(jax.random.fold_in(arg_keys[17], 71), 0),
        "down_weight": draw_down_weight(jax.random.fold_in(arg_keys[17], 71), 0),
        "query_gain": jnp.clip(jnp.exp(math.log(2.0) - 1.3862944 * jax.random.uniform(arg_keys[8], (D,), jnp.float32) ** steps_of(arg_keys[8], (D,), ((0, 4),), -0.2, 0.2)), 0.5, 2.0),
        "key_gain": jnp.clip(jnp.exp(math.log(2.0) - 1.3862944 * jax.random.uniform(arg_keys[9], (D,), jnp.float32) ** steps_of(arg_keys[9], (D,), ((0, 4),), -0.2, 0.2)), 0.5, 2.0),
        "attention_gain": jnp.clip(1.0 + 0.18 * jax.random.normal(arg_keys[10], (D,), jnp.float32), 0.1, 1.9),
        "feedforward_gain": jnp.clip(1.0 + 0.18 * jax.random.normal(arg_keys[11], (D,), jnp.float32), 0.1, 1.9),
        "key_cache": draw_key_cache(jax.random.fold_in(arg_keys[17], 71), 0),
        "value_cache": gaussian(arg_keys[13], (PAGES, PAGE, D), 1.0, 6.0, ((0, 32), (2, 4))),
        "lengths": draw_lengths(jax.random.fold_in(arg_keys[17], 71), 0),
        "page_owner": draw_page_owner(jax.random.fold_in(arg_keys[17], 71), 0),
        "page_index": draw_page_index(jax.random.fold_in(arg_keys[17], 71), 0),
    }


epsilon = 1e-06
rope_base = 500000.0
very_low = -1e+30
exact_mode = lax.Precision.HIGHEST
pages_per_block = 4

def inverse_rms(values):
    return lax.rsqrt(lax.optimization_barrier(jnp.sum(values * values, axis=-1, keepdims=True)) / D + epsilon)

def rotary(values, positions):
    half_width = HD // 2
    frequencies = rope_base ** (-2.0 * jnp.arange(half_width, dtype=jnp.float32) / HD)
    angles = positions.astype(jnp.float32)[:, None] * frequencies[None, :]
    cosine = jnp.cos(angles)[:, None, :]
    sine_part = jnp.sin(angles)[:, None, :]
    first_half = values[..., :half_width]
    second_half = values[..., half_width:]
    return jnp.concatenate([first_half * cosine - second_half * sine_part, second_half * cosine + first_half * sine_part], axis=-1)

def project(token_rows, weight):
    return jnp.dot(token_rows, weight, preferred_element_type=jnp.float32)

def to_bf16_and_back(values):
    return lax.optimization_barrier(values.astype(jnp.bfloat16)).astype(jnp.float32)

def reference(states, query_weight, key_weight, value_weight, output_weight, gate_weight, up_weight, down_weight, query_gain, key_gain, attention_gain, feedforward_gain, key_cache, value_cache, lengths, page_owner, page_index):
    token_rows = states.reshape(STEPS * R, D)
    positions = (lengths[None, :] + jnp.arange(STEPS, dtype=jnp.int32)[:, None]).reshape(-1)
    query_raw = project(token_rows, query_weight)
    key_raw = project(token_rows, key_weight)
    value_raw = project(token_rows, value_weight)
    queries = query_raw * inverse_rms(query_raw) * query_gain
    queries = rotary(queries.reshape(STEPS * R, HEADS, HD), positions).astype(jnp.bfloat16).reshape(STEPS, R, HEADS, HD)
    new_keys = key_raw * inverse_rms(key_raw) * key_gain
    new_keys = rotary(new_keys.reshape(STEPS * R, HEADS, HD), positions).astype(jnp.bfloat16).reshape(STEPS, R, HEADS, HD)
    new_values = value_raw.astype(jnp.bfloat16).reshape(STEPS, R, HEADS, HD)
    score_scale = HD ** (-0.5)
    requests = jnp.arange(R, dtype=jnp.int32)

    def fold_block(carried, page_block):
        maxima, totals, running = carried
        key_block, value_block, owners, indices = page_block
        matches = owners[:, None] == requests[None, :]
        onehot = matches.astype(jnp.float32)
        picked = jnp.take(queries, jnp.maximum(owners, 0), axis=1).astype(jnp.float32)
        scores = jnp.einsum('sghd,gthd->sgth', picked, key_block.astype(jnp.float32), precision=exact_mode) * score_scale
        page_lengths = lax.optimization_barrier(jnp.sum(jnp.where(matches, lengths[None, :], 0), axis=1))
        token_spots = indices[:, None] * PAGE + jnp.arange(PAGE, dtype=jnp.int32)[None, :]
        validity = (token_spots < page_lengths[:, None])[None, :, :, None]
        masked = jnp.where(validity, scores, very_low)
        page_top = lax.optimization_barrier(jnp.max(masked, axis=2))
        request_top = lax.optimization_barrier(jnp.max(jnp.where(matches.T[None, :, :, None], page_top[:, None, :, :], very_low), axis=2))
        highest = jnp.maximum(maxima, request_top)
        page_ref = jnp.take(highest, jnp.maximum(owners, 0), axis=1)
        weights = jnp.where(validity, jnp.exp(masked - page_ref[:, :, None, :]), 0.0)
        page_total = lax.optimization_barrier(jnp.sum(weights, axis=2))
        page_sum = jnp.einsum('sgth,gthd->sghd', to_bf16_and_back(weights), value_block.astype(jnp.float32), precision=exact_mode)
        factor = jnp.exp(maxima - highest)
        totals = totals * factor + jnp.einsum('gr,sgh->srh', onehot, page_total, precision=exact_mode)
        running = running * factor[..., None] + jnp.einsum('gr,sghd->srhd', onehot, page_sum, precision=exact_mode)
        return ((highest, totals, running), None)
    blocks = (key_cache.reshape(-1, pages_per_block, PAGE, HEADS, HD), value_cache.reshape(-1, pages_per_block, PAGE, HEADS, HD), page_owner.reshape(-1, pages_per_block), page_index.reshape(-1, pages_per_block))
    initial = (jnp.full((STEPS, R, HEADS), very_low, jnp.float32), jnp.zeros((STEPS, R, HEADS), jnp.float32), jnp.zeros((STEPS, R, HEADS, HD), jnp.float32))
    (maxima, totals, running), _ = lax.scan(fold_block, initial, blocks)
    fresh_scores = jnp.einsum('srhd,trhd->srht', queries.astype(jnp.float32), new_keys.astype(jnp.float32), precision=exact_mode) * score_scale
    allowed = (jnp.arange(STEPS)[None, :] <= jnp.arange(STEPS)[:, None])[:, None, None, :]
    fresh_scores = jnp.where(allowed, fresh_scores, very_low)
    highest = jnp.maximum(maxima, lax.optimization_barrier(jnp.max(fresh_scores, axis=-1)))
    fresh_weights = jnp.where(allowed, jnp.exp(fresh_scores - highest[..., None]), 0.0)
    factor = jnp.exp(maxima - highest)
    totals = totals * factor + lax.optimization_barrier(jnp.sum(fresh_weights, axis=-1))
    running = running * factor[..., None] + jnp.einsum('srht,trhd->srhd', to_bf16_and_back(fresh_weights), new_values.astype(jnp.float32), precision=exact_mode)
    attended = (running / totals[..., None]).astype(jnp.bfloat16).reshape(STEPS * R, D)
    attention_out = project(attended, output_weight)
    hidden = (token_rows.astype(jnp.float32) + attention_out * inverse_rms(attention_out) * attention_gain).astype(jnp.bfloat16)
    gate = project(hidden, gate_weight)
    up_part = project(hidden, up_weight)
    active = (jax.nn.silu(gate) * up_part).astype(jnp.bfloat16)
    mlp_out = project(active, down_weight)
    decoded = (hidden.astype(jnp.float32) + mlp_out * inverse_rms(mlp_out) * feedforward_gain).astype(jnp.bfloat16)
    return decoded.reshape(STEPS, R, D)
```

```python
import jax
import jax.numpy as jnp
from jax import lax
from jax.sharding import PartitionSpec as P

D = 2048
HD = 128
R = 16
STEPS = 4
PAGE = 256


epsilon = 1e-06
rope_base = 500000.0
very_low = -1e30


def rotary(values, positions):
    half_width = HD // 2
    frequencies = rope_base ** (-2.0 * jnp.arange(half_width, dtype=jnp.float32) / HD)
    angles = positions.astype(jnp.float32)[:, None] * frequencies[None, :]
    cosine = jnp.cos(angles)[:, None, :]
    sine_part = jnp.sin(angles)[:, None, :]
    first_half = values[..., :half_width]
    second_half = values[..., half_width:]
    return jnp.concatenate(
        [
            first_half * cosine - second_half * sine_part,
            second_half * cosine + first_half * sine_part,
        ],
        axis=-1,
    )


def seq_columns(block, width):
    per = block.shape[1] // width
    seq = lax.axis_index("seq")
    piece = lax.dynamic_slice_in_dim(block, (seq % per) * width, width, 1)
    gathered = lax.all_gather(piece, "mp")
    return lax.dynamic_index_in_dim(gathered, seq // per, 0, keepdims=False)


def seq_total(partial_value):
    return lax.psum(partial_value, "seq")


def feature_sums(squares):
    return lax.psum(squares, "mp")


def inverse_rms(square_total):
    return lax.rsqrt(square_total / D + epsilon)[:, None]


def local(
    states,
    query_weight,
    key_weight,
    value_weight,
    output_weight,
    gate_weight,
    up_weight,
    down_weight,
    query_gain,
    key_gain,
    attention_gain,
    feedforward_gain,
    key_cache,
    value_cache,
    lengths,
    page_owner,
    page_index,
):
    local_width = query_weight.shape[1]
    local_heads = local_width // HD
    rows = STEPS * R
    score_scale = HD ** (-0.5)
    token_rows = states.reshape(rows, local_width)
    positions = (lengths[None, :] + jnp.arange(STEPS, dtype=jnp.int32)[:, None]).reshape(rows)

    sliced = seq_columns(token_rows, query_weight.shape[0])
    summed = seq_total(
        jnp.concatenate(
            [
                jnp.dot(sliced, query_weight, preferred_element_type=jnp.float32),
                jnp.dot(sliced, key_weight, preferred_element_type=jnp.float32),
                jnp.dot(sliced, value_weight, preferred_element_type=jnp.float32),
            ],
            axis=1,
        )
    )
    query_raw = summed[:, :local_width]
    key_raw = summed[:, local_width : 2 * local_width]
    value_raw = summed[:, 2 * local_width :]
    squares = feature_sums(
        jnp.stack([jnp.sum(query_raw * query_raw, axis=1), jnp.sum(key_raw * key_raw, axis=1)], axis=1)
    )
    queries = rotary(
        (query_raw * inverse_rms(squares[:, 0]) * query_gain).reshape(rows, local_heads, HD), positions
    ).astype(jnp.bfloat16)
    new_keys = rotary(
        (key_raw * inverse_rms(squares[:, 1]) * key_gain).reshape(rows, local_heads, HD), positions
    ).astype(jnp.bfloat16)
    new_values = value_raw.astype(jnp.bfloat16).reshape(rows, local_heads, HD)

    pages = key_cache.shape[0]
    tokens = pages * PAGE
    keys = key_cache.reshape(tokens, local_heads, HD)
    values = value_cache.reshape(tokens, local_heads, HD)
    token_owner = jnp.repeat(page_owner, PAGE)
    token_spot = (page_index[:, None] * PAGE + jnp.arange(PAGE, dtype=jnp.int32)[None, :]).reshape(tokens)
    request_of_row = jnp.tile(jnp.arange(R, dtype=jnp.int32), STEPS)
    length_of_row = jnp.tile(lengths, STEPS)
    validity = (token_owner[None, :] == request_of_row[:, None]) & (
        token_spot[None, :] < length_of_row[:, None]
    )
    scores = (
        jnp.einsum("qhd,thd->hqt", queries, keys, preferred_element_type=jnp.float32) * score_scale
    )
    masked = jnp.where(validity[None], scores, very_low)
    maxima = jnp.max(masked, axis=2)
    weights = jnp.where(validity[None], jnp.exp(masked - maxima[..., None]), 0.0)
    totals = jnp.sum(weights, axis=2)
    running = jnp.einsum(
        "hqt,thd->hqd", weights.astype(jnp.bfloat16), values, preferred_element_type=jnp.float32
    )

    all_maxima, all_totals, all_running = lax.all_gather((maxima, totals, running), "seq")
    cache_highest = jnp.max(all_maxima, axis=0)
    scale = jnp.exp(all_maxima - cache_highest[None])
    cache_totals = jnp.sum(all_totals * scale, axis=0)
    cache_running = jnp.sum(all_running * scale[..., None], axis=0)

    q4 = queries.reshape(STEPS, R, local_heads, HD)
    k4 = new_keys.reshape(STEPS, R, local_heads, HD)
    v4 = new_values.reshape(STEPS, R, local_heads, HD)
    fresh_scores = (
        jnp.einsum("srhd,trhd->hsrt", q4, k4, preferred_element_type=jnp.float32) * score_scale
    )
    allowed = (jnp.arange(STEPS)[None, :] <= jnp.arange(STEPS)[:, None])[None, :, None, :]
    fresh_scores = jnp.where(allowed, fresh_scores, very_low)
    cache_highest = cache_highest.reshape(local_heads, STEPS, R)
    highest = jnp.maximum(cache_highest, jnp.max(fresh_scores, axis=-1))
    fresh_weights = jnp.where(allowed, jnp.exp(fresh_scores - highest[..., None]), 0.0)
    factor = jnp.exp(cache_highest - highest)
    final_totals = cache_totals.reshape(local_heads, STEPS, R) * factor + jnp.sum(fresh_weights, axis=-1)
    final_running = cache_running.reshape(local_heads, STEPS, R, HD) * factor[..., None] + jnp.einsum(
        "hsrt,trhd->hsrd", fresh_weights.astype(jnp.bfloat16), v4, preferred_element_type=jnp.float32
    )
    attended = (final_running / final_totals[..., None]).astype(jnp.bfloat16)
    attended = jnp.transpose(attended, (1, 2, 0, 3)).reshape(rows, local_width)

    sliced = seq_columns(attended, output_weight.shape[0])
    attention_out = seq_total(jnp.dot(sliced, output_weight, preferred_element_type=jnp.float32))
    attention_squares = feature_sums(jnp.sum(attention_out * attention_out, axis=1))
    hidden = (
        token_rows.astype(jnp.float32) + attention_out * inverse_rms(attention_squares) * attention_gain
    ).astype(jnp.bfloat16)

    hidden_cols = seq_columns(hidden, gate_weight.shape[0])
    hidden_units = gate_weight.shape[1]
    summed_both = seq_total(
        jnp.concatenate(
            [
                jnp.dot(hidden_cols, gate_weight, preferred_element_type=jnp.float32),
                jnp.dot(hidden_cols, up_weight, preferred_element_type=jnp.float32),
            ],
            axis=1,
        )
    )
    active = (jax.nn.silu(summed_both[:, :hidden_units]) * summed_both[:, hidden_units:]).astype(
        jnp.bfloat16
    )
    active_cols = seq_columns(active, down_weight.shape[0])
    mlp_out = seq_total(jnp.dot(active_cols, down_weight, preferred_element_type=jnp.float32))
    mlp_squares = feature_sums(jnp.sum(mlp_out * mlp_out, axis=1))
    decoded = (
        hidden.astype(jnp.float32) + mlp_out * inverse_rms(mlp_squares) * feedforward_gain
    ).astype(jnp.bfloat16)
    return decoded.reshape(STEPS, R, local_width)


def solution(mesh):
    in_specs = (
        P(None, None, "mp"),
        P("seq", "mp"),
        P("seq", "mp"),
        P("seq", "mp"),
        P("seq", "mp"),
        P("seq", "mp"),
        P("seq", "mp"),
        P("seq", "mp"),
        P("mp"),
        P("mp"),
        P("mp"),
        P("mp"),
        P("seq", None, "mp"),
        P("seq", None, "mp"),
        P(),
        P("seq"),
        P("seq"),
    )
    out_specs = P(None, None, "mp")
    return jax.shard_map(local, mesh=mesh, in_specs=in_specs, out_specs=out_specs, check_vma=False)
```

```python
import jax
import jax.numpy as jnp
from jax import lax
from jax.sharding import PartitionSpec as P

D = 2048
HD = 128
R = 16
STEPS = 4
PAGE = 256


epsilon = 1e-06
rope_base = 500000.0
very_low = -1e30
SEQ_SIZE = 32


def rotary(values, positions):
    half_width = HD // 2
    frequencies = rope_base ** (-2.0 * jnp.arange(half_width, dtype=jnp.float32) / HD)
    angles = positions.astype(jnp.float32)[:, None] * frequencies[None, :]
    cosine = jnp.cos(angles)[:, None, :]
    sine_part = jnp.sin(angles)[:, None, :]
    first_half = values[..., :half_width]
    second_half = values[..., half_width:]
    return jnp.concatenate(
        [
            first_half * cosine - second_half * sine_part,
            second_half * cosine + first_half * sine_part,
        ],
        axis=-1,
    )


def seq_columns(block, width):
    per = block.shape[1] // width
    seq = lax.axis_index("seq")
    piece = lax.dynamic_slice_in_dim(block, (seq % per) * width, width, 1)
    gathered = lax.all_gather(piece, "mp")
    return lax.dynamic_index_in_dim(gathered, seq // per, 0, keepdims=False)


def seq_total(partial_value):
    count = SEQ_SIZE
    rounds = count.bit_length() - 1
    me = lax.axis_index("seq")
    current = partial_value
    for bit in range(rounds):
        half = current.shape[1] // 2
        mine = (me >> bit) & 1
        keep = lax.dynamic_slice_in_dim(current, mine * half, half, 1)
        send = lax.dynamic_slice_in_dim(current, (1 - mine) * half, half, 1)
        pairs = [(i, i ^ (1 << bit)) for i in range(count)]
        current = keep + lax.ppermute(send, "seq", pairs)
    for bit in reversed(range(rounds)):
        mine = (me >> bit) & 1
        pairs = [(i, i ^ (1 << bit)) for i in range(count)]
        other = lax.ppermute(current, "seq", pairs)
        low = jnp.where(mine == 0, current, other)
        high = jnp.where(mine == 0, other, current)
        current = jnp.concatenate([low, high], axis=1)
    return current


def feature_sums(squares):
    return jnp.sum(lax.all_gather(squares, "mp"), axis=0)


def inverse_rms(square_total):
    return lax.rsqrt(square_total / D + epsilon)[:, None]


def local(
    states,
    query_weight,
    key_weight,
    value_weight,
    output_weight,
    gate_weight,
    up_weight,
    down_weight,
    query_gain,
    key_gain,
    attention_gain,
    feedforward_gain,
    key_cache,
    value_cache,
    lengths,
    page_owner,
    page_index,
):
    local_width = query_weight.shape[1]
    local_heads = local_width // HD
    rows = STEPS * R
    score_scale = HD ** (-0.5)
    token_rows = states.reshape(rows, local_width)
    positions = (lengths[None, :] + jnp.arange(STEPS, dtype=jnp.int32)[:, None]).reshape(rows)

    sliced = seq_columns(token_rows, query_weight.shape[0])
    summed = seq_total(
        jnp.concatenate(
            [
                jnp.dot(sliced, query_weight, preferred_element_type=jnp.float32),
                jnp.dot(sliced, key_weight, preferred_element_type=jnp.float32),
                jnp.dot(sliced, value_weight, preferred_element_type=jnp.float32),
            ],
            axis=1,
        )
    )
    query_raw = summed[:, :local_width]
    key_raw = summed[:, local_width : 2 * local_width]
    value_raw = summed[:, 2 * local_width :]
    squares = feature_sums(
        jnp.stack([jnp.sum(query_raw * query_raw, axis=1), jnp.sum(key_raw * key_raw, axis=1)], axis=1)
    )
    queries = rotary(
        (query_raw * inverse_rms(squares[:, 0]) * query_gain).reshape(rows, local_heads, HD), positions
    ).astype(jnp.bfloat16)
    new_keys = rotary(
        (key_raw * inverse_rms(squares[:, 1]) * key_gain).reshape(rows, local_heads, HD), positions
    ).astype(jnp.bfloat16)
    new_values = value_raw.astype(jnp.bfloat16).reshape(rows, local_heads, HD)

    pages = key_cache.shape[0]
    tokens = pages * PAGE
    keys = key_cache.reshape(tokens, local_width)
    values = value_cache.reshape(tokens, local_width)
    token_owner = jnp.repeat(page_owner, PAGE)
    token_spot = (page_index[:, None] * PAGE + jnp.arange(PAGE, dtype=jnp.int32)[None, :]).reshape(tokens)
    request_of_row = jnp.tile(jnp.arange(R, dtype=jnp.int32), STEPS)
    length_of_row = jnp.tile(lengths, STEPS)
    validity = (token_owner[None, :] == request_of_row[:, None]) & (
        token_spot[None, :] < length_of_row[:, None]
    )
    flat_queries = queries.reshape(rows, local_width)
    scores = jnp.stack(
        [
            lax.dot_general(
                flat_queries[:, h * HD : (h + 1) * HD],
                keys[:, h * HD : (h + 1) * HD],
                (((1,), (1,)), ((), ())),
                preferred_element_type=jnp.float32,
            )
            for h in range(local_heads)
        ]
    ) * score_scale
    masked = jnp.where(validity[None], scores, very_low)
    maxima = jnp.max(masked, axis=2)
    weights = jnp.where(validity[None], jnp.exp(masked - maxima[..., None]), 0.0)
    totals = jnp.sum(weights, axis=2)
    rounded = weights.astype(jnp.bfloat16)
    running = jnp.stack(
        [
            jnp.dot(rounded[h], values[:, h * HD : (h + 1) * HD], preferred_element_type=jnp.float32)
            for h in range(local_heads)
        ]
    )

    all_maxima, all_totals, all_running = lax.all_gather((maxima, totals, running), "seq")
    cache_highest = jnp.max(all_maxima, axis=0)
    scale = jnp.exp(all_maxima - cache_highest[None])
    cache_totals = jnp.sum(all_totals * scale, axis=0)
    cache_running = jnp.sum(all_running * scale[..., None], axis=0)

    q4 = queries.reshape(STEPS, R, local_heads, HD)
    k4 = new_keys.reshape(STEPS, R, local_heads, HD)
    v4 = new_values.reshape(STEPS, R, local_heads, HD)
    fresh_scores = (
        jnp.einsum("srhd,trhd->hsrt", q4, k4, preferred_element_type=jnp.float32) * score_scale
    )
    allowed = (jnp.arange(STEPS)[None, :] <= jnp.arange(STEPS)[:, None])[None, :, None, :]
    fresh_scores = jnp.where(allowed, fresh_scores, very_low)
    cache_highest = cache_highest.reshape(local_heads, STEPS, R)
    highest = jnp.maximum(cache_highest, jnp.max(fresh_scores, axis=-1))
    fresh_weights = jnp.where(allowed, jnp.exp(fresh_scores - highest[..., None]), 0.0)
    factor = jnp.exp(cache_highest - highest)
    final_totals = cache_totals.reshape(local_heads, STEPS, R) * factor + jnp.sum(fresh_weights, axis=-1)
    final_running = cache_running.reshape(local_heads, STEPS, R, HD) * factor[..., None] + jnp.einsum(
        "hsrt,trhd->hsrd", fresh_weights.astype(jnp.bfloat16), v4, preferred_element_type=jnp.float32
    )
    attended = (final_running / final_totals[..., None]).astype(jnp.bfloat16)
    attended = jnp.transpose(attended, (1, 2, 0, 3)).reshape(rows, local_width)

    sliced = seq_columns(attended, output_weight.shape[0])
    attention_out = seq_total(jnp.dot(sliced, output_weight, preferred_element_type=jnp.float32))
    attention_squares = feature_sums(jnp.sum(attention_out * attention_out, axis=1))
    hidden = (
        token_rows.astype(jnp.float32) + attention_out * inverse_rms(attention_squares) * attention_gain
    ).astype(jnp.bfloat16)

    hidden_cols = seq_columns(hidden, gate_weight.shape[0])
    hidden_units = gate_weight.shape[1]
    summed_both = seq_total(
        jnp.concatenate(
            [
                jnp.dot(hidden_cols, gate_weight, preferred_element_type=jnp.float32),
                jnp.dot(hidden_cols, up_weight, preferred_element_type=jnp.float32),
            ],
            axis=1,
        )
    )
    active = (jax.nn.silu(summed_both[:, :hidden_units]) * summed_both[:, hidden_units:]).astype(
        jnp.bfloat16
    )
    active_cols = seq_columns(active, down_weight.shape[0])
    mlp_out = seq_total(jnp.dot(active_cols, down_weight, preferred_element_type=jnp.float32))
    mlp_squares = feature_sums(jnp.sum(mlp_out * mlp_out, axis=1))
    decoded = (
        hidden.astype(jnp.float32) + mlp_out * inverse_rms(mlp_squares) * feedforward_gain
    ).astype(jnp.bfloat16)
    return decoded.reshape(STEPS, R, local_width)


def solution(mesh):
    global SEQ_SIZE
    SEQ_SIZE = mesh.shape["seq"]
    in_specs = (
        P(None, None, "mp"),
        P("seq", "mp"),
        P("seq", "mp"),
        P("seq", "mp"),
        P("seq", "mp"),
        P("seq", "mp"),
        P("seq", "mp"),
        P("seq", "mp"),
        P("mp"),
        P("mp"),
        P("mp"),
        P("mp"),
        P("seq", None, "mp"),
        P("seq", None, "mp"),
        P(),
        P("seq"),
        P("seq"),
    )
    out_specs = P(None, None, "mp")
    return jax.shard_map(local, mesh=mesh, in_specs=in_specs, out_specs=out_specs, check_vma=False)
```

```python
import jax
import jax.numpy as jnp
from jax import lax
from jax.sharding import PartitionSpec as P

D = 2048
HD = 128
R = 16
STEPS = 4
PAGE = 256


epsilon = 1e-06
rope_base = 500000.0
very_low = -1e30
SEQ_SIZE = 32
MP_SIZE = 4
SEQ_FACTORS = (2, 4, 4)


def rotary(values, positions):
    half_width = HD // 2
    frequencies = rope_base ** (-2.0 * jnp.arange(half_width, dtype=jnp.float32) / HD)
    angles = positions.astype(jnp.float32)[:, None] * frequencies[None, :]
    cosine = jnp.cos(angles)[:, None, :]
    sine_part = jnp.sin(angles)[:, None, :]
    first_half = values[..., :half_width]
    second_half = values[..., half_width:]
    return jnp.concatenate(
        [
            first_half * cosine - second_half * sine_part,
            second_half * cosine + first_half * sine_part,
        ],
        axis=-1,
    )


def seq_columns(block, width):
    per = block.shape[1] // width
    seq = lax.axis_index("seq")
    mp = lax.axis_index("mp")
    piece = lax.dynamic_slice_in_dim(block, (seq % per) * width, width, 1)
    result = piece
    for shift in range(1, MP_SIZE):
        pairs = [
            (i * MP_SIZE + i // per, i * MP_SIZE + (i // per + shift) % MP_SIZE) for i in range(SEQ_SIZE)
        ]
        received = lax.ppermute(piece, ("seq", "mp"), pairs)
        result = jnp.where(mp == (seq // per + shift) % MP_SIZE, received, result)
    return result


def seq_groups():
    groups = []
    stride = 1
    for size in SEQ_FACTORS:
        groups.append((stride, size))
        stride *= size
    return groups


def seq_total(partial_value):
    me = lax.axis_index("seq")
    current = partial_value
    for stride, size in seq_groups():
        digit = (me // stride) % size
        part = current.shape[1] // size
        total = lax.dynamic_slice_in_dim(current, digit * part, part, 1)
        for shift in range(1, size):
            pairs = [
                (i, i + (((i // stride) % size + shift) % size - (i // stride) % size) * stride)
                for i in range(SEQ_SIZE)
            ]
            send = lax.dynamic_slice_in_dim(current, ((digit + shift) % size) * part, part, 1)
            total = total + lax.ppermute(send, "seq", pairs)
        current = total
    for stride, size in reversed(seq_groups()):
        digit = (me // stride) % size
        part = current.shape[1]
        whole = jnp.zeros((current.shape[0], part * size), current.dtype)
        whole = lax.dynamic_update_slice_in_dim(whole, current, digit * part, 1)
        for shift in range(1, size):
            pairs = [
                (i, i + (((i // stride) % size + shift) % size - (i // stride) % size) * stride)
                for i in range(SEQ_SIZE)
            ]
            received = lax.ppermute(current, "seq", pairs)
            whole = lax.dynamic_update_slice_in_dim(whole, received, ((digit - shift) % size) * part, 1)
        current = whole
    return current


def feature_sums(squares):
    return jnp.sum(lax.all_gather(squares, "mp"), axis=0)


def inverse_rms(square_total):
    return lax.rsqrt(square_total / D + epsilon)[:, None]


def local(
    states,
    query_weight,
    key_weight,
    value_weight,
    output_weight,
    gate_weight,
    up_weight,
    down_weight,
    query_gain,
    key_gain,
    attention_gain,
    feedforward_gain,
    key_cache,
    value_cache,
    lengths,
    page_owner,
    page_index,
):
    local_width = query_weight.shape[1]
    local_heads = local_width // HD
    rows = STEPS * R
    score_scale = HD ** (-0.5)
    token_rows = states.reshape(rows, local_width)
    positions = (lengths[None, :] + jnp.arange(STEPS, dtype=jnp.int32)[:, None]).reshape(rows)

    sliced = seq_columns(token_rows, query_weight.shape[0])
    summed = seq_total(
        jnp.concatenate(
            [
                jnp.dot(sliced, query_weight, preferred_element_type=jnp.float32),
                jnp.dot(sliced, key_weight, preferred_element_type=jnp.float32),
                jnp.dot(sliced, value_weight, preferred_element_type=jnp.float32),
            ],
            axis=1,
        )
    )
    query_raw = summed[:, :local_width]
    key_raw = summed[:, local_width : 2 * local_width]
    value_raw = summed[:, 2 * local_width :]
    squares = feature_sums(
        jnp.stack([jnp.sum(query_raw * query_raw, axis=1), jnp.sum(key_raw * key_raw, axis=1)], axis=1)
    )
    queries = rotary(
        (query_raw * inverse_rms(squares[:, 0]) * query_gain).reshape(rows, local_heads, HD), positions
    ).astype(jnp.bfloat16)
    new_keys = rotary(
        (key_raw * inverse_rms(squares[:, 1]) * key_gain).reshape(rows, local_heads, HD), positions
    ).astype(jnp.bfloat16)
    new_values = value_raw.astype(jnp.bfloat16).reshape(rows, local_heads, HD)

    pages = key_cache.shape[0]
    tokens = pages * PAGE
    keys = key_cache.reshape(tokens, local_width)
    values = value_cache.reshape(tokens, local_width)
    token_owner = jnp.repeat(page_owner, PAGE)
    token_spot = (page_index[:, None] * PAGE + jnp.arange(PAGE, dtype=jnp.int32)[None, :]).reshape(tokens)
    request_of_row = jnp.tile(jnp.arange(R, dtype=jnp.int32), STEPS)
    length_of_row = jnp.tile(lengths, STEPS)
    validity = (token_owner[None, :] == request_of_row[:, None]) & (
        token_spot[None, :] < length_of_row[:, None]
    )
    flat_queries = queries.reshape(rows, local_width)
    scores = jnp.stack(
        [
            lax.dot_general(
                flat_queries[:, h * HD : (h + 1) * HD],
                keys[:, h * HD : (h + 1) * HD],
                (((1,), (1,)), ((), ())),
                preferred_element_type=jnp.float32,
            )
            for h in range(local_heads)
        ]
    ) * score_scale
    masked = jnp.where(validity[None], scores, very_low)
    maxima = jnp.max(masked, axis=2)
    weights = jnp.where(validity[None], jnp.exp(masked - maxima[..., None]), 0.0)
    totals = jnp.sum(weights, axis=2)
    rounded = weights.astype(jnp.bfloat16)
    running = jnp.stack(
        [
            jnp.dot(rounded[h], values[:, h * HD : (h + 1) * HD], preferred_element_type=jnp.float32)
            for h in range(local_heads)
        ]
    )

    stats = lax.all_gather(
        jnp.concatenate([running, maxima[..., None], totals[..., None]], axis=2), "seq"
    )
    all_running = stats[..., :HD]
    all_maxima = stats[..., HD]
    all_totals = stats[..., HD + 1]
    cache_highest = jnp.max(all_maxima, axis=0)
    scale = jnp.exp(all_maxima - cache_highest[None])
    cache_totals = jnp.sum(all_totals * scale, axis=0)
    cache_running = jnp.sum(all_running * scale[..., None], axis=0)

    q4 = queries.reshape(STEPS, R, local_heads, HD)
    k4 = new_keys.reshape(STEPS, R, local_heads, HD)
    v4 = new_values.reshape(STEPS, R, local_heads, HD)
    fresh_scores = (
        jnp.einsum("srhd,trhd->hsrt", q4, k4, preferred_element_type=jnp.float32) * score_scale
    )
    allowed = (jnp.arange(STEPS)[None, :] <= jnp.arange(STEPS)[:, None])[None, :, None, :]
    fresh_scores = jnp.where(allowed, fresh_scores, very_low)
    cache_highest = cache_highest.reshape(local_heads, STEPS, R)
    highest = jnp.maximum(cache_highest, jnp.max(fresh_scores, axis=-1))
    fresh_weights = jnp.where(allowed, jnp.exp(fresh_scores - highest[..., None]), 0.0)
    factor = jnp.exp(cache_highest - highest)
    final_totals = cache_totals.reshape(local_heads, STEPS, R) * factor + jnp.sum(fresh_weights, axis=-1)
    final_running = cache_running.reshape(local_heads, STEPS, R, HD) * factor[..., None] + jnp.einsum(
        "hsrt,trhd->hsrd", fresh_weights.astype(jnp.bfloat16), v4, preferred_element_type=jnp.float32
    )
    attended = (final_running / final_totals[..., None]).astype(jnp.bfloat16)
    attended = jnp.transpose(attended, (1, 2, 0, 3)).reshape(rows, local_width)

    sliced = seq_columns(attended, output_weight.shape[0])
    attention_out = seq_total(jnp.dot(sliced, output_weight, preferred_element_type=jnp.float32))
    attention_squares = feature_sums(jnp.sum(attention_out * attention_out, axis=1))
    hidden = (
        token_rows.astype(jnp.float32) + attention_out * inverse_rms(attention_squares) * attention_gain
    ).astype(jnp.bfloat16)

    hidden_cols = seq_columns(hidden, gate_weight.shape[0])
    hidden_units = gate_weight.shape[1]
    summed_both = seq_total(
        jnp.concatenate(
            [
                jnp.dot(hidden_cols, gate_weight, preferred_element_type=jnp.float32),
                jnp.dot(hidden_cols, up_weight, preferred_element_type=jnp.float32),
            ],
            axis=1,
        )
    )
    active = (jax.nn.silu(summed_both[:, :hidden_units]) * summed_both[:, hidden_units:]).astype(
        jnp.bfloat16
    )
    active_cols = seq_columns(active, down_weight.shape[0])
    mlp_out = seq_total(jnp.dot(active_cols, down_weight, preferred_element_type=jnp.float32))
    mlp_squares = feature_sums(jnp.sum(mlp_out * mlp_out, axis=1))
    decoded = (
        hidden.astype(jnp.float32) + mlp_out * inverse_rms(mlp_squares) * feedforward_gain
    ).astype(jnp.bfloat16)
    return decoded.reshape(STEPS, R, local_width)


def solution(mesh):
    global SEQ_SIZE, MP_SIZE, SEQ_FACTORS
    SEQ_SIZE = mesh.shape["seq"]
    MP_SIZE = mesh.shape["mp"]
    factors = []
    left = SEQ_SIZE
    if left % 2 == 0:
        factors.append(2)
        left //= 2
    while left % 4 == 0:
        factors.append(4)
        left //= 4
    if left > 1:
        factors.append(left)
    SEQ_FACTORS = tuple(factors)
    in_specs = (
        P(None, None, "mp"),
        P("seq", "mp"),
        P("seq", "mp"),
        P("seq", "mp"),
        P("seq", "mp"),
        P("seq", "mp"),
        P("seq", "mp"),
        P("seq", "mp"),
        P("mp"),
        P("mp"),
        P("mp"),
        P("mp"),
        P("seq", None, "mp"),
        P("seq", None, "mp"),
        P(),
        P("seq"),
        P("seq"),
    )
    out_specs = P(None, None, "mp")
    return jax.shard_map(local, mesh=mesh, in_specs=in_specs, out_specs=out_specs, check_vma=False)
```

```python
import jax
import jax.numpy as jnp
from jax import lax
from jax.sharding import PartitionSpec as P

D = 2048
HD = 128
R = 16
STEPS = 4
PAGE = 256


epsilon = 1e-06
rope_base = 500000.0
very_low = -1e30
SEQ_SIZE = 32
MP_SIZE = 4
SEQ_FACTORS = (2, 4, 4)


def rotary(values, positions):
    half_width = HD // 2
    frequencies = rope_base ** (-2.0 * jnp.arange(half_width, dtype=jnp.float32) / HD)
    angles = positions.astype(jnp.float32)[:, None] * frequencies[None, :]
    cosine = jnp.cos(angles)[:, None, :]
    sine_part = jnp.sin(angles)[:, None, :]
    first_half = values[..., :half_width]
    second_half = values[..., half_width:]
    return jnp.concatenate(
        [
            first_half * cosine - second_half * sine_part,
            second_half * cosine + first_half * sine_part,
        ],
        axis=-1,
    )


def seq_columns(block, width):
    per = block.shape[1] // width
    seq = lax.axis_index("seq")
    mp = lax.axis_index("mp")
    piece = lax.dynamic_slice_in_dim(block, (seq % per) * width, width, 1)
    result = piece
    for shift in range(1, MP_SIZE):
        pairs = [
            (i * MP_SIZE + i // per, i * MP_SIZE + (i // per + shift) % MP_SIZE) for i in range(SEQ_SIZE)
        ]
        received = lax.ppermute(piece, ("seq", "mp"), pairs)
        result = jnp.where(mp == (seq // per + shift) % MP_SIZE, received, result)
    return result


def seq_groups():
    groups = []
    stride = 1
    for size in SEQ_FACTORS:
        groups.append((stride, size))
        stride *= size
    return groups


def digit_pairs(count, stride, size, shift):
    return [
        (i, i + (((i // stride) % size + shift) % size - (i // stride) % size) * stride)
        for i in range(count)
    ]


def exchange(value, axis, count, stride, size):
    digit = (lax.axis_index(axis) // stride) % size
    stack = jnp.zeros((size,) + value.shape, value.dtype)
    stack = lax.dynamic_update_index_in_dim(stack, value, digit, 0)
    for shift in range(1, size):
        received = lax.ppermute(value, axis, digit_pairs(count, stride, size, shift))
        stack = lax.dynamic_update_index_in_dim(stack, received, (digit - shift) % size, 0)
    return stack


def scatter_digit(current, stride, size):
    me = lax.axis_index("seq")
    digit = (me // stride) % size
    part = current.shape[1] // size
    total = lax.dynamic_slice_in_dim(current, digit * part, part, 1)
    for shift in range(1, size):
        send = lax.dynamic_slice_in_dim(current, ((digit + shift) % size) * part, part, 1)
        total = total + lax.ppermute(send, "seq", digit_pairs(SEQ_SIZE, stride, size, shift))
    return total


def gather_digit(current, stride, size):
    me = lax.axis_index("seq")
    digit = (me // stride) % size
    part = current.shape[1]
    whole = jnp.zeros((current.shape[0], part * size), current.dtype)
    whole = lax.dynamic_update_slice_in_dim(whole, current, digit * part, 1)
    for shift in range(1, size):
        received = lax.ppermute(current, "seq", digit_pairs(SEQ_SIZE, stride, size, shift))
        whole = lax.dynamic_update_slice_in_dim(whole, received, ((digit - shift) % size) * part, 1)
    return whole


def seq_total(partial_value, ladder=False):
    groups = seq_groups()
    current = partial_value
    if ladder:
        for stride, size in groups:
            current = scatter_digit(current, stride, size)
        for stride, size in reversed(groups):
            current = gather_digit(current, stride, size)
        return current
    stride, size = groups[0]
    current = scatter_digit(current, stride, size)
    for other_stride, other_size in groups[1:]:
        current = jnp.sum(exchange(current, "seq", SEQ_SIZE, other_stride, other_size), axis=0)
    return gather_digit(current, stride, size)


def merge_stack(stack):
    member_max = stack[..., HD]
    highest = jnp.max(member_max, axis=0)
    scale = jnp.exp(member_max - highest[None])
    totals = jnp.sum(stack[..., HD + 1] * scale, axis=0)
    running = jnp.sum(stack[..., :HD] * scale[..., None], axis=0)
    return jnp.concatenate([running, highest[..., None], totals[..., None]], axis=-1)


def feature_sums(squares):
    return jnp.sum(exchange(squares, "mp", MP_SIZE, 1, MP_SIZE), axis=0)


def inverse_rms(square_total):
    return lax.rsqrt(square_total / D + epsilon)[:, None]


def local(
    states,
    query_weight,
    key_weight,
    value_weight,
    output_weight,
    gate_weight,
    up_weight,
    down_weight,
    query_gain,
    key_gain,
    attention_gain,
    feedforward_gain,
    key_cache,
    value_cache,
    lengths,
    page_owner,
    page_index,
):
    local_width = query_weight.shape[1]
    local_heads = local_width // HD
    rows = STEPS * R
    score_scale = HD ** (-0.5)
    token_rows = states.reshape(rows, local_width)
    positions = (lengths[None, :] + jnp.arange(STEPS, dtype=jnp.int32)[:, None]).reshape(rows)

    sliced = seq_columns(token_rows, query_weight.shape[0])
    summed = seq_total(
        jnp.concatenate(
            [
                jnp.dot(sliced, query_weight, preferred_element_type=jnp.float32),
                jnp.dot(sliced, key_weight, preferred_element_type=jnp.float32),
                jnp.dot(sliced, value_weight, preferred_element_type=jnp.float32),
            ],
            axis=1,
        )
    )
    query_raw = summed[:, :local_width]
    key_raw = summed[:, local_width : 2 * local_width]
    value_raw = summed[:, 2 * local_width :]
    squares = feature_sums(
        jnp.stack([jnp.sum(query_raw * query_raw, axis=1), jnp.sum(key_raw * key_raw, axis=1)], axis=1)
    )
    queries = rotary(
        (query_raw * inverse_rms(squares[:, 0]) * query_gain).reshape(rows, local_heads, HD), positions
    ).astype(jnp.bfloat16)
    new_keys = rotary(
        (key_raw * inverse_rms(squares[:, 1]) * key_gain).reshape(rows, local_heads, HD), positions
    ).astype(jnp.bfloat16)
    new_values = value_raw.astype(jnp.bfloat16).reshape(rows, local_heads, HD)

    pages = key_cache.shape[0]
    tokens = pages * PAGE
    keys = key_cache.reshape(tokens, local_width)
    values = value_cache.reshape(tokens, local_width)
    token_owner = jnp.repeat(page_owner, PAGE)
    token_spot = (page_index[:, None] * PAGE + jnp.arange(PAGE, dtype=jnp.int32)[None, :]).reshape(tokens)
    request_of_row = jnp.tile(jnp.arange(R, dtype=jnp.int32), STEPS)
    length_of_row = jnp.tile(lengths, STEPS)
    validity = (token_owner[None, :] == request_of_row[:, None]) & (
        token_spot[None, :] < length_of_row[:, None]
    )
    flat_queries = queries.reshape(rows, local_width)
    scores = jnp.stack(
        [
            lax.dot_general(
                flat_queries[:, h * HD : (h + 1) * HD],
                keys[:, h * HD : (h + 1) * HD],
                (((1,), (1,)), ((), ())),
                preferred_element_type=jnp.float32,
            )
            for h in range(local_heads)
        ]
    ) * score_scale
    masked = jnp.where(validity[None], scores, very_low)
    maxima = jnp.max(masked, axis=2)
    weights = jnp.where(validity[None], jnp.exp(masked - maxima[..., None]), 0.0)
    totals = jnp.sum(weights, axis=2)
    rounded = weights.astype(jnp.bfloat16)
    running = jnp.stack(
        [
            jnp.dot(rounded[h], values[:, h * HD : (h + 1) * HD], preferred_element_type=jnp.float32)
            for h in range(local_heads)
        ]
    )

    stats = jnp.concatenate([running, maxima[..., None], totals[..., None]], axis=2)
    for stride, size in seq_groups():
        stats = merge_stack(exchange(stats, "seq", SEQ_SIZE, stride, size))
    cache_running = stats[..., :HD]
    cache_highest = stats[..., HD]
    cache_totals = stats[..., HD + 1]

    q4 = queries.reshape(STEPS, R, local_heads, HD)
    k4 = new_keys.reshape(STEPS, R, local_heads, HD)
    v4 = new_values.reshape(STEPS, R, local_heads, HD)
    fresh_scores = (
        jnp.einsum("srhd,trhd->hsrt", q4, k4, preferred_element_type=jnp.float32) * score_scale
    )
    allowed = (jnp.arange(STEPS)[None, :] <= jnp.arange(STEPS)[:, None])[None, :, None, :]
    fresh_scores = jnp.where(allowed, fresh_scores, very_low)
    cache_highest = cache_highest.reshape(local_heads, STEPS, R)
    highest = jnp.maximum(cache_highest, jnp.max(fresh_scores, axis=-1))
    fresh_weights = jnp.where(allowed, jnp.exp(fresh_scores - highest[..., None]), 0.0)
    factor = jnp.exp(cache_highest - highest)
    final_totals = cache_totals.reshape(local_heads, STEPS, R) * factor + jnp.sum(fresh_weights, axis=-1)
    final_running = cache_running.reshape(local_heads, STEPS, R, HD) * factor[..., None] + jnp.einsum(
        "hsrt,trhd->hsrd", fresh_weights.astype(jnp.bfloat16), v4, preferred_element_type=jnp.float32
    )
    attended = (final_running / final_totals[..., None]).astype(jnp.bfloat16)
    attended = jnp.transpose(attended, (1, 2, 0, 3)).reshape(rows, local_width)

    sliced = seq_columns(attended, output_weight.shape[0])
    attention_out = seq_total(jnp.dot(sliced, output_weight, preferred_element_type=jnp.float32))
    attention_squares = feature_sums(jnp.sum(attention_out * attention_out, axis=1))
    hidden = (
        token_rows.astype(jnp.float32) + attention_out * inverse_rms(attention_squares) * attention_gain
    ).astype(jnp.bfloat16)

    hidden_cols = seq_columns(hidden, gate_weight.shape[0])
    hidden_units = gate_weight.shape[1]
    summed_both = seq_total(
        jnp.concatenate(
            [
                jnp.dot(hidden_cols, gate_weight, preferred_element_type=jnp.float32),
                jnp.dot(hidden_cols, up_weight, preferred_element_type=jnp.float32),
            ],
            axis=1,
        ),
        ladder=True,
    )
    active = (jax.nn.silu(summed_both[:, :hidden_units]) * summed_both[:, hidden_units:]).astype(
        jnp.bfloat16
    )
    active_cols = seq_columns(active, down_weight.shape[0])
    mlp_out = seq_total(jnp.dot(active_cols, down_weight, preferred_element_type=jnp.float32))
    mlp_squares = feature_sums(jnp.sum(mlp_out * mlp_out, axis=1))
    decoded = (
        hidden.astype(jnp.float32) + mlp_out * inverse_rms(mlp_squares) * feedforward_gain
    ).astype(jnp.bfloat16)
    return decoded.reshape(STEPS, R, local_width)


def solution(mesh):
    global SEQ_SIZE, MP_SIZE, SEQ_FACTORS
    SEQ_SIZE = mesh.shape["seq"]
    MP_SIZE = mesh.shape["mp"]
    factors = []
    left = SEQ_SIZE
    if left % 2 == 0:
        factors.append(2)
        left //= 2
    while left % 4 == 0:
        factors.append(4)
        left //= 4
    if left > 1:
        factors.append(left)
    SEQ_FACTORS = tuple(factors)
    in_specs = (
        P(None, None, "mp"),
        P("seq", "mp"),
        P("seq", "mp"),
        P("seq", "mp"),
        P("seq", "mp"),
        P("seq", "mp"),
        P("seq", "mp"),
        P("seq", "mp"),
        P("mp"),
        P("mp"),
        P("mp"),
        P("mp"),
        P("seq", None, "mp"),
        P("seq", None, "mp"),
        P(),
        P("seq"),
        P("seq"),
    )
    out_specs = P(None, None, "mp")
    return jax.shard_map(local, mesh=mesh, in_specs=in_specs, out_specs=out_specs, check_vma=False)
```

```python
import jax
import jax.numpy as jnp
from jax import lax
from jax.sharding import PartitionSpec as P

D = 2048
HD = 128
R = 16
STEPS = 4
PAGE = 256


epsilon = 1e-06
rope_base = 500000.0
very_low = -1e30
SEQ_SIZE = 32
MP_SIZE = 4
SEQ_FACTORS = (2, 4, 4)


def rotary(values, positions):
    half_width = HD // 2
    frequencies = rope_base ** (-2.0 * jnp.arange(half_width, dtype=jnp.float32) / HD)
    angles = positions.astype(jnp.float32)[:, None] * frequencies[None, :]
    cosine = jnp.cos(angles)[:, None, :]
    sine_part = jnp.sin(angles)[:, None, :]
    first_half = values[..., :half_width]
    second_half = values[..., half_width:]
    return jnp.concatenate(
        [
            first_half * cosine - second_half * sine_part,
            second_half * cosine + first_half * sine_part,
        ],
        axis=-1,
    )


def seq_columns(block, width):
    per = block.shape[1] // width
    seq = lax.axis_index("seq")
    piece = lax.dynamic_slice_in_dim(block, (seq % per) * width, width, 1)
    pairs = [
        (s * MP_SIZE + m, (m * per + s % per) * MP_SIZE + s // per)
        for s in range(SEQ_SIZE)
        for m in range(MP_SIZE)
    ]
    return lax.ppermute(piece, ("seq", "mp"), pairs)


def seq_groups():
    groups = []
    stride = 1
    for size in SEQ_FACTORS:
        groups.append((stride, size))
        stride *= size
    return groups


def digit_pairs(count, stride, size, shift):
    return [
        (i, i + (((i // stride) % size + shift) % size - (i // stride) % size) * stride)
        for i in range(count)
    ]


def exchange(value, axis, count, stride, size):
    digit = (lax.axis_index(axis) // stride) % size
    stack = jnp.zeros((size,) + value.shape, value.dtype)
    stack = lax.dynamic_update_index_in_dim(stack, value, digit, 0)
    for shift in range(1, size):
        received = lax.ppermute(value, axis, digit_pairs(count, stride, size, shift))
        stack = lax.dynamic_update_index_in_dim(stack, received, (digit - shift) % size, 0)
    return stack


def scatter_digit(current, stride, size):
    me = lax.axis_index("seq")
    digit = (me // stride) % size
    part = current.shape[1] // size
    total = lax.dynamic_slice_in_dim(current, digit * part, part, 1)
    for shift in range(1, size):
        send = lax.dynamic_slice_in_dim(current, ((digit + shift) % size) * part, part, 1)
        total = total + lax.ppermute(send, "seq", digit_pairs(SEQ_SIZE, stride, size, shift))
    return total


def gather_digit(current, stride, size):
    me = lax.axis_index("seq")
    digit = (me // stride) % size
    part = current.shape[1]
    whole = jnp.zeros((current.shape[0], part * size), current.dtype)
    whole = lax.dynamic_update_slice_in_dim(whole, current, digit * part, 1)
    for shift in range(1, size):
        received = lax.ppermute(current, "seq", digit_pairs(SEQ_SIZE, stride, size, shift))
        whole = lax.dynamic_update_slice_in_dim(whole, received, ((digit - shift) % size) * part, 1)
    return whole


def seq_total(partial_value, ladder=False):
    groups = seq_groups()
    current = partial_value
    if ladder:
        for stride, size in groups:
            current = scatter_digit(current, stride, size)
        for stride, size in reversed(groups):
            current = gather_digit(current, stride, size)
        return current
    stride, size = groups[0]
    current = scatter_digit(current, stride, size)
    for other_stride, other_size in groups[1:]:
        current = jnp.sum(exchange(current, "seq", SEQ_SIZE, other_stride, other_size), axis=0)
    return gather_digit(current, stride, size)


def gate_up_active(gate_part, up_part):
    rows, units = gate_part.shape
    unit_block = units // SEQ_SIZE
    arranged = jnp.stack(
        [gate_part.reshape(rows, SEQ_SIZE, unit_block), up_part.reshape(rows, SEQ_SIZE, unit_block)],
        axis=2,
    ).reshape(rows, 2 * units)
    groups = seq_groups()
    for stride, size in groups:
        arranged = scatter_digit(arranged, stride, size)
    active = (jax.nn.silu(arranged[:, :unit_block]) * arranged[:, unit_block:]).astype(jnp.bfloat16)
    last_stride, last_size = groups[-1]
    active = gather_digit(active, last_stride, last_size)
    per = SEQ_SIZE // MP_SIZE
    pairs = []
    for s in range(SEQ_SIZE):
        lead = 0
        for stride, size in groups[:-1]:
            lead = lead * size + (s // stride) % size
        last = (s // last_stride) % last_size
        for m in range(MP_SIZE):
            pairs.append((s * MP_SIZE + m, (m * per + lead) * MP_SIZE + last))
    return lax.ppermute(active, ("seq", "mp"), pairs)


def merge_stack(stack):
    member_max = stack[..., HD]
    highest = jnp.max(member_max, axis=0)
    scale = jnp.exp(member_max - highest[None])
    totals = jnp.sum(stack[..., HD + 1] * scale, axis=0)
    running = jnp.sum(stack[..., :HD] * scale[..., None], axis=0)
    return jnp.concatenate([running, highest[..., None], totals[..., None]], axis=-1)


def feature_sums(squares):
    return jnp.sum(exchange(squares, "mp", MP_SIZE, 1, MP_SIZE), axis=0)


def inverse_rms(square_total):
    return lax.rsqrt(square_total / D + epsilon)[:, None]


def local(
    states,
    query_weight,
    key_weight,
    value_weight,
    output_weight,
    gate_weight,
    up_weight,
    down_weight,
    query_gain,
    key_gain,
    attention_gain,
    feedforward_gain,
    key_cache,
    value_cache,
    lengths,
    page_owner,
    page_index,
):
    local_width = query_weight.shape[1]
    local_heads = local_width // HD
    rows = STEPS * R
    score_scale = HD ** (-0.5)
    token_rows = states.reshape(rows, local_width)
    positions = (lengths[None, :] + jnp.arange(STEPS, dtype=jnp.int32)[:, None]).reshape(rows)

    sliced = seq_columns(token_rows, query_weight.shape[0])
    summed = seq_total(
        jnp.concatenate(
            [
                jnp.dot(sliced, query_weight, preferred_element_type=jnp.float32),
                jnp.dot(sliced, key_weight, preferred_element_type=jnp.float32),
                jnp.dot(sliced, value_weight, preferred_element_type=jnp.float32),
            ],
            axis=1,
        )
    )
    query_raw = summed[:, :local_width]
    key_raw = summed[:, local_width : 2 * local_width]
    value_raw = summed[:, 2 * local_width :]
    squares = feature_sums(
        jnp.stack([jnp.sum(query_raw * query_raw, axis=1), jnp.sum(key_raw * key_raw, axis=1)], axis=1)
    )
    queries = rotary(
        (query_raw * inverse_rms(squares[:, 0]) * query_gain).reshape(rows, local_heads, HD), positions
    ).astype(jnp.bfloat16)
    new_keys = rotary(
        (key_raw * inverse_rms(squares[:, 1]) * key_gain).reshape(rows, local_heads, HD), positions
    ).astype(jnp.bfloat16)
    new_values = value_raw.astype(jnp.bfloat16).reshape(rows, local_heads, HD)

    pages = key_cache.shape[0]
    tokens = pages * PAGE
    keys = key_cache.reshape(tokens, local_width)
    values = value_cache.reshape(tokens, local_width)
    token_owner = jnp.repeat(page_owner, PAGE)
    token_spot = (page_index[:, None] * PAGE + jnp.arange(PAGE, dtype=jnp.int32)[None, :]).reshape(tokens)
    request_of_row = jnp.tile(jnp.arange(R, dtype=jnp.int32), STEPS)
    length_of_row = jnp.tile(lengths, STEPS)
    validity = (token_owner[None, :] == request_of_row[:, None]) & (
        token_spot[None, :] < length_of_row[:, None]
    )
    flat_queries = queries.reshape(rows, local_width)
    scores = jnp.stack(
        [
            lax.dot_general(
                flat_queries[:, h * HD : (h + 1) * HD],
                keys[:, h * HD : (h + 1) * HD],
                (((1,), (1,)), ((), ())),
                preferred_element_type=jnp.float32,
            )
            for h in range(local_heads)
        ]
    ) * score_scale
    masked = jnp.where(validity[None], scores, very_low)
    maxima = jnp.max(masked, axis=2)
    weights = jnp.where(validity[None], jnp.exp(masked - maxima[..., None]), 0.0)
    totals = jnp.sum(weights, axis=2)
    rounded = weights.astype(jnp.bfloat16)
    running = jnp.stack(
        [
            jnp.dot(rounded[h], values[:, h * HD : (h + 1) * HD], preferred_element_type=jnp.float32)
            for h in range(local_heads)
        ]
    )

    stats = jnp.concatenate([running, maxima[..., None], totals[..., None]], axis=2)
    for stride, size in seq_groups():
        stats = merge_stack(exchange(stats, "seq", SEQ_SIZE, stride, size))
    cache_running = stats[..., :HD]
    cache_highest = stats[..., HD]
    cache_totals = stats[..., HD + 1]

    q4 = queries.reshape(STEPS, R, local_heads, HD)
    k4 = new_keys.reshape(STEPS, R, local_heads, HD)
    v4 = new_values.reshape(STEPS, R, local_heads, HD)
    fresh_scores = (
        jnp.einsum("srhd,trhd->hsrt", q4, k4, preferred_element_type=jnp.float32) * score_scale
    )
    allowed = (jnp.arange(STEPS)[None, :] <= jnp.arange(STEPS)[:, None])[None, :, None, :]
    fresh_scores = jnp.where(allowed, fresh_scores, very_low)
    cache_highest = cache_highest.reshape(local_heads, STEPS, R)
    highest = jnp.maximum(cache_highest, jnp.max(fresh_scores, axis=-1))
    fresh_weights = jnp.where(allowed, jnp.exp(fresh_scores - highest[..., None]), 0.0)
    factor = jnp.exp(cache_highest - highest)
    final_totals = cache_totals.reshape(local_heads, STEPS, R) * factor + jnp.sum(fresh_weights, axis=-1)
    final_running = cache_running.reshape(local_heads, STEPS, R, HD) * factor[..., None] + jnp.einsum(
        "hsrt,trhd->hsrd", fresh_weights.astype(jnp.bfloat16), v4, preferred_element_type=jnp.float32
    )
    attended = (final_running / final_totals[..., None]).astype(jnp.bfloat16)
    attended = jnp.transpose(attended, (1, 2, 0, 3)).reshape(rows, local_width)

    sliced = seq_columns(attended, output_weight.shape[0])
    attention_out = seq_total(jnp.dot(sliced, output_weight, preferred_element_type=jnp.float32))
    attention_squares = feature_sums(jnp.sum(attention_out * attention_out, axis=1))
    hidden = (
        token_rows.astype(jnp.float32) + attention_out * inverse_rms(attention_squares) * attention_gain
    ).astype(jnp.bfloat16)

    hidden_cols = seq_columns(hidden, gate_weight.shape[0])
    active_cols = gate_up_active(
        jnp.dot(hidden_cols, gate_weight, preferred_element_type=jnp.float32),
        jnp.dot(hidden_cols, up_weight, preferred_element_type=jnp.float32),
    )
    mlp_out = seq_total(jnp.dot(active_cols, down_weight, preferred_element_type=jnp.float32))
    mlp_squares = feature_sums(jnp.sum(mlp_out * mlp_out, axis=1))
    decoded = (
        hidden.astype(jnp.float32) + mlp_out * inverse_rms(mlp_squares) * feedforward_gain
    ).astype(jnp.bfloat16)
    return decoded.reshape(STEPS, R, local_width)


def solution(mesh):
    global SEQ_SIZE, MP_SIZE, SEQ_FACTORS
    SEQ_SIZE = mesh.shape["seq"]
    MP_SIZE = mesh.shape["mp"]
    factors = []
    left = SEQ_SIZE // MP_SIZE
    if left % 2 == 0:
        factors.append(2)
        left //= 2
    while left % 4 == 0:
        factors.append(4)
        left //= 4
    if left > 1:
        factors.append(left)
    factors.append(MP_SIZE)
    SEQ_FACTORS = tuple(factors)
    in_specs = (
        P(None, None, "mp"),
        P("seq", "mp"),
        P("seq", "mp"),
        P("seq", "mp"),
        P("seq", "mp"),
        P("seq", "mp"),
        P("seq", "mp"),
        P("seq", "mp"),
        P("mp"),
        P("mp"),
        P("mp"),
        P("mp"),
        P("seq", None, "mp"),
        P("seq", None, "mp"),
        P(),
        P("seq"),
        P("seq"),
    )
    out_specs = P(None, None, "mp")
    return jax.shard_map(local, mesh=mesh, in_specs=in_specs, out_specs=out_specs, check_vma=False)
```

```python
import jax
import jax.numpy as jnp
from jax import lax
from jax.sharding import PartitionSpec as P

D = 2048
HD = 128
R = 16
STEPS = 4
PAGE = 256


epsilon = 1e-06
rope_base = 500000.0
very_low = -1e30
SEQ_SIZE = 32
MP_SIZE = 4
SEQ_FACTORS = (2, 4, 4)


def rotary(values, positions):
    half_width = HD // 2
    frequencies = rope_base ** (-2.0 * jnp.arange(half_width, dtype=jnp.float32) / HD)
    angles = positions.astype(jnp.float32)[:, None] * frequencies[None, :]
    cosine = jnp.cos(angles)[:, None, :]
    sine_part = jnp.sin(angles)[:, None, :]
    first_half = values[..., :half_width]
    second_half = values[..., half_width:]
    return jnp.concatenate(
        [
            first_half * cosine - second_half * sine_part,
            second_half * cosine + first_half * sine_part,
        ],
        axis=-1,
    )


def seq_columns(block, width):
    per = block.shape[1] // width
    seq = lax.axis_index("seq")
    piece = lax.dynamic_slice_in_dim(block, (seq % per) * width, width, 1)
    pairs = [
        (s * MP_SIZE + m, (m * per + s % per) * MP_SIZE + s // per)
        for s in range(SEQ_SIZE)
        for m in range(MP_SIZE)
    ]
    return lax.ppermute(piece, ("seq", "mp"), pairs)


def seq_groups():
    groups = []
    stride = 1
    for size in SEQ_FACTORS:
        groups.append((stride, size))
        stride *= size
    return groups


def digit_pairs(count, stride, size, shift):
    return [
        (i, i + (((i // stride) % size + shift) % size - (i // stride) % size) * stride)
        for i in range(count)
    ]


def exchange(value, axis, count, stride, size):
    digit = (lax.axis_index(axis) // stride) % size
    stack = jnp.zeros((size,) + value.shape, value.dtype)
    stack = lax.dynamic_update_index_in_dim(stack, value, digit, 0)
    for shift in range(1, size):
        received = lax.ppermute(value, axis, digit_pairs(count, stride, size, shift))
        stack = lax.dynamic_update_index_in_dim(stack, received, (digit - shift) % size, 0)
    return stack


def scatter_digit(current, stride, size):
    me = lax.axis_index("seq")
    digit = (me // stride) % size
    part = current.shape[1] // size
    total = lax.dynamic_slice_in_dim(current, digit * part, part, 1)
    for shift in range(1, size):
        send = lax.dynamic_slice_in_dim(current, ((digit + shift) % size) * part, part, 1)
        total = total + lax.ppermute(send, "seq", digit_pairs(SEQ_SIZE, stride, size, shift))
    return total


def gather_digit(current, stride, size):
    me = lax.axis_index("seq")
    digit = (me // stride) % size
    part = current.shape[1]
    whole = jnp.zeros((current.shape[0], part * size), current.dtype)
    whole = lax.dynamic_update_slice_in_dim(whole, current, digit * part, 1)
    for shift in range(1, size):
        received = lax.ppermute(current, "seq", digit_pairs(SEQ_SIZE, stride, size, shift))
        whole = lax.dynamic_update_slice_in_dim(whole, received, ((digit - shift) % size) * part, 1)
    return whole


def seq_total(partial_value, ladder=False, butterfly=False):
    groups = seq_groups()
    current = partial_value
    if ladder:
        for stride, size in groups:
            current = scatter_digit(current, stride, size)
        for stride, size in reversed(groups):
            current = gather_digit(current, stride, size)
        return current
    if butterfly:
        for stride, size in groups:
            current = jnp.sum(exchange(current, "seq", SEQ_SIZE, stride, size), axis=0)
        return current
    stride, size = groups[0]
    current = scatter_digit(current, stride, size)
    for other_stride, other_size in groups[1:]:
        current = jnp.sum(exchange(current, "seq", SEQ_SIZE, other_stride, other_size), axis=0)
    return gather_digit(current, stride, size)


def gate_up_active(gate_part, up_part):
    rows, units = gate_part.shape
    unit_block = units // SEQ_SIZE
    arranged = jnp.stack(
        [gate_part.reshape(rows, SEQ_SIZE, unit_block), up_part.reshape(rows, SEQ_SIZE, unit_block)],
        axis=2,
    ).reshape(rows, 2 * units)
    groups = seq_groups()
    for stride, size in groups:
        arranged = scatter_digit(arranged, stride, size)
    active = (jax.nn.silu(arranged[:, :unit_block]) * arranged[:, unit_block:]).astype(jnp.bfloat16)
    last_stride, last_size = groups[-1]
    active = gather_digit(active, last_stride, last_size)
    per = SEQ_SIZE // MP_SIZE
    pairs = []
    for s in range(SEQ_SIZE):
        lead = 0
        for stride, size in groups[:-1]:
            lead = lead * size + (s // stride) % size
        last = (s // last_stride) % last_size
        for m in range(MP_SIZE):
            pairs.append((s * MP_SIZE + m, (m * per + lead) * MP_SIZE + last))
    return lax.ppermute(active, ("seq", "mp"), pairs)


def merge_stack(stack):
    member_max = stack[..., HD]
    highest = jnp.max(member_max, axis=0)
    scale = jnp.exp(member_max - highest[None])
    totals = jnp.sum(stack[..., HD + 1] * scale, axis=0)
    running = jnp.sum(stack[..., :HD] * scale[..., None], axis=0)
    return jnp.concatenate([running, highest[..., None], totals[..., None]], axis=-1)


def feature_sums(squares):
    return jnp.sum(exchange(squares, "mp", MP_SIZE, 1, MP_SIZE), axis=0)


def inverse_rms(square_total):
    return lax.rsqrt(square_total / D + epsilon)[:, None]


def local(
    states,
    query_weight,
    key_weight,
    value_weight,
    output_weight,
    gate_weight,
    up_weight,
    down_weight,
    query_gain,
    key_gain,
    attention_gain,
    feedforward_gain,
    key_cache,
    value_cache,
    lengths,
    page_owner,
    page_index,
):
    local_width = query_weight.shape[1]
    local_heads = local_width // HD
    rows = STEPS * R
    score_scale = HD ** (-0.5)
    token_rows = states.reshape(rows, local_width)
    positions = (lengths[None, :] + jnp.arange(STEPS, dtype=jnp.int32)[:, None]).reshape(rows)

    sliced = seq_columns(token_rows, query_weight.shape[0])
    summed = seq_total(
        jnp.concatenate(
            [
                jnp.dot(sliced, query_weight, preferred_element_type=jnp.float32),
                jnp.dot(sliced, key_weight, preferred_element_type=jnp.float32),
                jnp.dot(sliced, value_weight, preferred_element_type=jnp.float32),
            ],
            axis=1,
        )
    )
    query_raw = summed[:, :local_width]
    key_raw = summed[:, local_width : 2 * local_width]
    value_raw = summed[:, 2 * local_width :]
    squares = feature_sums(
        jnp.stack([jnp.sum(query_raw * query_raw, axis=1), jnp.sum(key_raw * key_raw, axis=1)], axis=1)
    )
    queries = rotary(
        (query_raw * inverse_rms(squares[:, 0]) * query_gain).reshape(rows, local_heads, HD), positions
    ).astype(jnp.bfloat16)
    new_keys = rotary(
        (key_raw * inverse_rms(squares[:, 1]) * key_gain).reshape(rows, local_heads, HD), positions
    ).astype(jnp.bfloat16)
    new_values = value_raw.astype(jnp.bfloat16).reshape(rows, local_heads, HD)

    pages = key_cache.shape[0]
    tokens = pages * PAGE
    keys = key_cache.reshape(tokens, local_width)
    values = value_cache.reshape(tokens, local_width)
    token_owner = jnp.repeat(page_owner, PAGE)
    token_spot = (page_index[:, None] * PAGE + jnp.arange(PAGE, dtype=jnp.int32)[None, :]).reshape(tokens)
    request_of_row = jnp.tile(jnp.arange(R, dtype=jnp.int32), STEPS)
    length_of_row = jnp.tile(lengths, STEPS)
    validity = (token_owner[None, :] == request_of_row[:, None]) & (
        token_spot[None, :] < length_of_row[:, None]
    )
    flat_queries = queries.reshape(rows, local_width)
    scores = jnp.stack(
        [
            lax.dot_general(
                flat_queries[:, h * HD : (h + 1) * HD],
                keys[:, h * HD : (h + 1) * HD],
                (((1,), (1,)), ((), ())),
                preferred_element_type=jnp.float32,
            )
            for h in range(local_heads)
        ]
    ) * score_scale
    masked = jnp.where(validity[None], scores, very_low)
    maxima = jnp.max(masked, axis=2)
    weights = jnp.where(validity[None], jnp.exp(masked - maxima[..., None]), 0.0)
    totals = jnp.sum(weights, axis=2)
    rounded = weights.astype(jnp.bfloat16)
    running = jnp.stack(
        [
            jnp.dot(rounded[h], values[:, h * HD : (h + 1) * HD], preferred_element_type=jnp.float32)
            for h in range(local_heads)
        ]
    )

    seq = lax.axis_index("seq")
    slice_width = local_width // SEQ_SIZE
    per_head = HD // slice_width
    send = jnp.concatenate(
        [
            running.reshape(local_heads, rows, per_head, slice_width).transpose(0, 2, 1, 3),
            jnp.broadcast_to(maxima[:, None, :, None], (local_heads, per_head, rows, 1)),
            jnp.broadcast_to(totals[:, None, :, None], (local_heads, per_head, rows, 1)),
        ],
        axis=3,
    ).reshape(SEQ_SIZE, rows, slice_width + 2)
    sources = lax.all_to_all(send, "seq", 0, 0, tiled=True)
    source_max = sources[..., slice_width]
    cache_highest = jnp.max(source_max, axis=0)
    scale = jnp.exp(source_max - cache_highest[None])
    cache_totals = jnp.sum(sources[..., slice_width + 1] * scale, axis=0)
    cache_running = jnp.sum(sources[..., :slice_width] * scale[..., None], axis=0)

    head = seq // per_head
    offset = (seq % per_head) * slice_width
    q4 = lax.dynamic_index_in_dim(queries, head, 1, keepdims=False).reshape(STEPS, R, HD)
    k4 = lax.dynamic_index_in_dim(new_keys, head, 1, keepdims=False).reshape(STEPS, R, HD)
    v4 = lax.dynamic_slice_in_dim(
        lax.dynamic_index_in_dim(new_values, head, 1, keepdims=False), offset, slice_width, 1
    ).reshape(STEPS, R, slice_width)
    fresh_scores = jnp.einsum("srd,trd->srt", q4, k4, preferred_element_type=jnp.float32) * score_scale
    allowed = (jnp.arange(STEPS)[None, :] <= jnp.arange(STEPS)[:, None])[:, None, :]
    fresh_scores = jnp.where(allowed, fresh_scores, very_low)
    cache_highest = cache_highest.reshape(STEPS, R)
    highest = jnp.maximum(cache_highest, jnp.max(fresh_scores, axis=-1))
    fresh_weights = jnp.where(allowed, jnp.exp(fresh_scores - highest[..., None]), 0.0)
    factor = jnp.exp(cache_highest - highest)
    final_totals = cache_totals.reshape(STEPS, R) * factor + jnp.sum(fresh_weights, axis=-1)
    final_running = cache_running.reshape(STEPS, R, slice_width) * factor[..., None] + jnp.einsum(
        "srt,trd->srd", fresh_weights.astype(jnp.bfloat16), v4, preferred_element_type=jnp.float32
    )
    attended = (final_running / final_totals[..., None]).astype(jnp.bfloat16).reshape(rows, slice_width)

    width = output_weight.shape[0]
    per = local_width // width
    holders = width // slice_width
    sliced = jnp.zeros((rows, width), jnp.bfloat16)
    mp = lax.axis_index("mp")
    for shift in range(MP_SIZE):
        pairs = [
            (s * MP_SIZE + m, (m * per + s // holders) * MP_SIZE + (s % holders + shift) % MP_SIZE)
            for s in range(SEQ_SIZE)
            for m in range(MP_SIZE)
        ]
        received = lax.ppermute(attended, ("seq", "mp"), pairs)
        sliced = lax.dynamic_update_slice_in_dim(
            sliced, received, ((mp - shift) % MP_SIZE) * slice_width, 1
        )
    attention_out = seq_total(
        jnp.dot(sliced, output_weight, preferred_element_type=jnp.float32), butterfly=True
    )
    attention_squares = feature_sums(jnp.sum(attention_out * attention_out, axis=1))
    hidden = (
        token_rows.astype(jnp.float32) + attention_out * inverse_rms(attention_squares) * attention_gain
    ).astype(jnp.bfloat16)

    hidden_cols = seq_columns(hidden, gate_weight.shape[0])
    active_cols = gate_up_active(
        jnp.dot(hidden_cols, gate_weight, preferred_element_type=jnp.float32),
        jnp.dot(hidden_cols, up_weight, preferred_element_type=jnp.float32),
    )
    mlp_out = seq_total(
        jnp.dot(active_cols, down_weight, preferred_element_type=jnp.float32), butterfly=True
    )
    mlp_squares = feature_sums(jnp.sum(mlp_out * mlp_out, axis=1))
    decoded = (
        hidden.astype(jnp.float32) + mlp_out * inverse_rms(mlp_squares) * feedforward_gain
    ).astype(jnp.bfloat16)
    return decoded.reshape(STEPS, R, local_width)


def solution(mesh):
    global SEQ_SIZE, MP_SIZE, SEQ_FACTORS
    SEQ_SIZE = mesh.shape["seq"]
    MP_SIZE = mesh.shape["mp"]
    factors = []
    left = SEQ_SIZE // MP_SIZE
    if left % 2 == 0:
        factors.append(2)
        left //= 2
    while left % 4 == 0:
        factors.append(4)
        left //= 4
    if left > 1:
        factors.append(left)
    factors.append(MP_SIZE)
    SEQ_FACTORS = tuple(factors)
    in_specs = (
        P(None, None, "mp"),
        P("seq", "mp"),
        P("seq", "mp"),
        P("seq", "mp"),
        P("seq", "mp"),
        P("seq", "mp"),
        P("seq", "mp"),
        P("seq", "mp"),
        P("mp"),
        P("mp"),
        P("mp"),
        P("mp"),
        P("seq", None, "mp"),
        P("seq", None, "mp"),
        P(),
        P("seq"),
        P("seq"),
    )
    out_specs = P(None, None, "mp")
    return jax.shard_map(local, mesh=mesh, in_specs=in_specs, out_specs=out_specs, check_vma=False)
```

```python
import jax
import jax.numpy as jnp
from jax import lax
from jax.sharding import PartitionSpec as P

D = 2048
HD = 128
R = 16
STEPS = 4
PAGE = 256


epsilon = 1e-06
rope_base = 500000.0
very_low = -1e30
SEQ_SIZE = 32
MP_SIZE = 4
SEQ_FACTORS = (2, 4, 4)


def rotary(values, positions):
    half_width = HD // 2
    frequencies = rope_base ** (-2.0 * jnp.arange(half_width, dtype=jnp.float32) / HD)
    angles = positions.astype(jnp.float32)[:, None] * frequencies[None, :]
    cosine = jnp.cos(angles)[:, None, :]
    sine_part = jnp.sin(angles)[:, None, :]
    first_half = values[..., :half_width]
    second_half = values[..., half_width:]
    return jnp.concatenate(
        [
            first_half * cosine - second_half * sine_part,
            second_half * cosine + first_half * sine_part,
        ],
        axis=-1,
    )


def seq_columns(block, width):
    per = block.shape[1] // width
    seq = lax.axis_index("seq")
    piece = lax.dynamic_slice_in_dim(block, (seq % per) * width, width, 1)
    pairs = [
        (s * MP_SIZE + m, (m * per + s % per) * MP_SIZE + s // per)
        for s in range(SEQ_SIZE)
        for m in range(MP_SIZE)
    ]
    return lax.ppermute(piece, ("seq", "mp"), pairs)


def seq_groups():
    groups = []
    stride = 1
    for size in SEQ_FACTORS:
        groups.append((stride, size))
        stride *= size
    return groups


def digit_pairs(count, stride, size, shift):
    return [
        (i, i + (((i // stride) % size + shift) % size - (i // stride) % size) * stride)
        for i in range(count)
    ]


def exchange(value, axis, count, stride, size):
    digit = (lax.axis_index(axis) // stride) % size
    stack = jnp.zeros((size,) + value.shape, value.dtype)
    stack = lax.dynamic_update_index_in_dim(stack, value, digit, 0)
    for shift in range(1, size):
        received = lax.ppermute(value, axis, digit_pairs(count, stride, size, shift))
        stack = lax.dynamic_update_index_in_dim(stack, received, (digit - shift) % size, 0)
    return stack


def scatter_digit(current, stride, size):
    me = lax.axis_index("seq")
    digit = (me // stride) % size
    part = current.shape[1] // size
    total = lax.dynamic_slice_in_dim(current, digit * part, part, 1)
    for shift in range(1, size):
        send = lax.dynamic_slice_in_dim(current, ((digit + shift) % size) * part, part, 1)
        total = total + lax.ppermute(send, "seq", digit_pairs(SEQ_SIZE, stride, size, shift))
    return total


def gather_digit(current, stride, size):
    me = lax.axis_index("seq")
    digit = (me // stride) % size
    part = current.shape[1]
    whole = jnp.zeros((current.shape[0], part * size), current.dtype)
    whole = lax.dynamic_update_slice_in_dim(whole, current, digit * part, 1)
    for shift in range(1, size):
        received = lax.ppermute(current, "seq", digit_pairs(SEQ_SIZE, stride, size, shift))
        whole = lax.dynamic_update_slice_in_dim(whole, received, ((digit - shift) % size) * part, 1)
    return whole


def seq_total(partial_value, ladder=False, butterfly=False):
    groups = seq_groups()
    current = partial_value
    if ladder:
        for stride, size in groups:
            current = scatter_digit(current, stride, size)
        for stride, size in reversed(groups):
            current = gather_digit(current, stride, size)
        return current
    if butterfly:
        for stride, size in groups:
            current = jnp.sum(exchange(current, "seq", SEQ_SIZE, stride, size), axis=0)
        return current
    stride, size = groups[0]
    current = scatter_digit(current, stride, size)
    for other_stride, other_size in groups[1:]:
        current = jnp.sum(exchange(current, "seq", SEQ_SIZE, other_stride, other_size), axis=0)
    return gather_digit(current, stride, size)


def gate_up_active(gate_part, up_part):
    rows, units = gate_part.shape
    unit_block = units // SEQ_SIZE
    arranged = jnp.stack(
        [gate_part.reshape(rows, SEQ_SIZE, unit_block), up_part.reshape(rows, SEQ_SIZE, unit_block)],
        axis=2,
    ).reshape(rows, 2 * units)
    groups = seq_groups()
    for stride, size in groups:
        arranged = scatter_digit(arranged, stride, size)
    active = (jax.nn.silu(arranged[:, :unit_block]) * arranged[:, unit_block:]).astype(jnp.bfloat16)
    last_stride, last_size = groups[-1]
    active = gather_digit(active, last_stride, last_size)
    per = SEQ_SIZE // MP_SIZE
    pairs = []
    for s in range(SEQ_SIZE):
        lead = 0
        for stride, size in groups[:-1]:
            lead = lead * size + (s // stride) % size
        last = (s // last_stride) % last_size
        for m in range(MP_SIZE):
            pairs.append((s * MP_SIZE + m, (m * per + lead) * MP_SIZE + last))
    return lax.ppermute(active, ("seq", "mp"), pairs)


def merge_stack(stack):
    member_max = stack[..., HD]
    highest = jnp.max(member_max, axis=0)
    scale = jnp.exp(member_max - highest[None])
    totals = jnp.sum(stack[..., HD + 1] * scale, axis=0)
    running = jnp.sum(stack[..., :HD] * scale[..., None], axis=0)
    return jnp.concatenate([running, highest[..., None], totals[..., None]], axis=-1)


def feature_sums(squares):
    return jnp.sum(exchange(squares, "mp", MP_SIZE, 1, MP_SIZE), axis=0)


def inverse_rms(square_total):
    return lax.rsqrt(square_total / D + epsilon)[:, None]


def local(
    states,
    query_weight,
    key_weight,
    value_weight,
    output_weight,
    gate_weight,
    up_weight,
    down_weight,
    query_gain,
    key_gain,
    attention_gain,
    feedforward_gain,
    key_cache,
    value_cache,
    lengths,
    page_owner,
    page_index,
):
    local_width = query_weight.shape[1]
    local_heads = local_width // HD
    rows = STEPS * R
    score_scale = HD ** (-0.5)
    token_rows = states.reshape(rows, local_width)
    positions = (lengths[None, :] + jnp.arange(STEPS, dtype=jnp.int32)[:, None]).reshape(rows)

    sliced = seq_columns(token_rows, query_weight.shape[0])
    summed = seq_total(
        jnp.concatenate(
            [
                jnp.dot(sliced, query_weight, preferred_element_type=jnp.float32),
                jnp.dot(sliced, key_weight, preferred_element_type=jnp.float32),
                jnp.dot(sliced, value_weight, preferred_element_type=jnp.float32),
            ],
            axis=1,
        )
    )
    query_raw = summed[:, :local_width]
    key_raw = summed[:, local_width : 2 * local_width]
    value_raw = summed[:, 2 * local_width :]
    squares = feature_sums(
        jnp.stack([jnp.sum(query_raw * query_raw, axis=1), jnp.sum(key_raw * key_raw, axis=1)], axis=1)
    )
    queries = rotary(
        (query_raw * inverse_rms(squares[:, 0]) * query_gain).reshape(rows, local_heads, HD), positions
    ).astype(jnp.bfloat16)
    new_keys = rotary(
        (key_raw * inverse_rms(squares[:, 1]) * key_gain).reshape(rows, local_heads, HD), positions
    ).astype(jnp.bfloat16)
    new_values = value_raw.astype(jnp.bfloat16).reshape(rows, local_heads, HD)

    pages = key_cache.shape[0]
    tokens = pages * PAGE
    keys = key_cache.reshape(tokens, local_width)
    values = value_cache.reshape(tokens, local_width)
    token_owner = jnp.repeat(page_owner, PAGE)
    token_spot = (page_index[:, None] * PAGE + jnp.arange(PAGE, dtype=jnp.int32)[None, :]).reshape(tokens)
    request_of_row = jnp.tile(jnp.arange(R, dtype=jnp.int32), STEPS)
    length_of_row = jnp.tile(lengths, STEPS)
    validity = (token_owner[None, :] == request_of_row[:, None]) & (
        token_spot[None, :] < length_of_row[:, None]
    )
    flat_queries = queries.reshape(rows, local_width)
    scores = jnp.stack(
        [
            lax.dot_general(
                flat_queries[:, h * HD : (h + 1) * HD],
                keys[:, h * HD : (h + 1) * HD],
                (((1,), (1,)), ((), ())),
                preferred_element_type=jnp.float32,
            )
            for h in range(local_heads)
        ]
    ) * score_scale
    masked = jnp.where(validity[None], scores, very_low)
    maxima = jnp.max(masked, axis=2)
    weights = jnp.where(validity[None], jnp.exp(masked - maxima[..., None]), 0.0)
    totals = jnp.sum(weights, axis=2)
    rounded = weights.astype(jnp.bfloat16)
    running = jnp.stack(
        [
            jnp.dot(rounded[h], values[:, h * HD : (h + 1) * HD], preferred_element_type=jnp.float32)
            for h in range(local_heads)
        ]
    )

    seq = lax.axis_index("seq")
    slice_width = local_width // SEQ_SIZE
    per_head = HD // slice_width
    send = jnp.concatenate(
        [
            running.reshape(local_heads, rows, per_head, slice_width).transpose(0, 2, 1, 3),
            jnp.broadcast_to(maxima[:, None, :, None], (local_heads, per_head, rows, 1)),
            jnp.broadcast_to(totals[:, None, :, None], (local_heads, per_head, rows, 1)),
        ],
        axis=3,
    ).reshape(SEQ_SIZE, rows, slice_width + 2)
    sources = lax.all_to_all(send, "seq", 0, 0, tiled=True)
    source_max = sources[..., slice_width]
    cache_highest = jnp.max(source_max, axis=0)
    scale = jnp.exp(source_max - cache_highest[None])
    cache_totals = jnp.sum(sources[..., slice_width + 1] * scale, axis=0)
    cache_running = jnp.sum(sources[..., :slice_width] * scale[..., None], axis=0)

    head = seq // per_head
    offset = (seq % per_head) * slice_width
    q4 = lax.dynamic_index_in_dim(queries, head, 1, keepdims=False).reshape(STEPS, R, HD)
    k4 = lax.dynamic_index_in_dim(new_keys, head, 1, keepdims=False).reshape(STEPS, R, HD)
    v4 = lax.dynamic_slice_in_dim(
        lax.dynamic_index_in_dim(new_values, head, 1, keepdims=False), offset, slice_width, 1
    ).reshape(STEPS, R, slice_width)
    fresh_scores = jnp.einsum("srd,trd->srt", q4, k4, preferred_element_type=jnp.float32) * score_scale
    allowed = (jnp.arange(STEPS)[None, :] <= jnp.arange(STEPS)[:, None])[:, None, :]
    fresh_scores = jnp.where(allowed, fresh_scores, very_low)
    cache_highest = cache_highest.reshape(STEPS, R)
    highest = jnp.maximum(cache_highest, jnp.max(fresh_scores, axis=-1))
    fresh_weights = jnp.where(allowed, jnp.exp(fresh_scores - highest[..., None]), 0.0)
    factor = jnp.exp(cache_highest - highest)
    final_totals = cache_totals.reshape(STEPS, R) * factor + jnp.sum(fresh_weights, axis=-1)
    final_running = cache_running.reshape(STEPS, R, slice_width) * factor[..., None] + jnp.einsum(
        "srt,trd->srd", fresh_weights.astype(jnp.bfloat16), v4, preferred_element_type=jnp.float32
    )
    attended = (final_running / final_totals[..., None]).astype(jnp.bfloat16).reshape(rows, slice_width)

    width = output_weight.shape[0]
    per = local_width // width
    holders = width // slice_width
    sliced = jnp.zeros((rows, width), jnp.bfloat16)
    mp = lax.axis_index("mp")
    for shift in range(MP_SIZE):
        pairs = [
            (s * MP_SIZE + m, (m * per + s // holders) * MP_SIZE + (s % holders + shift) % MP_SIZE)
            for s in range(SEQ_SIZE)
            for m in range(MP_SIZE)
        ]
        received = lax.ppermute(attended, ("seq", "mp"), pairs)
        sliced = lax.dynamic_update_slice_in_dim(
            sliced, received, ((mp - shift) % MP_SIZE) * slice_width, 1
        )
    attention_out = seq_total(
        jnp.dot(sliced, output_weight, preferred_element_type=jnp.float32)
    )
    attention_squares = feature_sums(jnp.sum(attention_out * attention_out, axis=1))
    hidden = (
        token_rows.astype(jnp.float32) + attention_out * inverse_rms(attention_squares) * attention_gain
    ).astype(jnp.bfloat16)

    hidden_cols = seq_columns(hidden, gate_weight.shape[0])
    active_cols = gate_up_active(
        jnp.dot(hidden_cols, gate_weight, preferred_element_type=jnp.float32),
        jnp.dot(hidden_cols, up_weight, preferred_element_type=jnp.float32),
    )
    mlp_out = seq_total(
        jnp.dot(active_cols, down_weight, preferred_element_type=jnp.float32)
    )
    mlp_squares = feature_sums(jnp.sum(mlp_out * mlp_out, axis=1))
    decoded = (
        hidden.astype(jnp.float32) + mlp_out * inverse_rms(mlp_squares) * feedforward_gain
    ).astype(jnp.bfloat16)
    return decoded.reshape(STEPS, R, local_width)


def solution(mesh):
    global SEQ_SIZE, MP_SIZE, SEQ_FACTORS
    SEQ_SIZE = mesh.shape["seq"]
    MP_SIZE = mesh.shape["mp"]
    factors = []
    left = SEQ_SIZE // MP_SIZE
    if left % 2 == 0:
        factors.append(2)
        left //= 2
    while left % 4 == 0:
        factors.append(4)
        left //= 4
    if left > 1:
        factors.append(left)
    factors.append(MP_SIZE)
    SEQ_FACTORS = tuple(factors)
    in_specs = (
        P(None, None, "mp"),
        P("seq", "mp"),
        P("seq", "mp"),
        P("seq", "mp"),
        P("seq", "mp"),
        P("seq", "mp"),
        P("seq", "mp"),
        P("seq", "mp"),
        P("mp"),
        P("mp"),
        P("mp"),
        P("mp"),
        P("seq", None, "mp"),
        P("seq", None, "mp"),
        P(),
        P("seq"),
        P("seq"),
    )
    out_specs = P(None, None, "mp")
    return jax.shard_map(local, mesh=mesh, in_specs=in_specs, out_specs=out_specs, check_vma=False)
```

```python
import jax
import jax.numpy as jnp
from jax import lax
from jax.sharding import PartitionSpec as P

D = 2048
HD = 128
R = 16
STEPS = 4
PAGE = 256


epsilon = 1e-06
rope_base = 500000.0
very_low = -1e30
SEQ_SIZE = 32
MP_SIZE = 4
SEQ_FACTORS = (2, 4, 4)


def rotary(values, positions):
    half_width = HD // 2
    frequencies = rope_base ** (-2.0 * jnp.arange(half_width, dtype=jnp.float32) / HD)
    angles = positions.astype(jnp.float32)[:, None] * frequencies[None, :]
    cosine = jnp.cos(angles)[:, None, :]
    sine_part = jnp.sin(angles)[:, None, :]
    first_half = values[..., :half_width]
    second_half = values[..., half_width:]
    return jnp.concatenate(
        [
            first_half * cosine - second_half * sine_part,
            second_half * cosine + first_half * sine_part,
        ],
        axis=-1,
    )


def seq_columns(block, width):
    per = block.shape[1] // width
    seq = lax.axis_index("seq")
    piece = lax.dynamic_slice_in_dim(block, (seq % per) * width, width, 1)
    pairs = [
        (s * MP_SIZE + m, (m * per + s % per) * MP_SIZE + s // per)
        for s in range(SEQ_SIZE)
        for m in range(MP_SIZE)
    ]
    return lax.ppermute(piece, ("seq", "mp"), pairs)


def seq_groups():
    groups = []
    stride = 1
    for size in SEQ_FACTORS:
        groups.append((stride, size))
        stride *= size
    return groups


def digit_pairs(count, stride, size, shift):
    return [
        (i, i + (((i // stride) % size + shift) % size - (i // stride) % size) * stride)
        for i in range(count)
    ]


def exchange(value, axis, count, stride, size):
    digit = (lax.axis_index(axis) // stride) % size
    stack = jnp.zeros((size,) + value.shape, value.dtype)
    stack = lax.dynamic_update_index_in_dim(stack, value, digit, 0)
    for shift in range(1, size):
        received = lax.ppermute(value, axis, digit_pairs(count, stride, size, shift))
        stack = lax.dynamic_update_index_in_dim(stack, received, (digit - shift) % size, 0)
    return stack


def scatter_digit(current, stride, size):
    me = lax.axis_index("seq")
    digit = (me // stride) % size
    part = current.shape[1] // size
    total = lax.dynamic_slice_in_dim(current, digit * part, part, 1)
    for shift in range(1, size):
        send = lax.dynamic_slice_in_dim(current, ((digit + shift) % size) * part, part, 1)
        total = total + lax.ppermute(send, "seq", digit_pairs(SEQ_SIZE, stride, size, shift))
    return total


def gather_digit(current, stride, size):
    me = lax.axis_index("seq")
    digit = (me // stride) % size
    part = current.shape[1]
    whole = jnp.zeros((current.shape[0], part * size), current.dtype)
    whole = lax.dynamic_update_slice_in_dim(whole, current, digit * part, 1)
    for shift in range(1, size):
        received = lax.ppermute(current, "seq", digit_pairs(SEQ_SIZE, stride, size, shift))
        whole = lax.dynamic_update_slice_in_dim(whole, received, ((digit - shift) % size) * part, 1)
    return whole


def seq_total(partial_value, ladder=False, butterfly=False):
    groups = seq_groups()
    current = partial_value
    if ladder:
        for stride, size in groups:
            current = scatter_digit(current, stride, size)
        for stride, size in reversed(groups):
            current = gather_digit(current, stride, size)
        return current
    if butterfly:
        for stride, size in groups:
            current = jnp.sum(exchange(current, "seq", SEQ_SIZE, stride, size), axis=0)
        return current
    stride, size = groups[0]
    current = scatter_digit(current, stride, size)
    for other_stride, other_size in groups[1:]:
        current = jnp.sum(exchange(current, "seq", SEQ_SIZE, other_stride, other_size), axis=0)
    return gather_digit(current, stride, size)


def gate_up_active(gate_part, up_part):
    rows, units = gate_part.shape
    unit_block = units // SEQ_SIZE
    arranged = jnp.stack(
        [gate_part.reshape(rows, SEQ_SIZE, unit_block), up_part.reshape(rows, SEQ_SIZE, unit_block)],
        axis=2,
    ).reshape(rows, 2 * units)
    groups = seq_groups()
    for stride, size in groups:
        arranged = scatter_digit(arranged, stride, size)
    active = (jax.nn.silu(arranged[:, :unit_block]) * arranged[:, unit_block:]).astype(jnp.bfloat16)
    last_stride, last_size = groups[-1]
    active = gather_digit(active, last_stride, last_size)
    per = SEQ_SIZE // MP_SIZE
    pairs = []
    for s in range(SEQ_SIZE):
        lead = 0
        for stride, size in groups[:-1]:
            lead = lead * size + (s // stride) % size
        last = (s // last_stride) % last_size
        for m in range(MP_SIZE):
            pairs.append((s * MP_SIZE + m, (m * per + lead) * MP_SIZE + last))
    return lax.ppermute(active, ("seq", "mp"), pairs)


def merge_stack(stack):
    member_max = stack[..., HD]
    highest = jnp.max(member_max, axis=0)
    scale = jnp.exp(member_max - highest[None])
    totals = jnp.sum(stack[..., HD + 1] * scale, axis=0)
    running = jnp.sum(stack[..., :HD] * scale[..., None], axis=0)
    return jnp.concatenate([running, highest[..., None], totals[..., None]], axis=-1)


def feature_sums(squares):
    return jnp.sum(exchange(squares, "mp", MP_SIZE, 1, MP_SIZE), axis=0)


def inverse_rms(square_total):
    return lax.rsqrt(square_total / D + epsilon)[:, None]


def local(
    states,
    query_weight,
    key_weight,
    value_weight,
    output_weight,
    gate_weight,
    up_weight,
    down_weight,
    query_gain,
    key_gain,
    attention_gain,
    feedforward_gain,
    key_cache,
    value_cache,
    lengths,
    page_owner,
    page_index,
):
    local_width = query_weight.shape[1]
    local_heads = local_width // HD
    rows = STEPS * R
    score_scale = HD ** (-0.5)
    token_rows = states.reshape(rows, local_width)
    positions = (lengths[None, :] + jnp.arange(STEPS, dtype=jnp.int32)[:, None]).reshape(rows)

    sliced = seq_columns(token_rows, query_weight.shape[0])
    summed = seq_total(
        jnp.concatenate(
            [
                jnp.dot(sliced, query_weight, preferred_element_type=jnp.float32),
                jnp.dot(sliced, key_weight, preferred_element_type=jnp.float32),
                jnp.dot(sliced, value_weight, preferred_element_type=jnp.float32),
            ],
            axis=1,
        )
    )
    query_raw = summed[:, :local_width]
    key_raw = summed[:, local_width : 2 * local_width]
    value_raw = summed[:, 2 * local_width :]
    squares = feature_sums(
        jnp.stack([jnp.sum(query_raw * query_raw, axis=1), jnp.sum(key_raw * key_raw, axis=1)], axis=1)
    )
    queries = rotary(
        (query_raw * inverse_rms(squares[:, 0]) * query_gain).reshape(rows, local_heads, HD), positions
    ).astype(jnp.bfloat16)
    new_keys = rotary(
        (key_raw * inverse_rms(squares[:, 1]) * key_gain).reshape(rows, local_heads, HD), positions
    ).astype(jnp.bfloat16)
    new_values = value_raw.astype(jnp.bfloat16).reshape(rows, local_heads, HD)

    pages = key_cache.shape[0]
    tokens = pages * PAGE
    keys = key_cache.reshape(tokens, local_width)
    values = value_cache.reshape(tokens, local_width)
    token_owner = jnp.repeat(page_owner, PAGE)
    token_spot = (page_index[:, None] * PAGE + jnp.arange(PAGE, dtype=jnp.int32)[None, :]).reshape(tokens)
    validity = (token_owner[None, :] == jnp.arange(R, dtype=jnp.int32)[:, None]) & (
        token_spot[None, :] < lengths[:, None]
    )
    head_of_feature = jnp.arange(local_width, dtype=jnp.int32) // HD
    flat_queries = queries.reshape(rows, local_width)
    block_queries = jnp.where(
        head_of_feature[None, None, :] == jnp.arange(local_heads, dtype=jnp.int32)[:, None, None],
        flat_queries[None],
        jnp.zeros((), jnp.bfloat16),
    ).reshape(local_heads * rows, local_width)
    scores = lax.dot_general(
        block_queries, keys, (((1,), (1,)), ((), ())), preferred_element_type=jnp.float32
    ).reshape(local_heads, STEPS, R, tokens) * score_scale
    valid = validity[None, None]
    masked = jnp.where(valid, scores, very_low)
    maxima = jnp.max(masked, axis=3)
    weights = jnp.where(valid, jnp.exp(masked - maxima[..., None]), 0.0)
    totals = jnp.sum(weights, axis=3).reshape(local_heads, rows)
    maxima = maxima.reshape(local_heads, rows)
    all_heads = lax.dot_general(
        values,
        weights.astype(jnp.bfloat16).reshape(local_heads * rows, tokens),
        (((0,), (1,)), ((), ())),
        preferred_element_type=jnp.float32,
    ).reshape(local_heads, HD, local_heads, rows)
    running = jnp.stack([all_heads[h, :, h].T for h in range(local_heads)])

    seq = lax.axis_index("seq")
    slice_width = local_width // SEQ_SIZE
    per_head = HD // slice_width
    send = jnp.concatenate(
        [
            running.reshape(local_heads, rows, per_head, slice_width).transpose(0, 2, 1, 3),
            jnp.broadcast_to(maxima[:, None, :, None], (local_heads, per_head, rows, 1)),
            jnp.broadcast_to(totals[:, None, :, None], (local_heads, per_head, rows, 1)),
        ],
        axis=3,
    ).reshape(SEQ_SIZE, rows, slice_width + 2)
    sources = lax.all_to_all(send, "seq", 0, 0, tiled=True)
    source_max = sources[..., slice_width]
    cache_highest = jnp.max(source_max, axis=0)
    scale = jnp.exp(source_max - cache_highest[None])
    cache_totals = jnp.sum(sources[..., slice_width + 1] * scale, axis=0)
    cache_running = jnp.sum(sources[..., :slice_width] * scale[..., None], axis=0)

    head = seq // per_head
    offset = (seq % per_head) * slice_width
    q4 = lax.dynamic_index_in_dim(queries, head, 1, keepdims=False).reshape(STEPS, R, HD)
    k4 = lax.dynamic_index_in_dim(new_keys, head, 1, keepdims=False).reshape(STEPS, R, HD)
    v4 = lax.dynamic_slice_in_dim(
        lax.dynamic_index_in_dim(new_values, head, 1, keepdims=False), offset, slice_width, 1
    ).reshape(STEPS, R, slice_width)
    fresh_scores = jnp.einsum("srd,trd->srt", q4, k4, preferred_element_type=jnp.float32) * score_scale
    allowed = (jnp.arange(STEPS)[None, :] <= jnp.arange(STEPS)[:, None])[:, None, :]
    fresh_scores = jnp.where(allowed, fresh_scores, very_low)
    cache_highest = cache_highest.reshape(STEPS, R)
    highest = jnp.maximum(cache_highest, jnp.max(fresh_scores, axis=-1))
    fresh_weights = jnp.where(allowed, jnp.exp(fresh_scores - highest[..., None]), 0.0)
    factor = jnp.exp(cache_highest - highest)
    final_totals = cache_totals.reshape(STEPS, R) * factor + jnp.sum(fresh_weights, axis=-1)
    final_running = cache_running.reshape(STEPS, R, slice_width) * factor[..., None] + jnp.einsum(
        "srt,trd->srd", fresh_weights.astype(jnp.bfloat16), v4, preferred_element_type=jnp.float32
    )
    attended = (final_running / final_totals[..., None]).astype(jnp.bfloat16).reshape(rows, slice_width)

    width = output_weight.shape[0]
    per = local_width // width
    holders = width // slice_width
    sliced = jnp.zeros((rows, width), jnp.bfloat16)
    mp = lax.axis_index("mp")
    for shift in range(MP_SIZE):
        pairs = [
            (s * MP_SIZE + m, (m * per + s // holders) * MP_SIZE + (s % holders + shift) % MP_SIZE)
            for s in range(SEQ_SIZE)
            for m in range(MP_SIZE)
        ]
        received = lax.ppermute(attended, ("seq", "mp"), pairs)
        sliced = lax.dynamic_update_slice_in_dim(
            sliced, received, ((mp - shift) % MP_SIZE) * slice_width, 1
        )
    attention_out = seq_total(
        jnp.dot(sliced, output_weight, preferred_element_type=jnp.float32)
    )
    attention_squares = feature_sums(jnp.sum(attention_out * attention_out, axis=1))
    hidden = (
        token_rows.astype(jnp.float32) + attention_out * inverse_rms(attention_squares) * attention_gain
    ).astype(jnp.bfloat16)

    hidden_cols = seq_columns(hidden, gate_weight.shape[0])
    active_cols = gate_up_active(
        jnp.dot(hidden_cols, gate_weight, preferred_element_type=jnp.float32),
        jnp.dot(hidden_cols, up_weight, preferred_element_type=jnp.float32),
    )
    mlp_out = seq_total(
        jnp.dot(active_cols, down_weight, preferred_element_type=jnp.float32)
    )
    mlp_squares = feature_sums(jnp.sum(mlp_out * mlp_out, axis=1))
    decoded = (
        hidden.astype(jnp.float32) + mlp_out * inverse_rms(mlp_squares) * feedforward_gain
    ).astype(jnp.bfloat16)
    return decoded.reshape(STEPS, R, local_width)


def solution(mesh):
    global SEQ_SIZE, MP_SIZE, SEQ_FACTORS
    SEQ_SIZE = mesh.shape["seq"]
    MP_SIZE = mesh.shape["mp"]
    factors = []
    left = SEQ_SIZE // MP_SIZE
    if left % 2 == 0:
        factors.append(2)
        left //= 2
    while left % 4 == 0:
        factors.append(4)
        left //= 4
    if left > 1:
        factors.append(left)
    factors.append(MP_SIZE)
    SEQ_FACTORS = tuple(factors)
    in_specs = (
        P(None, None, "mp"),
        P("seq", "mp"),
        P("seq", "mp"),
        P("seq", "mp"),
        P("seq", "mp"),
        P("seq", "mp"),
        P("seq", "mp"),
        P("seq", "mp"),
        P("mp"),
        P("mp"),
        P("mp"),
        P("mp"),
        P("seq", None, "mp"),
        P("seq", None, "mp"),
        P(),
        P("seq"),
        P("seq"),
    )
    out_specs = P(None, None, "mp")
    return jax.shard_map(local, mesh=mesh, in_specs=in_specs, out_specs=out_specs, check_vma=False)
```

```python
import jax
import jax.numpy as jnp
from jax import lax
from jax.sharding import PartitionSpec as P

D = 2048
HD = 128
R = 16
STEPS = 4
PAGE = 256


epsilon = 1e-06
rope_base = 500000.0
very_low = -1e30
SEQ_SIZE = 32
MP_SIZE = 4
SEQ_FACTORS = (2, 4, 4)


def rotary(values, positions):
    half_width = HD // 2
    frequencies = rope_base ** (-2.0 * jnp.arange(half_width, dtype=jnp.float32) / HD)
    angles = positions.astype(jnp.float32)[:, None] * frequencies[None, :]
    cosine = jnp.cos(angles)[:, None, :]
    sine_part = jnp.sin(angles)[:, None, :]
    first_half = values[..., :half_width]
    second_half = values[..., half_width:]
    return jnp.concatenate(
        [
            first_half * cosine - second_half * sine_part,
            second_half * cosine + first_half * sine_part,
        ],
        axis=-1,
    )


def seq_columns(block, width):
    per = block.shape[1] // width
    seq = lax.axis_index("seq")
    piece = lax.dynamic_slice_in_dim(block, (seq % per) * width, width, 1)
    pairs = [
        (s * MP_SIZE + m, (m * per + s % per) * MP_SIZE + s // per)
        for s in range(SEQ_SIZE)
        for m in range(MP_SIZE)
    ]
    return lax.ppermute(piece, ("seq", "mp"), pairs)


def seq_groups():
    groups = []
    stride = 1
    for size in SEQ_FACTORS:
        groups.append((stride, size))
        stride *= size
    return groups


def digit_pairs(count, stride, size, shift):
    return [
        (i, i + (((i // stride) % size + shift) % size - (i // stride) % size) * stride)
        for i in range(count)
    ]


def exchange(value, axis, count, stride, size):
    digit = (lax.axis_index(axis) // stride) % size
    stack = jnp.zeros((size,) + value.shape, value.dtype)
    stack = lax.dynamic_update_index_in_dim(stack, value, digit, 0)
    for shift in range(1, size):
        received = lax.ppermute(value, axis, digit_pairs(count, stride, size, shift))
        stack = lax.dynamic_update_index_in_dim(stack, received, (digit - shift) % size, 0)
    return stack


def scatter_digit(current, stride, size):
    me = lax.axis_index("seq")
    digit = (me // stride) % size
    part = current.shape[1] // size
    total = lax.dynamic_slice_in_dim(current, digit * part, part, 1)
    for shift in range(1, size):
        send = lax.dynamic_slice_in_dim(current, ((digit + shift) % size) * part, part, 1)
        total = total + lax.ppermute(send, "seq", digit_pairs(SEQ_SIZE, stride, size, shift))
    return total


def gather_digit(current, stride, size):
    me = lax.axis_index("seq")
    digit = (me // stride) % size
    part = current.shape[1]
    whole = jnp.zeros((current.shape[0], part * size), current.dtype)
    whole = lax.dynamic_update_slice_in_dim(whole, current, digit * part, 1)
    for shift in range(1, size):
        received = lax.ppermute(current, "seq", digit_pairs(SEQ_SIZE, stride, size, shift))
        whole = lax.dynamic_update_slice_in_dim(whole, received, ((digit - shift) % size) * part, 1)
    return whole


def seq_total(partial_value, ladder=False, butterfly=False):
    groups = seq_groups()
    current = partial_value
    if ladder:
        for stride, size in groups:
            current = scatter_digit(current, stride, size)
        for stride, size in reversed(groups):
            current = gather_digit(current, stride, size)
        return current
    if butterfly:
        for stride, size in groups:
            current = jnp.sum(exchange(current, "seq", SEQ_SIZE, stride, size), axis=0)
        return current
    stride, size = groups[0]
    current = scatter_digit(current, stride, size)
    for other_stride, other_size in groups[1:]:
        current = jnp.sum(exchange(current, "seq", SEQ_SIZE, other_stride, other_size), axis=0)
    return gather_digit(current, stride, size)


def gate_up_active(gate_part, up_part):
    rows, units = gate_part.shape
    unit_block = units // SEQ_SIZE
    arranged = jnp.stack(
        [gate_part.reshape(rows, SEQ_SIZE, unit_block), up_part.reshape(rows, SEQ_SIZE, unit_block)],
        axis=2,
    ).reshape(rows, 2 * units)
    groups = seq_groups()
    for stride, size in groups:
        arranged = scatter_digit(arranged, stride, size)
    active = (jax.nn.silu(arranged[:, :unit_block]) * arranged[:, unit_block:]).astype(jnp.bfloat16)
    last_stride, last_size = groups[-1]
    active = gather_digit(active, last_stride, last_size)
    per = SEQ_SIZE // MP_SIZE
    pairs = []
    for s in range(SEQ_SIZE):
        lead = 0
        for stride, size in groups[:-1]:
            lead = lead * size + (s // stride) % size
        last = (s // last_stride) % last_size
        for m in range(MP_SIZE):
            pairs.append((s * MP_SIZE + m, (m * per + lead) * MP_SIZE + last))
    return lax.ppermute(active, ("seq", "mp"), pairs)


def deliver(piece, width, local_width):
    slice_width = piece.shape[1]
    per = local_width // width
    holders = width // slice_width
    assert holders == MP_SIZE
    mp = lax.axis_index("mp")
    result = jnp.zeros((piece.shape[0], width), piece.dtype)
    for shift in range(MP_SIZE):
        pairs = [
            (s * MP_SIZE + m, (m * per + s // holders) * MP_SIZE + (s % holders + shift) % MP_SIZE)
            for s in range(SEQ_SIZE)
            for m in range(MP_SIZE)
        ]
        received = lax.ppermute(piece, ("seq", "mp"), pairs)
        result = lax.dynamic_update_slice_in_dim(
            result, received, ((mp - shift) % MP_SIZE) * slice_width, 1
        )
    return result


def full_rows(weight):
    rows, cols = weight.shape
    block = cols // SEQ_SIZE
    moved = lax.all_to_all(weight.reshape(rows, SEQ_SIZE, block), "seq", 1, 0, tiled=True)
    return moved.reshape(rows * SEQ_SIZE, block)


def merge_stack(stack):
    member_max = stack[..., HD]
    highest = jnp.max(member_max, axis=0)
    scale = jnp.exp(member_max - highest[None])
    totals = jnp.sum(stack[..., HD + 1] * scale, axis=0)
    running = jnp.sum(stack[..., :HD] * scale[..., None], axis=0)
    return jnp.concatenate([running, highest[..., None], totals[..., None]], axis=-1)


def feature_sums(squares):
    return jnp.sum(exchange(squares, "mp", MP_SIZE, 1, MP_SIZE), axis=0)


def inverse_rms(square_total):
    return lax.rsqrt(square_total / D + epsilon)[:, None]


def local(
    states,
    query_weight,
    key_weight,
    value_weight,
    output_weight,
    gate_weight,
    up_weight,
    down_weight,
    query_gain,
    key_gain,
    attention_gain,
    feedforward_gain,
    key_cache,
    value_cache,
    lengths,
    page_owner,
    page_index,
):
    local_width = query_weight.shape[1]
    local_heads = local_width // HD
    rows = STEPS * R
    score_scale = HD ** (-0.5)
    token_rows = states.reshape(rows, local_width)
    positions = (lengths[None, :] + jnp.arange(STEPS, dtype=jnp.int32)[:, None]).reshape(rows)

    sliced = seq_columns(token_rows, query_weight.shape[0])
    summed = seq_total(
        jnp.concatenate(
            [
                jnp.dot(sliced, query_weight, preferred_element_type=jnp.float32),
                jnp.dot(sliced, key_weight, preferred_element_type=jnp.float32),
                jnp.dot(sliced, value_weight, preferred_element_type=jnp.float32),
            ],
            axis=1,
        )
    )
    query_raw = summed[:, :local_width]
    key_raw = summed[:, local_width : 2 * local_width]
    value_raw = summed[:, 2 * local_width :]
    squares = feature_sums(
        jnp.stack([jnp.sum(query_raw * query_raw, axis=1), jnp.sum(key_raw * key_raw, axis=1)], axis=1)
    )
    queries = rotary(
        (query_raw * inverse_rms(squares[:, 0]) * query_gain).reshape(rows, local_heads, HD), positions
    ).astype(jnp.bfloat16)
    new_keys = rotary(
        (key_raw * inverse_rms(squares[:, 1]) * key_gain).reshape(rows, local_heads, HD), positions
    ).astype(jnp.bfloat16)
    new_values = value_raw.astype(jnp.bfloat16).reshape(rows, local_heads, HD)

    pages = key_cache.shape[0]
    tokens = pages * PAGE
    keys = key_cache.reshape(tokens, local_width)
    values = value_cache.reshape(tokens, local_width)
    token_owner = jnp.repeat(page_owner, PAGE)
    token_spot = (page_index[:, None] * PAGE + jnp.arange(PAGE, dtype=jnp.int32)[None, :]).reshape(tokens)
    validity = (token_owner[None, :] == jnp.arange(R, dtype=jnp.int32)[:, None]) & (
        token_spot[None, :] < lengths[:, None]
    )
    head_of_feature = jnp.arange(local_width, dtype=jnp.int32) // HD
    flat_queries = queries.reshape(rows, local_width)
    block_queries = jnp.where(
        head_of_feature[None, None, :] == jnp.arange(local_heads, dtype=jnp.int32)[:, None, None],
        flat_queries[None],
        jnp.zeros((), jnp.bfloat16),
    ).reshape(local_heads * rows, local_width)
    scores = lax.dot_general(
        block_queries, keys, (((1,), (1,)), ((), ())), preferred_element_type=jnp.float32
    ).reshape(local_heads, STEPS, R, tokens) * score_scale
    valid = validity[None, None]
    masked = jnp.where(valid, scores, very_low)
    maxima = jnp.max(masked, axis=3)
    weights = jnp.where(valid, jnp.exp(masked - maxima[..., None]), 0.0)
    totals = jnp.sum(weights, axis=3).reshape(local_heads, rows)
    maxima = maxima.reshape(local_heads, rows)
    all_heads = lax.dot_general(
        values,
        weights.astype(jnp.bfloat16).reshape(local_heads * rows, tokens),
        (((0,), (1,)), ((), ())),
        preferred_element_type=jnp.float32,
    ).reshape(local_heads, HD, local_heads, rows)
    running = jnp.stack([all_heads[h, :, h].T for h in range(local_heads)])

    seq = lax.axis_index("seq")
    slice_width = local_width // SEQ_SIZE
    per_head = HD // slice_width
    send = jnp.concatenate(
        [
            running.reshape(local_heads, rows, per_head, slice_width).transpose(0, 2, 1, 3),
            jnp.broadcast_to(maxima[:, None, :, None], (local_heads, per_head, rows, 1)),
            jnp.broadcast_to(totals[:, None, :, None], (local_heads, per_head, rows, 1)),
        ],
        axis=3,
    ).reshape(SEQ_SIZE, rows, slice_width + 2)
    sources = lax.all_to_all(send, "seq", 0, 0, tiled=True)
    source_max = sources[..., slice_width]
    cache_highest = jnp.max(source_max, axis=0)
    scale = jnp.exp(source_max - cache_highest[None])
    cache_totals = jnp.sum(sources[..., slice_width + 1] * scale, axis=0)
    cache_running = jnp.sum(sources[..., :slice_width] * scale[..., None], axis=0)

    head = seq // per_head
    offset = (seq % per_head) * slice_width
    q4 = lax.dynamic_index_in_dim(queries, head, 1, keepdims=False).reshape(STEPS, R, HD)
    k4 = lax.dynamic_index_in_dim(new_keys, head, 1, keepdims=False).reshape(STEPS, R, HD)
    v4 = lax.dynamic_slice_in_dim(
        lax.dynamic_index_in_dim(new_values, head, 1, keepdims=False), offset, slice_width, 1
    ).reshape(STEPS, R, slice_width)
    fresh_scores = jnp.einsum("srd,trd->srt", q4, k4, preferred_element_type=jnp.float32) * score_scale
    allowed = (jnp.arange(STEPS)[None, :] <= jnp.arange(STEPS)[:, None])[:, None, :]
    fresh_scores = jnp.where(allowed, fresh_scores, very_low)
    cache_highest = cache_highest.reshape(STEPS, R)
    highest = jnp.maximum(cache_highest, jnp.max(fresh_scores, axis=-1))
    fresh_weights = jnp.where(allowed, jnp.exp(fresh_scores - highest[..., None]), 0.0)
    factor = jnp.exp(cache_highest - highest)
    final_totals = cache_totals.reshape(STEPS, R) * factor + jnp.sum(fresh_weights, axis=-1)
    final_running = cache_running.reshape(STEPS, R, slice_width) * factor[..., None] + jnp.einsum(
        "srt,trd->srd", fresh_weights.astype(jnp.bfloat16), v4, preferred_element_type=jnp.float32
    )
    attended = (final_running / final_totals[..., None]).astype(jnp.bfloat16).reshape(rows, slice_width)

    sliced = deliver(attended, output_weight.shape[0], local_width)
    attention_out = seq_total(
        jnp.dot(sliced, output_weight, preferred_element_type=jnp.float32)
    )
    attention_squares = feature_sums(jnp.sum(attention_out * attention_out, axis=1))
    hidden = (
        token_rows.astype(jnp.float32) + attention_out * inverse_rms(attention_squares) * attention_gain
    ).astype(jnp.bfloat16)

    hidden_all = lax.all_gather(hidden, "mp", axis=1, tiled=True)
    gate = jnp.dot(hidden_all, full_rows(gate_weight), preferred_element_type=jnp.float32)
    up_part = jnp.dot(hidden_all, full_rows(up_weight), preferred_element_type=jnp.float32)
    active = (jax.nn.silu(gate) * up_part).astype(jnp.bfloat16)
    active_cols = deliver(active, down_weight.shape[0], gate_weight.shape[1])
    mlp_out = seq_total(
        jnp.dot(active_cols, down_weight, preferred_element_type=jnp.float32)
    )
    mlp_squares = feature_sums(jnp.sum(mlp_out * mlp_out, axis=1))
    decoded = (
        hidden.astype(jnp.float32) + mlp_out * inverse_rms(mlp_squares) * feedforward_gain
    ).astype(jnp.bfloat16)
    return decoded.reshape(STEPS, R, local_width)


def solution(mesh):
    global SEQ_SIZE, MP_SIZE, SEQ_FACTORS
    SEQ_SIZE = mesh.shape["seq"]
    MP_SIZE = mesh.shape["mp"]
    factors = []
    left = SEQ_SIZE // MP_SIZE
    if left % 2 == 0:
        factors.append(2)
        left //= 2
    while left % 4 == 0:
        factors.append(4)
        left //= 4
    if left > 1:
        factors.append(left)
    factors.append(MP_SIZE)
    SEQ_FACTORS = tuple(factors)
    in_specs = (
        P(None, None, "mp"),
        P("seq", "mp"),
        P("seq", "mp"),
        P("seq", "mp"),
        P("seq", "mp"),
        P("seq", "mp"),
        P("seq", "mp"),
        P("seq", "mp"),
        P("mp"),
        P("mp"),
        P("mp"),
        P("mp"),
        P("seq", None, "mp"),
        P("seq", None, "mp"),
        P(),
        P("seq"),
        P("seq"),
    )
    out_specs = P(None, None, "mp")
    return jax.shard_map(local, mesh=mesh, in_specs=in_specs, out_specs=out_specs, check_vma=False)
```

```python
import jax
import jax.numpy as jnp
from jax import lax
from jax.sharding import PartitionSpec as P

D = 2048
HD = 128
R = 16
STEPS = 4
PAGE = 256


epsilon = 1e-06
rope_base = 500000.0
very_low = -1e30
SEQ_SIZE = 32
MP_SIZE = 4
SEQ_FACTORS = (2, 4, 4)


def rotary(values, positions):
    half_width = HD // 2
    frequencies = rope_base ** (-2.0 * jnp.arange(half_width, dtype=jnp.float32) / HD)
    angles = positions.astype(jnp.float32)[:, None] * frequencies[None, :]
    cosine = jnp.cos(angles)[:, None, :]
    sine_part = jnp.sin(angles)[:, None, :]
    first_half = values[..., :half_width]
    second_half = values[..., half_width:]
    return jnp.concatenate(
        [
            first_half * cosine - second_half * sine_part,
            second_half * cosine + first_half * sine_part,
        ],
        axis=-1,
    )


def seq_columns(block, width):
    per = block.shape[1] // width
    seq = lax.axis_index("seq")
    piece = lax.dynamic_slice_in_dim(block, (seq % per) * width, width, 1)
    pairs = [
        (s * MP_SIZE + m, (m * per + s % per) * MP_SIZE + s // per)
        for s in range(SEQ_SIZE)
        for m in range(MP_SIZE)
    ]
    return lax.ppermute(piece, ("seq", "mp"), pairs)


def seq_groups():
    groups = []
    stride = 1
    for size in SEQ_FACTORS:
        groups.append((stride, size))
        stride *= size
    return groups


def digit_pairs(count, stride, size, shift):
    return [
        (i, i + (((i // stride) % size + shift) % size - (i // stride) % size) * stride)
        for i in range(count)
    ]


def exchange(value, axis, count, stride, size):
    digit = (lax.axis_index(axis) // stride) % size
    stack = jnp.zeros((size,) + value.shape, value.dtype)
    stack = lax.dynamic_update_index_in_dim(stack, value, digit, 0)
    for shift in range(1, size):
        received = lax.ppermute(value, axis, digit_pairs(count, stride, size, shift))
        stack = lax.dynamic_update_index_in_dim(stack, received, (digit - shift) % size, 0)
    return stack


def scatter_digit(current, stride, size):
    me = lax.axis_index("seq")
    digit = (me // stride) % size
    part = current.shape[1] // size
    total = lax.dynamic_slice_in_dim(current, digit * part, part, 1)
    for shift in range(1, size):
        send = lax.dynamic_slice_in_dim(current, ((digit + shift) % size) * part, part, 1)
        total = total + lax.ppermute(send, "seq", digit_pairs(SEQ_SIZE, stride, size, shift))
    return total


def gather_digit(current, stride, size):
    me = lax.axis_index("seq")
    digit = (me // stride) % size
    part = current.shape[1]
    whole = jnp.zeros((current.shape[0], part * size), current.dtype)
    whole = lax.dynamic_update_slice_in_dim(whole, current, digit * part, 1)
    for shift in range(1, size):
        received = lax.ppermute(current, "seq", digit_pairs(SEQ_SIZE, stride, size, shift))
        whole = lax.dynamic_update_slice_in_dim(whole, received, ((digit - shift) % size) * part, 1)
    return whole


def seq_total(partial_value, ladder=False, butterfly=False):
    groups = seq_groups()
    current = partial_value
    if ladder:
        for stride, size in groups:
            current = scatter_digit(current, stride, size)
        for stride, size in reversed(groups):
            current = gather_digit(current, stride, size)
        return current
    if butterfly:
        for stride, size in groups:
            current = jnp.sum(exchange(current, "seq", SEQ_SIZE, stride, size), axis=0)
        return current
    stride, size = groups[0]
    current = scatter_digit(current, stride, size)
    for other_stride, other_size in groups[1:]:
        current = jnp.sum(exchange(current, "seq", SEQ_SIZE, other_stride, other_size), axis=0)
    return gather_digit(current, stride, size)


def gate_up_active(gate_part, up_part):
    rows, units = gate_part.shape
    unit_block = units // SEQ_SIZE
    arranged = jnp.stack(
        [gate_part.reshape(rows, SEQ_SIZE, unit_block), up_part.reshape(rows, SEQ_SIZE, unit_block)],
        axis=2,
    ).reshape(rows, 2 * units)
    groups = seq_groups()
    for stride, size in groups:
        arranged = scatter_digit(arranged, stride, size)
    active = (jax.nn.silu(arranged[:, :unit_block]) * arranged[:, unit_block:]).astype(jnp.bfloat16)
    last_stride, last_size = groups[-1]
    active = gather_digit(active, last_stride, last_size)
    per = SEQ_SIZE // MP_SIZE
    pairs = []
    for s in range(SEQ_SIZE):
        lead = 0
        for stride, size in groups[:-1]:
            lead = lead * size + (s // stride) % size
        last = (s // last_stride) % last_size
        for m in range(MP_SIZE):
            pairs.append((s * MP_SIZE + m, (m * per + lead) * MP_SIZE + last))
    return lax.ppermute(active, ("seq", "mp"), pairs)


def deliver(piece, width, local_width):
    slice_width = piece.shape[1]
    per = local_width // width
    holders = width // slice_width
    assert holders == MP_SIZE
    mp = lax.axis_index("mp")
    result = jnp.zeros((piece.shape[0], width), piece.dtype)
    for shift in range(MP_SIZE):
        pairs = [
            (s * MP_SIZE + m, (m * per + s // holders) * MP_SIZE + (s % holders + shift) % MP_SIZE)
            for s in range(SEQ_SIZE)
            for m in range(MP_SIZE)
        ]
        received = lax.ppermute(piece, ("seq", "mp"), pairs)
        result = lax.dynamic_update_slice_in_dim(
            result, received, ((mp - shift) % MP_SIZE) * slice_width, 1
        )
    return result


def full_rows(weight):
    rows, cols = weight.shape
    block = cols // SEQ_SIZE
    moved = lax.all_to_all(weight.reshape(rows, SEQ_SIZE, block), "seq", 1, 0, tiled=True)
    return moved.reshape(rows * SEQ_SIZE, block)


def merge_stack(stack):
    member_max = stack[..., HD]
    highest = jnp.max(member_max, axis=0)
    scale = jnp.exp(member_max - highest[None])
    totals = jnp.sum(stack[..., HD + 1] * scale, axis=0)
    running = jnp.sum(stack[..., :HD] * scale[..., None], axis=0)
    return jnp.concatenate([running, highest[..., None], totals[..., None]], axis=-1)


def feature_sums(squares):
    return jnp.sum(exchange(squares, "mp", MP_SIZE, 1, MP_SIZE), axis=0)


def inverse_rms(square_total):
    return lax.rsqrt(square_total / D + epsilon)[:, None]


def local(
    states,
    query_weight,
    key_weight,
    value_weight,
    output_weight,
    gate_weight,
    up_weight,
    down_weight,
    query_gain,
    key_gain,
    attention_gain,
    feedforward_gain,
    key_cache,
    value_cache,
    lengths,
    page_owner,
    page_index,
):
    local_width = query_weight.shape[1]
    local_heads = local_width // HD
    rows = STEPS * R
    score_scale = HD ** (-0.5)
    token_rows = states.reshape(rows, local_width)
    positions = (lengths[None, :] + jnp.arange(STEPS, dtype=jnp.int32)[:, None]).reshape(rows)

    sliced = seq_columns(token_rows, query_weight.shape[0])
    summed = seq_total(
        jnp.concatenate(
            [
                jnp.dot(sliced, query_weight, preferred_element_type=jnp.float32),
                jnp.dot(sliced, key_weight, preferred_element_type=jnp.float32),
                jnp.dot(sliced, value_weight, preferred_element_type=jnp.float32),
            ],
            axis=1,
        )
    )
    query_raw = summed[:, :local_width]
    key_raw = summed[:, local_width : 2 * local_width]
    value_raw = summed[:, 2 * local_width :]
    squares = feature_sums(
        jnp.stack([jnp.sum(query_raw * query_raw, axis=1), jnp.sum(key_raw * key_raw, axis=1)], axis=1)
    )
    queries = rotary(
        (query_raw * inverse_rms(squares[:, 0]) * query_gain).reshape(rows, local_heads, HD), positions
    ).astype(jnp.bfloat16)
    new_keys = rotary(
        (key_raw * inverse_rms(squares[:, 1]) * key_gain).reshape(rows, local_heads, HD), positions
    ).astype(jnp.bfloat16)
    new_values = value_raw.astype(jnp.bfloat16).reshape(rows, local_heads, HD)

    pages = key_cache.shape[0]
    tokens = pages * PAGE
    keys = key_cache.reshape(tokens, local_width)
    values = value_cache.reshape(tokens, local_width)
    token_owner = jnp.repeat(page_owner, PAGE)
    token_spot = (page_index[:, None] * PAGE + jnp.arange(PAGE, dtype=jnp.int32)[None, :]).reshape(tokens)
    validity = (token_owner[None, :] == jnp.arange(R, dtype=jnp.int32)[:, None]) & (
        token_spot[None, :] < lengths[:, None]
    )
    head_of_feature = jnp.arange(local_width, dtype=jnp.int32) // HD
    flat_queries = queries.reshape(rows, local_width)
    block_queries = jnp.where(
        head_of_feature[None, None, :] == jnp.arange(local_heads, dtype=jnp.int32)[:, None, None],
        flat_queries[None],
        jnp.zeros((), jnp.bfloat16),
    ).reshape(local_heads * rows, local_width)
    scores = lax.dot_general(
        block_queries, keys, (((1,), (1,)), ((), ())), preferred_element_type=jnp.float32
    ).reshape(local_heads, STEPS, R, tokens) * score_scale
    valid = validity[None, None]
    masked = jnp.where(valid, scores, very_low)
    maxima = jnp.max(masked, axis=3)
    weights = jnp.where(valid, jnp.exp(masked - maxima[..., None]), 0.0)
    totals = jnp.sum(weights, axis=3).reshape(local_heads, rows)
    maxima = maxima.reshape(local_heads, rows)
    all_heads = lax.dot_general(
        values,
        weights.astype(jnp.bfloat16).reshape(local_heads * rows, tokens),
        (((0,), (1,)), ((), ())),
        preferred_element_type=jnp.float32,
    ).reshape(local_heads, HD, local_heads, rows)
    running = jnp.stack([all_heads[h, :, h].T for h in range(local_heads)])

    seq = lax.axis_index("seq")
    slice_width = local_width // SEQ_SIZE
    per_head = HD // slice_width
    send = jnp.concatenate(
        [
            running.reshape(local_heads, rows, per_head, slice_width).transpose(0, 2, 1, 3),
            jnp.broadcast_to(maxima[:, None, :, None], (local_heads, per_head, rows, 1)),
            jnp.broadcast_to(totals[:, None, :, None], (local_heads, per_head, rows, 1)),
        ],
        axis=3,
    ).reshape(SEQ_SIZE, rows, slice_width + 2)
    sources = lax.all_to_all(send, "seq", 0, 0, tiled=True)
    source_max = sources[..., slice_width]
    cache_highest = jnp.max(source_max, axis=0)
    scale = jnp.exp(source_max - cache_highest[None])
    cache_totals = jnp.sum(sources[..., slice_width + 1] * scale, axis=0)
    cache_running = jnp.sum(sources[..., :slice_width] * scale[..., None], axis=0)

    head = seq // per_head
    offset = (seq % per_head) * slice_width
    q4 = lax.dynamic_index_in_dim(queries, head, 1, keepdims=False).reshape(STEPS, R, HD)
    k4 = lax.dynamic_index_in_dim(new_keys, head, 1, keepdims=False).reshape(STEPS, R, HD)
    v4 = lax.dynamic_slice_in_dim(
        lax.dynamic_index_in_dim(new_values, head, 1, keepdims=False), offset, slice_width, 1
    ).reshape(STEPS, R, slice_width)
    fresh_scores = jnp.einsum("srd,trd->srt", q4, k4, preferred_element_type=jnp.float32) * score_scale
    allowed = (jnp.arange(STEPS)[None, :] <= jnp.arange(STEPS)[:, None])[:, None, :]
    fresh_scores = jnp.where(allowed, fresh_scores, very_low)
    cache_highest = cache_highest.reshape(STEPS, R)
    highest = jnp.maximum(cache_highest, jnp.max(fresh_scores, axis=-1))
    fresh_weights = jnp.where(allowed, jnp.exp(fresh_scores - highest[..., None]), 0.0)
    factor = jnp.exp(cache_highest - highest)
    final_totals = cache_totals.reshape(STEPS, R) * factor + jnp.sum(fresh_weights, axis=-1)
    final_running = cache_running.reshape(STEPS, R, slice_width) * factor[..., None] + jnp.einsum(
        "srt,trd->srd", fresh_weights.astype(jnp.bfloat16), v4, preferred_element_type=jnp.float32
    )
    attended = (final_running / final_totals[..., None]).astype(jnp.bfloat16).reshape(rows, slice_width)

    sliced = deliver(attended, output_weight.shape[0], local_width)
    attention_out = seq_total(
        jnp.dot(sliced, output_weight, preferred_element_type=jnp.float32)
    )
    attention_squares = feature_sums(jnp.sum(attention_out * attention_out, axis=1))
    hidden = (
        token_rows.astype(jnp.float32) + attention_out * inverse_rms(attention_squares) * attention_gain
    ).astype(jnp.bfloat16)

    hidden_all = jnp.transpose(exchange(hidden, "mp", MP_SIZE, 1, MP_SIZE), (1, 0, 2)).reshape(
        rows, MP_SIZE * local_width
    )
    units = gate_weight.shape[1] // SEQ_SIZE
    both = full_rows(
        jnp.concatenate(
            [
                gate_weight.reshape(-1, SEQ_SIZE, units),
                up_weight.reshape(-1, SEQ_SIZE, units),
            ],
            axis=2,
        ).reshape(gate_weight.shape[0], 2 * gate_weight.shape[1])
    )
    gate = jnp.dot(hidden_all, both[:, :units], preferred_element_type=jnp.float32)
    up_part = jnp.dot(hidden_all, both[:, units:], preferred_element_type=jnp.float32)
    active = (jax.nn.silu(gate) * up_part).astype(jnp.bfloat16)
    active_cols = deliver(active, down_weight.shape[0], gate_weight.shape[1])
    mlp_out = seq_total(
        jnp.dot(active_cols, down_weight, preferred_element_type=jnp.float32)
    )
    mlp_squares = feature_sums(jnp.sum(mlp_out * mlp_out, axis=1))
    decoded = (
        hidden.astype(jnp.float32) + mlp_out * inverse_rms(mlp_squares) * feedforward_gain
    ).astype(jnp.bfloat16)
    return decoded.reshape(STEPS, R, local_width)


def solution(mesh):
    global SEQ_SIZE, MP_SIZE, SEQ_FACTORS
    SEQ_SIZE = mesh.shape["seq"]
    MP_SIZE = mesh.shape["mp"]
    factors = []
    left = SEQ_SIZE // MP_SIZE
    if left % 2 == 0:
        factors.append(2)
        left //= 2
    while left % 4 == 0:
        factors.append(4)
        left //= 4
    if left > 1:
        factors.append(left)
    factors.append(MP_SIZE)
    SEQ_FACTORS = tuple(factors)
    in_specs = (
        P(None, None, "mp"),
        P("seq", "mp"),
        P("seq", "mp"),
        P("seq", "mp"),
        P("seq", "mp"),
        P("seq", "mp"),
        P("seq", "mp"),
        P("seq", "mp"),
        P("mp"),
        P("mp"),
        P("mp"),
        P("mp"),
        P("seq", None, "mp"),
        P("seq", None, "mp"),
        P(),
        P("seq"),
        P("seq"),
    )
    out_specs = P(None, None, "mp")
    return jax.shard_map(local, mesh=mesh, in_specs=in_specs, out_specs=out_specs, check_vma=False)
```

```python
import jax
import jax.numpy as jnp
from jax import lax
from jax.sharding import PartitionSpec as P

D = 2048
HD = 128
R = 16
STEPS = 4
PAGE = 256


epsilon = 1e-06
rope_base = 500000.0
very_low = -1e30
SEQ_SIZE = 32
MP_SIZE = 4
SEQ_FACTORS = (2, 4, 4)


def rotary(values, positions):
    half_width = HD // 2
    frequencies = rope_base ** (-2.0 * jnp.arange(half_width, dtype=jnp.float32) / HD)
    angles = positions.astype(jnp.float32)[:, None] * frequencies[None, :]
    cosine = jnp.cos(angles)[:, None, :]
    sine_part = jnp.sin(angles)[:, None, :]
    first_half = values[..., :half_width]
    second_half = values[..., half_width:]
    return jnp.concatenate(
        [
            first_half * cosine - second_half * sine_part,
            second_half * cosine + first_half * sine_part,
        ],
        axis=-1,
    )


def seq_columns(block, width):
    per = block.shape[1] // width
    seq = lax.axis_index("seq")
    piece = lax.dynamic_slice_in_dim(block, (seq % per) * width, width, 1)
    pairs = [
        (s * MP_SIZE + m, (m * per + s % per) * MP_SIZE + s // per)
        for s in range(SEQ_SIZE)
        for m in range(MP_SIZE)
    ]
    return lax.ppermute(piece, ("seq", "mp"), pairs)


def seq_groups():
    groups = []
    stride = 1
    for size in SEQ_FACTORS:
        groups.append((stride, size))
        stride *= size
    return groups


def digit_pairs(count, stride, size, shift):
    return [
        (i, i + (((i // stride) % size + shift) % size - (i // stride) % size) * stride)
        for i in range(count)
    ]


def exchange(value, axis, count, stride, size):
    digit = (lax.axis_index(axis) // stride) % size
    stack = jnp.zeros((size,) + value.shape, value.dtype)
    stack = lax.dynamic_update_index_in_dim(stack, value, digit, 0)
    for shift in range(1, size):
        received = lax.ppermute(value, axis, digit_pairs(count, stride, size, shift))
        stack = lax.dynamic_update_index_in_dim(stack, received, (digit - shift) % size, 0)
    return stack


def scatter_digit(current, stride, size):
    me = lax.axis_index("seq")
    digit = (me // stride) % size
    part = current.shape[1] // size
    total = lax.dynamic_slice_in_dim(current, digit * part, part, 1)
    for shift in range(1, size):
        send = lax.dynamic_slice_in_dim(current, ((digit + shift) % size) * part, part, 1)
        total = total + lax.ppermute(send, "seq", digit_pairs(SEQ_SIZE, stride, size, shift))
    return total


def gather_digit(current, stride, size):
    me = lax.axis_index("seq")
    digit = (me // stride) % size
    part = current.shape[1]
    whole = jnp.zeros((current.shape[0], part * size), current.dtype)
    whole = lax.dynamic_update_slice_in_dim(whole, current, digit * part, 1)
    for shift in range(1, size):
        received = lax.ppermute(current, "seq", digit_pairs(SEQ_SIZE, stride, size, shift))
        whole = lax.dynamic_update_slice_in_dim(whole, received, ((digit - shift) % size) * part, 1)
    return whole


def seq_total(partial_value, ladder=False, butterfly=False):
    groups = seq_groups()
    current = partial_value
    if ladder:
        for stride, size in groups:
            current = scatter_digit(current, stride, size)
        for stride, size in reversed(groups):
            current = gather_digit(current, stride, size)
        return current
    if butterfly:
        for stride, size in groups:
            current = jnp.sum(exchange(current, "seq", SEQ_SIZE, stride, size), axis=0)
        return current
    stride, size = groups[0]
    current = scatter_digit(current, stride, size)
    for other_stride, other_size in groups[1:]:
        current = jnp.sum(exchange(current, "seq", SEQ_SIZE, other_stride, other_size), axis=0)
    return gather_digit(current, stride, size)


def gate_up_active(gate_part, up_part):
    rows, units = gate_part.shape
    unit_block = units // SEQ_SIZE
    arranged = jnp.stack(
        [gate_part.reshape(rows, SEQ_SIZE, unit_block), up_part.reshape(rows, SEQ_SIZE, unit_block)],
        axis=2,
    ).reshape(rows, 2 * units)
    groups = seq_groups()
    for stride, size in groups:
        arranged = scatter_digit(arranged, stride, size)
    active = (jax.nn.silu(arranged[:, :unit_block]) * arranged[:, unit_block:]).astype(jnp.bfloat16)
    last_stride, last_size = groups[-1]
    active = gather_digit(active, last_stride, last_size)
    per = SEQ_SIZE // MP_SIZE
    pairs = []
    for s in range(SEQ_SIZE):
        lead = 0
        for stride, size in groups[:-1]:
            lead = lead * size + (s // stride) % size
        last = (s // last_stride) % last_size
        for m in range(MP_SIZE):
            pairs.append((s * MP_SIZE + m, (m * per + lead) * MP_SIZE + last))
    return lax.ppermute(active, ("seq", "mp"), pairs)


def deliver(piece, width, local_width):
    slice_width = piece.shape[1]
    per = local_width // width
    holders = width // slice_width
    assert holders == MP_SIZE
    mp = lax.axis_index("mp")
    result = jnp.zeros((piece.shape[0], width), piece.dtype)
    for shift in range(MP_SIZE):
        pairs = [
            (s * MP_SIZE + m, (m * per + s // holders) * MP_SIZE + (s % holders + shift) % MP_SIZE)
            for s in range(SEQ_SIZE)
            for m in range(MP_SIZE)
        ]
        received = lax.ppermute(piece, ("seq", "mp"), pairs)
        result = lax.dynamic_update_slice_in_dim(
            result, received, ((mp - shift) % MP_SIZE) * slice_width, 1
        )
    return result


def full_rows(weight):
    rows, cols = weight.shape
    block = cols // SEQ_SIZE
    moved = lax.all_to_all(weight.reshape(rows, SEQ_SIZE, block), "seq", 1, 0, tiled=True)
    return moved.reshape(rows * SEQ_SIZE, block)


def merge_stack(stack):
    member_max = stack[..., HD]
    highest = jnp.max(member_max, axis=0)
    scale = jnp.exp(member_max - highest[None])
    totals = jnp.sum(stack[..., HD + 1] * scale, axis=0)
    running = jnp.sum(stack[..., :HD] * scale[..., None], axis=0)
    return jnp.concatenate([running, highest[..., None], totals[..., None]], axis=-1)


def feature_sums(squares):
    return jnp.sum(exchange(squares, "mp", MP_SIZE, 1, MP_SIZE), axis=0)


def inverse_rms(square_total):
    return lax.rsqrt(square_total / D + epsilon)[:, None]


def local(
    states,
    query_weight,
    key_weight,
    value_weight,
    output_weight,
    gate_weight,
    up_weight,
    down_weight,
    query_gain,
    key_gain,
    attention_gain,
    feedforward_gain,
    key_cache,
    value_cache,
    lengths,
    page_owner,
    page_index,
):
    local_width = query_weight.shape[1]
    local_heads = local_width // HD
    rows = STEPS * R
    score_scale = HD ** (-0.5)
    token_rows = states.reshape(rows, local_width)
    positions = (lengths[None, :] + jnp.arange(STEPS, dtype=jnp.int32)[:, None]).reshape(rows)

    block = local_width // SEQ_SIZE
    qkv_weight = full_rows(
        jnp.concatenate(
            [w.reshape(-1, SEQ_SIZE, block) for w in (query_weight, key_weight, value_weight)], axis=2
        ).reshape(query_weight.shape[0], 3 * local_width)
    )
    states_all = jnp.transpose(exchange(token_rows, "mp", MP_SIZE, 1, MP_SIZE), (1, 0, 2)).reshape(
        rows, MP_SIZE * local_width
    )
    own = jnp.dot(states_all, qkv_weight, preferred_element_type=jnp.float32)
    for stride, size in seq_groups():
        own = gather_digit(own, stride, size)
    gathered = own.reshape(rows, SEQ_SIZE, 3, block)
    query_raw = gathered[:, :, 0].reshape(rows, local_width)
    key_raw = gathered[:, :, 1].reshape(rows, local_width)
    value_raw = gathered[:, :, 2].reshape(rows, local_width)
    squares = feature_sums(
        jnp.stack([jnp.sum(query_raw * query_raw, axis=1), jnp.sum(key_raw * key_raw, axis=1)], axis=1)
    )
    queries = rotary(
        (query_raw * inverse_rms(squares[:, 0]) * query_gain).reshape(rows, local_heads, HD), positions
    ).astype(jnp.bfloat16)
    new_keys = rotary(
        (key_raw * inverse_rms(squares[:, 1]) * key_gain).reshape(rows, local_heads, HD), positions
    ).astype(jnp.bfloat16)
    new_values = value_raw.astype(jnp.bfloat16).reshape(rows, local_heads, HD)

    pages = key_cache.shape[0]
    tokens = pages * PAGE
    keys = key_cache.reshape(tokens, local_width)
    values = value_cache.reshape(tokens, local_width)
    token_owner = jnp.repeat(page_owner, PAGE)
    token_spot = (page_index[:, None] * PAGE + jnp.arange(PAGE, dtype=jnp.int32)[None, :]).reshape(tokens)
    validity = (token_owner[None, :] == jnp.arange(R, dtype=jnp.int32)[:, None]) & (
        token_spot[None, :] < lengths[:, None]
    )
    head_of_feature = jnp.arange(local_width, dtype=jnp.int32) // HD
    flat_queries = queries.reshape(rows, local_width)
    block_queries = jnp.where(
        head_of_feature[None, None, :] == jnp.arange(local_heads, dtype=jnp.int32)[:, None, None],
        flat_queries[None],
        jnp.zeros((), jnp.bfloat16),
    ).reshape(local_heads * rows, local_width)
    scores = lax.dot_general(
        block_queries, keys, (((1,), (1,)), ((), ())), preferred_element_type=jnp.float32
    ).reshape(local_heads, STEPS, R, tokens) * score_scale
    valid = validity[None, None]
    masked = jnp.where(valid, scores, very_low)
    maxima = jnp.max(masked, axis=3)
    weights = jnp.where(valid, jnp.exp(masked - maxima[..., None]), 0.0)
    totals = jnp.sum(weights, axis=3).reshape(local_heads, rows)
    maxima = maxima.reshape(local_heads, rows)
    all_heads = lax.dot_general(
        values,
        weights.astype(jnp.bfloat16).reshape(local_heads * rows, tokens),
        (((0,), (1,)), ((), ())),
        preferred_element_type=jnp.float32,
    ).reshape(local_heads, HD, local_heads, rows)
    running = jnp.stack([all_heads[h, :, h].T for h in range(local_heads)])

    seq = lax.axis_index("seq")
    slice_width = local_width // SEQ_SIZE
    per_head = HD // slice_width
    send = jnp.concatenate(
        [
            running.reshape(local_heads, rows, per_head, slice_width).transpose(0, 2, 1, 3),
            jnp.broadcast_to(maxima[:, None, :, None], (local_heads, per_head, rows, 1)),
            jnp.broadcast_to(totals[:, None, :, None], (local_heads, per_head, rows, 1)),
        ],
        axis=3,
    ).reshape(SEQ_SIZE, rows, slice_width + 2)
    sources = lax.all_to_all(send, "seq", 0, 0, tiled=True)
    source_max = sources[..., slice_width]
    cache_highest = jnp.max(source_max, axis=0)
    scale = jnp.exp(source_max - cache_highest[None])
    cache_totals = jnp.sum(sources[..., slice_width + 1] * scale, axis=0)
    cache_running = jnp.sum(sources[..., :slice_width] * scale[..., None], axis=0)

    head = seq // per_head
    offset = (seq % per_head) * slice_width
    q4 = lax.dynamic_index_in_dim(queries, head, 1, keepdims=False).reshape(STEPS, R, HD)
    k4 = lax.dynamic_index_in_dim(new_keys, head, 1, keepdims=False).reshape(STEPS, R, HD)
    v4 = lax.dynamic_slice_in_dim(
        lax.dynamic_index_in_dim(new_values, head, 1, keepdims=False), offset, slice_width, 1
    ).reshape(STEPS, R, slice_width)
    fresh_scores = jnp.einsum("srd,trd->srt", q4, k4, preferred_element_type=jnp.float32) * score_scale
    allowed = (jnp.arange(STEPS)[None, :] <= jnp.arange(STEPS)[:, None])[:, None, :]
    fresh_scores = jnp.where(allowed, fresh_scores, very_low)
    cache_highest = cache_highest.reshape(STEPS, R)
    highest = jnp.maximum(cache_highest, jnp.max(fresh_scores, axis=-1))
    fresh_weights = jnp.where(allowed, jnp.exp(fresh_scores - highest[..., None]), 0.0)
    factor = jnp.exp(cache_highest - highest)
    final_totals = cache_totals.reshape(STEPS, R) * factor + jnp.sum(fresh_weights, axis=-1)
    final_running = cache_running.reshape(STEPS, R, slice_width) * factor[..., None] + jnp.einsum(
        "srt,trd->srd", fresh_weights.astype(jnp.bfloat16), v4, preferred_element_type=jnp.float32
    )
    attended = (final_running / final_totals[..., None]).astype(jnp.bfloat16).reshape(rows, slice_width)

    sliced = deliver(attended, output_weight.shape[0], local_width)
    attention_out = seq_total(
        jnp.dot(sliced, output_weight, preferred_element_type=jnp.float32)
    )
    attention_squares = feature_sums(jnp.sum(attention_out * attention_out, axis=1))
    hidden = (
        token_rows.astype(jnp.float32) + attention_out * inverse_rms(attention_squares) * attention_gain
    ).astype(jnp.bfloat16)

    hidden_all = jnp.transpose(exchange(hidden, "mp", MP_SIZE, 1, MP_SIZE), (1, 0, 2)).reshape(
        rows, MP_SIZE * local_width
    )
    units = gate_weight.shape[1] // SEQ_SIZE
    both = full_rows(
        jnp.concatenate(
            [
                gate_weight.reshape(-1, SEQ_SIZE, units),
                up_weight.reshape(-1, SEQ_SIZE, units),
            ],
            axis=2,
        ).reshape(gate_weight.shape[0], 2 * gate_weight.shape[1])
    )
    gate = jnp.dot(hidden_all, both[:, :units], preferred_element_type=jnp.float32)
    up_part = jnp.dot(hidden_all, both[:, units:], preferred_element_type=jnp.float32)
    active = (jax.nn.silu(gate) * up_part).astype(jnp.bfloat16)
    active_cols = deliver(active, down_weight.shape[0], gate_weight.shape[1])
    mlp_out = seq_total(
        jnp.dot(active_cols, down_weight, preferred_element_type=jnp.float32)
    )
    mlp_squares = feature_sums(jnp.sum(mlp_out * mlp_out, axis=1))
    decoded = (
        hidden.astype(jnp.float32) + mlp_out * inverse_rms(mlp_squares) * feedforward_gain
    ).astype(jnp.bfloat16)
    return decoded.reshape(STEPS, R, local_width)


def solution(mesh):
    global SEQ_SIZE, MP_SIZE, SEQ_FACTORS
    SEQ_SIZE = mesh.shape["seq"]
    MP_SIZE = mesh.shape["mp"]
    factors = []
    left = SEQ_SIZE // MP_SIZE
    if left % 2 == 0:
        factors.append(2)
        left //= 2
    while left % 4 == 0:
        factors.append(4)
        left //= 4
    if left > 1:
        factors.append(left)
    factors.append(MP_SIZE)
    SEQ_FACTORS = tuple(factors)
    in_specs = (
        P(None, None, "mp"),
        P("seq", "mp"),
        P("seq", "mp"),
        P("seq", "mp"),
        P("seq", "mp"),
        P("seq", "mp"),
        P("seq", "mp"),
        P("seq", "mp"),
        P("mp"),
        P("mp"),
        P("mp"),
        P("mp"),
        P("seq", None, "mp"),
        P("seq", None, "mp"),
        P(),
        P("seq"),
        P("seq"),
    )
    out_specs = P(None, None, "mp")
    return jax.shard_map(local, mesh=mesh, in_specs=in_specs, out_specs=out_specs, check_vma=False)
```

```python
import jax
import jax.numpy as jnp
from jax import lax
from jax.sharding import PartitionSpec as P

D = 2048
HD = 128
R = 16
STEPS = 4
PAGE = 256


epsilon = 1e-06
rope_base = 500000.0
very_low = -1e30
SEQ_SIZE = 32
MP_SIZE = 4
SEQ_FACTORS = (2, 4, 4)


def rotary(values, positions):
    half_width = HD // 2
    frequencies = rope_base ** (-2.0 * jnp.arange(half_width, dtype=jnp.float32) / HD)
    angles = positions.astype(jnp.float32)[:, None] * frequencies[None, :]
    cosine = jnp.cos(angles)[:, None, :]
    sine_part = jnp.sin(angles)[:, None, :]
    first_half = values[..., :half_width]
    second_half = values[..., half_width:]
    return jnp.concatenate(
        [
            first_half * cosine - second_half * sine_part,
            second_half * cosine + first_half * sine_part,
        ],
        axis=-1,
    )


def seq_columns(block, width):
    per = block.shape[1] // width
    seq = lax.axis_index("seq")
    piece = lax.dynamic_slice_in_dim(block, (seq % per) * width, width, 1)
    pairs = [
        (s * MP_SIZE + m, (m * per + s % per) * MP_SIZE + s // per)
        for s in range(SEQ_SIZE)
        for m in range(MP_SIZE)
    ]
    return lax.ppermute(piece, ("seq", "mp"), pairs)


def seq_groups():
    groups = []
    stride = 1
    for size in SEQ_FACTORS:
        groups.append((stride, size))
        stride *= size
    return groups


def digit_pairs(count, stride, size, shift):
    return [
        (i, i + (((i // stride) % size + shift) % size - (i // stride) % size) * stride)
        for i in range(count)
    ]


def exchange(value, axis, count, stride, size):
    digit = (lax.axis_index(axis) // stride) % size
    pieces = [value] + [
        lax.ppermute(value, axis, digit_pairs(count, stride, size, shift)) for shift in range(1, size)
    ]
    return jnp.stack([pick(pieces, (digit - slot) % size) for slot in range(size)])


def pick(pieces, index):
    chosen = pieces[0]
    for k in range(1, len(pieces)):
        chosen = jnp.where(index == k, pieces[k], chosen)
    return chosen


def scatter_digit(current, stride, size):
    me = lax.axis_index("seq")
    digit = (me // stride) % size
    part = current.shape[1] // size
    total = lax.dynamic_slice_in_dim(current, digit * part, part, 1)
    for shift in range(1, size):
        send = lax.dynamic_slice_in_dim(current, ((digit + shift) % size) * part, part, 1)
        total = total + lax.ppermute(send, "seq", digit_pairs(SEQ_SIZE, stride, size, shift))
    return total


def gather_digit(current, stride, size):
    me = lax.axis_index("seq")
    digit = (me // stride) % size
    part = current.shape[1]
    whole = jnp.zeros((current.shape[0], part * size), current.dtype)
    whole = lax.dynamic_update_slice_in_dim(whole, current, digit * part, 1)
    for shift in range(1, size):
        received = lax.ppermute(current, "seq", digit_pairs(SEQ_SIZE, stride, size, shift))
        whole = lax.dynamic_update_slice_in_dim(whole, received, ((digit - shift) % size) * part, 1)
    return whole


def seq_total(partial_value, ladder=False, butterfly=False):
    groups = seq_groups()
    current = partial_value
    if ladder:
        for stride, size in groups:
            current = scatter_digit(current, stride, size)
        for stride, size in reversed(groups):
            current = gather_digit(current, stride, size)
        return current
    if butterfly:
        for stride, size in groups:
            current = jnp.sum(exchange(current, "seq", SEQ_SIZE, stride, size), axis=0)
        return current
    stride, size = groups[0]
    current = scatter_digit(current, stride, size)
    for other_stride, other_size in groups[1:]:
        current = jnp.sum(exchange(current, "seq", SEQ_SIZE, other_stride, other_size), axis=0)
    return gather_digit(current, stride, size)


def gate_up_active(gate_part, up_part):
    rows, units = gate_part.shape
    unit_block = units // SEQ_SIZE
    arranged = jnp.stack(
        [gate_part.reshape(rows, SEQ_SIZE, unit_block), up_part.reshape(rows, SEQ_SIZE, unit_block)],
        axis=2,
    ).reshape(rows, 2 * units)
    groups = seq_groups()
    for stride, size in groups:
        arranged = scatter_digit(arranged, stride, size)
    active = (jax.nn.silu(arranged[:, :unit_block]) * arranged[:, unit_block:]).astype(jnp.bfloat16)
    last_stride, last_size = groups[-1]
    active = gather_digit(active, last_stride, last_size)
    per = SEQ_SIZE // MP_SIZE
    pairs = []
    for s in range(SEQ_SIZE):
        lead = 0
        for stride, size in groups[:-1]:
            lead = lead * size + (s // stride) % size
        last = (s // last_stride) % last_size
        for m in range(MP_SIZE):
            pairs.append((s * MP_SIZE + m, (m * per + lead) * MP_SIZE + last))
    return lax.ppermute(active, ("seq", "mp"), pairs)


def deliver(piece, width, local_width):
    slice_width = piece.shape[1]
    per = local_width // width
    holders = width // slice_width
    assert holders == MP_SIZE
    mp = lax.axis_index("mp")
    received = []
    for shift in range(MP_SIZE):
        pairs = [
            (s * MP_SIZE + m, (m * per + s // holders) * MP_SIZE + (s % holders + shift) % MP_SIZE)
            for s in range(SEQ_SIZE)
            for m in range(MP_SIZE)
        ]
        received.append(lax.ppermute(piece, ("seq", "mp"), pairs))
    return jnp.concatenate([pick(received, (mp - slot) % MP_SIZE) for slot in range(MP_SIZE)], axis=1)


def full_rows(weight):
    rows, cols = weight.shape
    block = cols // SEQ_SIZE
    moved = lax.all_to_all(weight.reshape(rows, SEQ_SIZE, block), "seq", 1, 0, tiled=True)
    return moved.reshape(rows * SEQ_SIZE, block)


def merge_stack(stack):
    member_max = stack[..., HD]
    highest = jnp.max(member_max, axis=0)
    scale = jnp.exp(member_max - highest[None])
    totals = jnp.sum(stack[..., HD + 1] * scale, axis=0)
    running = jnp.sum(stack[..., :HD] * scale[..., None], axis=0)
    return jnp.concatenate([running, highest[..., None], totals[..., None]], axis=-1)


def feature_sums(squares):
    return jnp.sum(exchange(squares, "mp", MP_SIZE, 1, MP_SIZE), axis=0)


def inverse_rms(square_total):
    return lax.rsqrt(square_total / D + epsilon)[:, None]


def local(
    states,
    query_weight,
    key_weight,
    value_weight,
    output_weight,
    gate_weight,
    up_weight,
    down_weight,
    query_gain,
    key_gain,
    attention_gain,
    feedforward_gain,
    key_cache,
    value_cache,
    lengths,
    page_owner,
    page_index,
):
    local_width = query_weight.shape[1]
    local_heads = local_width // HD
    rows = STEPS * R
    score_scale = HD ** (-0.5)
    token_rows = states.reshape(rows, local_width)
    positions = (lengths[None, :] + jnp.arange(STEPS, dtype=jnp.int32)[:, None]).reshape(rows)

    sliced = seq_columns(token_rows, query_weight.shape[0])
    summed = seq_total(
        jnp.concatenate(
            [
                jnp.dot(sliced, query_weight, preferred_element_type=jnp.float32),
                jnp.dot(sliced, key_weight, preferred_element_type=jnp.float32),
                jnp.dot(sliced, value_weight, preferred_element_type=jnp.float32),
            ],
            axis=1,
        )
    )
    query_raw = summed[:, :local_width]
    key_raw = summed[:, local_width : 2 * local_width]
    value_raw = summed[:, 2 * local_width :]
    squares = feature_sums(
        jnp.stack([jnp.sum(query_raw * query_raw, axis=1), jnp.sum(key_raw * key_raw, axis=1)], axis=1)
    )
    queries = rotary(
        (query_raw * inverse_rms(squares[:, 0]) * query_gain).reshape(rows, local_heads, HD), positions
    ).astype(jnp.bfloat16)
    new_keys = rotary(
        (key_raw * inverse_rms(squares[:, 1]) * key_gain).reshape(rows, local_heads, HD), positions
    ).astype(jnp.bfloat16)
    new_values = value_raw.astype(jnp.bfloat16).reshape(rows, local_heads, HD)

    pages = key_cache.shape[0]
    tokens = pages * PAGE
    keys = key_cache.reshape(tokens, local_width)
    values = value_cache.reshape(tokens, local_width)
    token_owner = jnp.repeat(page_owner, PAGE)
    token_spot = (page_index[:, None] * PAGE + jnp.arange(PAGE, dtype=jnp.int32)[None, :]).reshape(tokens)
    validity = (token_owner[None, :] == jnp.arange(R, dtype=jnp.int32)[:, None]) & (
        token_spot[None, :] < lengths[:, None]
    )
    head_of_feature = jnp.arange(local_width, dtype=jnp.int32) // HD
    flat_queries = queries.reshape(rows, local_width)
    block_queries = jnp.where(
        head_of_feature[None, None, :] == jnp.arange(local_heads, dtype=jnp.int32)[:, None, None],
        flat_queries[None],
        jnp.zeros((), jnp.bfloat16),
    ).reshape(local_heads * rows, local_width)
    scores = lax.dot_general(
        block_queries, keys, (((1,), (1,)), ((), ())), preferred_element_type=jnp.float32
    ).reshape(local_heads, STEPS, R, tokens) * score_scale
    valid = validity[None, None]
    masked = jnp.where(valid, scores, very_low)
    maxima = jnp.max(masked, axis=3)
    weights = jnp.where(valid, jnp.exp(masked - maxima[..., None]), 0.0)
    totals = jnp.sum(weights, axis=3).reshape(local_heads, rows)
    maxima = maxima.reshape(local_heads, rows)
    all_heads = lax.dot_general(
        values,
        weights.astype(jnp.bfloat16).reshape(local_heads * rows, tokens),
        (((0,), (1,)), ((), ())),
        preferred_element_type=jnp.float32,
    ).reshape(local_heads, HD, local_heads, rows)
    running = jnp.stack([all_heads[h, :, h].T for h in range(local_heads)])

    seq = lax.axis_index("seq")
    slice_width = local_width // SEQ_SIZE
    per_head = HD // slice_width
    send = jnp.concatenate(
        [
            running.reshape(local_heads, rows, per_head, slice_width).transpose(0, 2, 1, 3),
            jnp.broadcast_to(maxima[:, None, :, None], (local_heads, per_head, rows, 1)),
            jnp.broadcast_to(totals[:, None, :, None], (local_heads, per_head, rows, 1)),
        ],
        axis=3,
    ).reshape(SEQ_SIZE, rows, slice_width + 2)
    sources = lax.all_to_all(send, "seq", 0, 0, tiled=True)
    source_max = sources[..., slice_width]
    cache_highest = jnp.max(source_max, axis=0)
    scale = jnp.exp(source_max - cache_highest[None])
    cache_totals = jnp.sum(sources[..., slice_width + 1] * scale, axis=0)
    cache_running = jnp.sum(sources[..., :slice_width] * scale[..., None], axis=0)

    head = seq // per_head
    offset = (seq % per_head) * slice_width
    q4 = lax.dynamic_index_in_dim(queries, head, 1, keepdims=False).reshape(STEPS, R, HD)
    k4 = lax.dynamic_index_in_dim(new_keys, head, 1, keepdims=False).reshape(STEPS, R, HD)
    v4 = lax.dynamic_slice_in_dim(
        lax.dynamic_index_in_dim(new_values, head, 1, keepdims=False), offset, slice_width, 1
    ).reshape(STEPS, R, slice_width)
    fresh_scores = jnp.einsum("srd,trd->srt", q4, k4, preferred_element_type=jnp.float32) * score_scale
    allowed = (jnp.arange(STEPS)[None, :] <= jnp.arange(STEPS)[:, None])[:, None, :]
    fresh_scores = jnp.where(allowed, fresh_scores, very_low)
    cache_highest = cache_highest.reshape(STEPS, R)
    highest = jnp.maximum(cache_highest, jnp.max(fresh_scores, axis=-1))
    fresh_weights = jnp.where(allowed, jnp.exp(fresh_scores - highest[..., None]), 0.0)
    factor = jnp.exp(cache_highest - highest)
    final_totals = cache_totals.reshape(STEPS, R) * factor + jnp.sum(fresh_weights, axis=-1)
    final_running = cache_running.reshape(STEPS, R, slice_width) * factor[..., None] + jnp.einsum(
        "srt,trd->srd", fresh_weights.astype(jnp.bfloat16), v4, preferred_element_type=jnp.float32
    )
    attended = (final_running / final_totals[..., None]).astype(jnp.bfloat16).reshape(rows, slice_width)

    sliced = deliver(attended, output_weight.shape[0], local_width)
    attention_out = seq_total(
        jnp.dot(sliced, output_weight, preferred_element_type=jnp.float32)
    )
    attention_squares = feature_sums(jnp.sum(attention_out * attention_out, axis=1))
    hidden = (
        token_rows.astype(jnp.float32) + attention_out * inverse_rms(attention_squares) * attention_gain
    ).astype(jnp.bfloat16)

    hidden_all = jnp.transpose(exchange(hidden, "mp", MP_SIZE, 1, MP_SIZE), (1, 0, 2)).reshape(
        rows, MP_SIZE * local_width
    )
    units = gate_weight.shape[1] // SEQ_SIZE
    both = full_rows(
        jnp.concatenate(
            [
                gate_weight.reshape(-1, SEQ_SIZE, units),
                up_weight.reshape(-1, SEQ_SIZE, units),
            ],
            axis=2,
        ).reshape(gate_weight.shape[0], 2 * gate_weight.shape[1])
    )
    gate = jnp.dot(hidden_all, both[:, :units], preferred_element_type=jnp.float32)
    up_part = jnp.dot(hidden_all, both[:, units:], preferred_element_type=jnp.float32)
    active = (jax.nn.silu(gate) * up_part).astype(jnp.bfloat16)
    active_cols = deliver(active, down_weight.shape[0], gate_weight.shape[1])
    mlp_out = seq_total(
        jnp.dot(active_cols, down_weight, preferred_element_type=jnp.float32)
    )
    mlp_squares = feature_sums(jnp.sum(mlp_out * mlp_out, axis=1))
    decoded = (
        hidden.astype(jnp.float32) + mlp_out * inverse_rms(mlp_squares) * feedforward_gain
    ).astype(jnp.bfloat16)
    return decoded.reshape(STEPS, R, local_width)


def solution(mesh):
    global SEQ_SIZE, MP_SIZE, SEQ_FACTORS
    SEQ_SIZE = mesh.shape["seq"]
    MP_SIZE = mesh.shape["mp"]
    factors = []
    left = SEQ_SIZE // MP_SIZE
    if left % 2 == 0:
        factors.append(2)
        left //= 2
    while left % 4 == 0:
        factors.append(4)
        left //= 4
    if left > 1:
        factors.append(left)
    factors.append(MP_SIZE)
    SEQ_FACTORS = tuple(factors)
    in_specs = (
        P(None, None, "mp"),
        P("seq", "mp"),
        P("seq", "mp"),
        P("seq", "mp"),
        P("seq", "mp"),
        P("seq", "mp"),
        P("seq", "mp"),
        P("seq", "mp"),
        P("mp"),
        P("mp"),
        P("mp"),
        P("mp"),
        P("seq", None, "mp"),
        P("seq", None, "mp"),
        P(),
        P("seq"),
        P("seq"),
    )
    out_specs = P(None, None, "mp")
    return jax.shard_map(local, mesh=mesh, in_specs=in_specs, out_specs=out_specs, check_vma=False)
```

```python
import jax
import jax.numpy as jnp
from jax import lax
from jax.sharding import PartitionSpec as P

D = 2048
HD = 128
R = 16
STEPS = 4
PAGE = 256


epsilon = 1e-06
rope_base = 500000.0
very_low = -1e30
SEQ_SIZE = 32
MP_SIZE = 4
SEQ_FACTORS = (2, 4, 4)


def rotary(values, positions):
    half_width = HD // 2
    frequencies = rope_base ** (-2.0 * jnp.arange(half_width, dtype=jnp.float32) / HD)
    angles = positions.astype(jnp.float32)[:, None] * frequencies[None, :]
    cosine = jnp.cos(angles)[:, None, :]
    sine_part = jnp.sin(angles)[:, None, :]
    first_half = values[..., :half_width]
    second_half = values[..., half_width:]
    return jnp.concatenate(
        [
            first_half * cosine - second_half * sine_part,
            second_half * cosine + first_half * sine_part,
        ],
        axis=-1,
    )


def seq_columns(block, width):
    per = block.shape[1] // width
    seq = lax.axis_index("seq")
    piece = pick([block[:, k * width : (k + 1) * width] for k in range(per)], seq % per)
    pairs = [
        (s * MP_SIZE + m, (m * per + s % per) * MP_SIZE + s // per)
        for s in range(SEQ_SIZE)
        for m in range(MP_SIZE)
    ]
    return lax.ppermute(piece, ("seq", "mp"), pairs)


def seq_groups():
    groups = []
    stride = 1
    for size in SEQ_FACTORS:
        groups.append((stride, size))
        stride *= size
    return groups


def digit_pairs(count, stride, size, shift):
    return [
        (i, i + (((i // stride) % size + shift) % size - (i // stride) % size) * stride)
        for i in range(count)
    ]


def exchange(value, axis, count, stride, size):
    digit = (lax.axis_index(axis) // stride) % size
    pieces = [value] + [
        lax.ppermute(value, axis, digit_pairs(count, stride, size, shift)) for shift in range(1, size)
    ]
    return jnp.stack([pick(pieces, (digit - slot) % size) for slot in range(size)])


def pick(pieces, index):
    chosen = pieces[0]
    for k in range(1, len(pieces)):
        chosen = jnp.where(index == k, pieces[k], chosen)
    return chosen


def scatter_digit(current, stride, size):
    me = lax.axis_index("seq")
    digit = (me // stride) % size
    part = current.shape[1] // size
    parts = [current[:, p * part : (p + 1) * part] for p in range(size)]
    total = pick(parts, digit)
    for shift in range(1, size):
        send = pick(parts, (digit + shift) % size)
        total = total + lax.ppermute(send, "seq", digit_pairs(SEQ_SIZE, stride, size, shift))
    return total


def gather_digit(current, stride, size):
    me = lax.axis_index("seq")
    digit = (me // stride) % size
    pieces = [current] + [
        lax.ppermute(current, "seq", digit_pairs(SEQ_SIZE, stride, size, shift))
        for shift in range(1, size)
    ]
    return jnp.concatenate([pick(pieces, (digit - slot) % size) for slot in range(size)], axis=1)


def seq_total(partial_value, ladder=False, butterfly=False):
    groups = seq_groups()
    current = partial_value
    if ladder:
        for stride, size in groups:
            current = scatter_digit(current, stride, size)
        for stride, size in reversed(groups):
            current = gather_digit(current, stride, size)
        return current
    if butterfly:
        for stride, size in groups:
            current = jnp.sum(exchange(current, "seq", SEQ_SIZE, stride, size), axis=0)
        return current
    stride, size = groups[0]
    current = scatter_digit(current, stride, size)
    for other_stride, other_size in groups[1:]:
        current = jnp.sum(exchange(current, "seq", SEQ_SIZE, other_stride, other_size), axis=0)
    return gather_digit(current, stride, size)


def gate_up_active(gate_part, up_part):
    rows, units = gate_part.shape
    unit_block = units // SEQ_SIZE
    arranged = jnp.stack(
        [gate_part.reshape(rows, SEQ_SIZE, unit_block), up_part.reshape(rows, SEQ_SIZE, unit_block)],
        axis=2,
    ).reshape(rows, 2 * units)
    groups = seq_groups()
    for stride, size in groups:
        arranged = scatter_digit(arranged, stride, size)
    active = (jax.nn.silu(arranged[:, :unit_block]) * arranged[:, unit_block:]).astype(jnp.bfloat16)
    last_stride, last_size = groups[-1]
    active = gather_digit(active, last_stride, last_size)
    per = SEQ_SIZE // MP_SIZE
    pairs = []
    for s in range(SEQ_SIZE):
        lead = 0
        for stride, size in groups[:-1]:
            lead = lead * size + (s // stride) % size
        last = (s // last_stride) % last_size
        for m in range(MP_SIZE):
            pairs.append((s * MP_SIZE + m, (m * per + lead) * MP_SIZE + last))
    return lax.ppermute(active, ("seq", "mp"), pairs)


def deliver(piece, width, local_width):
    slice_width = piece.shape[1]
    per = local_width // width
    holders = width // slice_width
    assert holders == MP_SIZE
    mp = lax.axis_index("mp")
    received = []
    for shift in range(MP_SIZE):
        pairs = [
            (s * MP_SIZE + m, (m * per + s // holders) * MP_SIZE + (s % holders + shift) % MP_SIZE)
            for s in range(SEQ_SIZE)
            for m in range(MP_SIZE)
        ]
        received.append(lax.ppermute(piece, ("seq", "mp"), pairs))
    return jnp.concatenate([pick(received, (mp - slot) % MP_SIZE) for slot in range(MP_SIZE)], axis=1)


def full_rows(weight):
    rows, cols = weight.shape
    block = cols // SEQ_SIZE
    moved = lax.all_to_all(weight.reshape(rows, SEQ_SIZE, block), "seq", 1, 0, tiled=True)
    return moved.reshape(rows * SEQ_SIZE, block)


def merge_stack(stack):
    member_max = stack[..., HD]
    highest = jnp.max(member_max, axis=0)
    scale = jnp.exp(member_max - highest[None])
    totals = jnp.sum(stack[..., HD + 1] * scale, axis=0)
    running = jnp.sum(stack[..., :HD] * scale[..., None], axis=0)
    return jnp.concatenate([running, highest[..., None], totals[..., None]], axis=-1)


def feature_sums(squares):
    return jnp.sum(exchange(squares, "mp", MP_SIZE, 1, MP_SIZE), axis=0)


def inverse_rms(square_total):
    return lax.rsqrt(square_total / D + epsilon)[:, None]


def local(
    states,
    query_weight,
    key_weight,
    value_weight,
    output_weight,
    gate_weight,
    up_weight,
    down_weight,
    query_gain,
    key_gain,
    attention_gain,
    feedforward_gain,
    key_cache,
    value_cache,
    lengths,
    page_owner,
    page_index,
):
    local_width = query_weight.shape[1]
    local_heads = local_width // HD
    rows = STEPS * R
    score_scale = HD ** (-0.5)
    token_rows = states.reshape(rows, local_width)
    positions = (lengths[None, :] + jnp.arange(STEPS, dtype=jnp.int32)[:, None]).reshape(rows)

    sliced = seq_columns(token_rows, query_weight.shape[0])
    summed = seq_total(
        jnp.concatenate(
            [
                jnp.dot(sliced, query_weight, preferred_element_type=jnp.float32),
                jnp.dot(sliced, key_weight, preferred_element_type=jnp.float32),
                jnp.dot(sliced, value_weight, preferred_element_type=jnp.float32),
            ],
            axis=1,
        )
    )
    query_raw = summed[:, :local_width]
    key_raw = summed[:, local_width : 2 * local_width]
    value_raw = summed[:, 2 * local_width :]
    squares = feature_sums(
        jnp.stack([jnp.sum(query_raw * query_raw, axis=1), jnp.sum(key_raw * key_raw, axis=1)], axis=1)
    )
    queries = rotary(
        (query_raw * inverse_rms(squares[:, 0]) * query_gain).reshape(rows, local_heads, HD), positions
    ).astype(jnp.bfloat16)
    new_keys = rotary(
        (key_raw * inverse_rms(squares[:, 1]) * key_gain).reshape(rows, local_heads, HD), positions
    ).astype(jnp.bfloat16)
    new_values = value_raw.astype(jnp.bfloat16).reshape(rows, local_heads, HD)

    pages = key_cache.shape[0]
    tokens = pages * PAGE
    keys = key_cache.reshape(tokens, local_width)
    values = value_cache.reshape(tokens, local_width)
    token_owner = jnp.repeat(page_owner, PAGE)
    token_spot = (page_index[:, None] * PAGE + jnp.arange(PAGE, dtype=jnp.int32)[None, :]).reshape(tokens)
    validity = (token_owner[None, :] == jnp.arange(R, dtype=jnp.int32)[:, None]) & (
        token_spot[None, :] < lengths[:, None]
    )
    head_of_feature = jnp.arange(local_width, dtype=jnp.int32) // HD
    flat_queries = queries.reshape(rows, local_width)
    block_queries = jnp.where(
        head_of_feature[None, None, :] == jnp.arange(local_heads, dtype=jnp.int32)[:, None, None],
        flat_queries[None],
        jnp.zeros((), jnp.bfloat16),
    ).reshape(local_heads * rows, local_width)
    scores = lax.dot_general(
        block_queries, keys, (((1,), (1,)), ((), ())), preferred_element_type=jnp.float32
    ).reshape(local_heads, STEPS, R, tokens) * score_scale
    valid = validity[None, None]
    masked = jnp.where(valid, scores, very_low)
    maxima = jnp.max(masked, axis=3)
    weights = jnp.where(valid, jnp.exp(masked - maxima[..., None]), 0.0)
    totals = jnp.sum(weights, axis=3).reshape(local_heads, rows)
    maxima = maxima.reshape(local_heads, rows)
    all_heads = lax.dot_general(
        values,
        weights.astype(jnp.bfloat16).reshape(local_heads * rows, tokens),
        (((0,), (1,)), ((), ())),
        preferred_element_type=jnp.float32,
    ).reshape(local_heads, HD, local_heads, rows)
    running = jnp.stack([all_heads[h, :, h].T for h in range(local_heads)])

    seq = lax.axis_index("seq")
    slice_width = local_width // SEQ_SIZE
    per_head = HD // slice_width
    send = jnp.concatenate(
        [
            running.reshape(local_heads, rows, per_head, slice_width).transpose(0, 2, 1, 3),
            jnp.broadcast_to(maxima[:, None, :, None], (local_heads, per_head, rows, 1)),
            jnp.broadcast_to(totals[:, None, :, None], (local_heads, per_head, rows, 1)),
        ],
        axis=3,
    ).reshape(SEQ_SIZE, rows, slice_width + 2)
    sources = lax.all_to_all(send, "seq", 0, 0, tiled=True)
    source_max = sources[..., slice_width]
    cache_highest = jnp.max(source_max, axis=0)
    scale = jnp.exp(source_max - cache_highest[None])
    cache_totals = jnp.sum(sources[..., slice_width + 1] * scale, axis=0)
    cache_running = jnp.sum(sources[..., :slice_width] * scale[..., None], axis=0)

    head = seq // per_head
    offset = (seq % per_head) * slice_width
    q4 = lax.dynamic_index_in_dim(queries, head, 1, keepdims=False).reshape(STEPS, R, HD)
    k4 = lax.dynamic_index_in_dim(new_keys, head, 1, keepdims=False).reshape(STEPS, R, HD)
    v4 = lax.dynamic_slice_in_dim(
        lax.dynamic_index_in_dim(new_values, head, 1, keepdims=False), offset, slice_width, 1
    ).reshape(STEPS, R, slice_width)
    fresh_scores = jnp.einsum("srd,trd->srt", q4, k4, preferred_element_type=jnp.float32) * score_scale
    allowed = (jnp.arange(STEPS)[None, :] <= jnp.arange(STEPS)[:, None])[:, None, :]
    fresh_scores = jnp.where(allowed, fresh_scores, very_low)
    cache_highest = cache_highest.reshape(STEPS, R)
    highest = jnp.maximum(cache_highest, jnp.max(fresh_scores, axis=-1))
    fresh_weights = jnp.where(allowed, jnp.exp(fresh_scores - highest[..., None]), 0.0)
    factor = jnp.exp(cache_highest - highest)
    final_totals = cache_totals.reshape(STEPS, R) * factor + jnp.sum(fresh_weights, axis=-1)
    final_running = cache_running.reshape(STEPS, R, slice_width) * factor[..., None] + jnp.einsum(
        "srt,trd->srd", fresh_weights.astype(jnp.bfloat16), v4, preferred_element_type=jnp.float32
    )
    attended = (final_running / final_totals[..., None]).astype(jnp.bfloat16).reshape(rows, slice_width)

    sliced = deliver(attended, output_weight.shape[0], local_width)
    attention_out = seq_total(
        jnp.dot(sliced, output_weight, preferred_element_type=jnp.float32)
    )
    attention_squares = feature_sums(jnp.sum(attention_out * attention_out, axis=1))
    hidden = (
        token_rows.astype(jnp.float32) + attention_out * inverse_rms(attention_squares) * attention_gain
    ).astype(jnp.bfloat16)

    hidden_all = jnp.transpose(exchange(hidden, "mp", MP_SIZE, 1, MP_SIZE), (1, 0, 2)).reshape(
        rows, MP_SIZE * local_width
    )
    units = gate_weight.shape[1] // SEQ_SIZE
    both = full_rows(
        jnp.concatenate(
            [
                gate_weight.reshape(-1, SEQ_SIZE, units),
                up_weight.reshape(-1, SEQ_SIZE, units),
            ],
            axis=2,
        ).reshape(gate_weight.shape[0], 2 * gate_weight.shape[1])
    )
    gate = jnp.dot(hidden_all, both[:, :units], preferred_element_type=jnp.float32)
    up_part = jnp.dot(hidden_all, both[:, units:], preferred_element_type=jnp.float32)
    active = (jax.nn.silu(gate) * up_part).astype(jnp.bfloat16)
    active_cols = deliver(active, down_weight.shape[0], gate_weight.shape[1])
    mlp_out = seq_total(
        jnp.dot(active_cols, down_weight, preferred_element_type=jnp.float32)
    )
    mlp_squares = feature_sums(jnp.sum(mlp_out * mlp_out, axis=1))
    decoded = (
        hidden.astype(jnp.float32) + mlp_out * inverse_rms(mlp_squares) * feedforward_gain
    ).astype(jnp.bfloat16)
    return decoded.reshape(STEPS, R, local_width)


def solution(mesh):
    global SEQ_SIZE, MP_SIZE, SEQ_FACTORS
    SEQ_SIZE = mesh.shape["seq"]
    MP_SIZE = mesh.shape["mp"]
    factors = []
    left = SEQ_SIZE // MP_SIZE
    if left % 2 == 0:
        factors.append(2)
        left //= 2
    while left % 4 == 0:
        factors.append(4)
        left //= 4
    if left > 1:
        factors.append(left)
    factors.append(MP_SIZE)
    SEQ_FACTORS = tuple(factors)
    in_specs = (
        P(None, None, "mp"),
        P("seq", "mp"),
        P("seq", "mp"),
        P("seq", "mp"),
        P("seq", "mp"),
        P("seq", "mp"),
        P("seq", "mp"),
        P("seq", "mp"),
        P("mp"),
        P("mp"),
        P("mp"),
        P("mp"),
        P("seq", None, "mp"),
        P("seq", None, "mp"),
        P(),
        P("seq"),
        P("seq"),
    )
    out_specs = P(None, None, "mp")
    return jax.shard_map(local, mesh=mesh, in_specs=in_specs, out_specs=out_specs, check_vma=False)
```

```python
import jax
import jax.numpy as jnp
from jax import lax
from jax.sharding import PartitionSpec as P

D = 2048
HD = 128
R = 16
STEPS = 4
PAGE = 256


epsilon = 1e-06
rope_base = 500000.0
very_low = -1e30
SEQ_SIZE = 32
MP_SIZE = 4
SEQ_FACTORS = (2, 4, 4)


def rotary(values, positions):
    half_width = HD // 2
    frequencies = rope_base ** (-2.0 * jnp.arange(half_width, dtype=jnp.float32) / HD)
    angles = positions.astype(jnp.float32)[:, None] * frequencies[None, :]
    cosine = jnp.cos(angles)[:, None, :]
    sine_part = jnp.sin(angles)[:, None, :]
    first_half = values[..., :half_width]
    second_half = values[..., half_width:]
    return jnp.concatenate(
        [
            first_half * cosine - second_half * sine_part,
            second_half * cosine + first_half * sine_part,
        ],
        axis=-1,
    )


def seq_columns(block, width):
    per = block.shape[1] // width
    seq = lax.axis_index("seq")
    piece = lax.dynamic_slice_in_dim(block, (seq % per) * width, width, 1)
    pairs = [
        (s * MP_SIZE + m, (m * per + s % per) * MP_SIZE + s // per)
        for s in range(SEQ_SIZE)
        for m in range(MP_SIZE)
    ]
    return lax.ppermute(piece, ("seq", "mp"), pairs)


def seq_groups():
    groups = []
    stride = 1
    for size in SEQ_FACTORS:
        groups.append((stride, size))
        stride *= size
    return groups


def digit_pairs(count, stride, size, shift):
    return [
        (i, i + (((i // stride) % size + shift) % size - (i // stride) % size) * stride)
        for i in range(count)
    ]


def exchange(value, axis, count, stride, size):
    digit = (lax.axis_index(axis) // stride) % size
    pieces = [value] + [
        lax.ppermute(value, axis, digit_pairs(count, stride, size, shift)) for shift in range(1, size)
    ]
    return jnp.stack([pick(pieces, (digit - slot) % size) for slot in range(size)])


def pick(pieces, index):
    chosen = pieces[0]
    for k in range(1, len(pieces)):
        chosen = jnp.where(index == k, pieces[k], chosen)
    return chosen


def scatter_digit(current, stride, size):
    me = lax.axis_index("seq")
    digit = (me // stride) % size
    part = current.shape[1] // size
    total = lax.dynamic_slice_in_dim(current, digit * part, part, 1)
    for shift in range(1, size):
        send = lax.dynamic_slice_in_dim(current, ((digit + shift) % size) * part, part, 1)
        total = total + lax.ppermute(send, "seq", digit_pairs(SEQ_SIZE, stride, size, shift))
    return total


def gather_digit(current, stride, size):
    me = lax.axis_index("seq")
    digit = (me // stride) % size
    part = current.shape[1]
    whole = jnp.zeros((current.shape[0], part * size), current.dtype)
    whole = lax.dynamic_update_slice_in_dim(whole, current, digit * part, 1)
    for shift in range(1, size):
        received = lax.ppermute(current, "seq", digit_pairs(SEQ_SIZE, stride, size, shift))
        whole = lax.dynamic_update_slice_in_dim(whole, received, ((digit - shift) % size) * part, 1)
    return whole


def seq_total(partial_value, ladder=False, butterfly=False):
    groups = seq_groups()
    current = partial_value
    if ladder:
        for stride, size in groups:
            current = scatter_digit(current, stride, size)
        for stride, size in reversed(groups):
            current = gather_digit(current, stride, size)
        return current
    if butterfly:
        for stride, size in groups:
            current = jnp.sum(exchange(current, "seq", SEQ_SIZE, stride, size), axis=0)
        return current
    stride, size = groups[0]
    current = scatter_digit(current, stride, size)
    for other_stride, other_size in groups[1:]:
        current = jnp.sum(exchange(current, "seq", SEQ_SIZE, other_stride, other_size), axis=0)
    return gather_digit(current, stride, size)


def gate_up_active(gate_part, up_part):
    rows, units = gate_part.shape
    unit_block = units // SEQ_SIZE
    arranged = jnp.stack(
        [gate_part.reshape(rows, SEQ_SIZE, unit_block), up_part.reshape(rows, SEQ_SIZE, unit_block)],
        axis=2,
    ).reshape(rows, 2 * units)
    groups = seq_groups()
    for stride, size in groups:
        arranged = scatter_digit(arranged, stride, size)
    active = (jax.nn.silu(arranged[:, :unit_block]) * arranged[:, unit_block:]).astype(jnp.bfloat16)
    last_stride, last_size = groups[-1]
    active = gather_digit(active, last_stride, last_size)
    per = SEQ_SIZE // MP_SIZE
    pairs = []
    for s in range(SEQ_SIZE):
        lead = 0
        for stride, size in groups[:-1]:
            lead = lead * size + (s // stride) % size
        last = (s // last_stride) % last_size
        for m in range(MP_SIZE):
            pairs.append((s * MP_SIZE + m, (m * per + lead) * MP_SIZE + last))
    return lax.ppermute(active, ("seq", "mp"), pairs)


def deliver(piece, width, local_width):
    slice_width = piece.shape[1]
    per = local_width // width
    holders = width // slice_width
    assert holders == MP_SIZE
    mp = lax.axis_index("mp")
    received = []
    for shift in range(MP_SIZE):
        pairs = [
            (s * MP_SIZE + m, (m * per + s // holders) * MP_SIZE + (s % holders + shift) % MP_SIZE)
            for s in range(SEQ_SIZE)
            for m in range(MP_SIZE)
        ]
        received.append(lax.ppermute(piece, ("seq", "mp"), pairs))
    return jnp.concatenate([pick(received, (mp - slot) % MP_SIZE) for slot in range(MP_SIZE)], axis=1)


def full_rows(weight):
    rows, cols = weight.shape
    block = cols // SEQ_SIZE
    moved = lax.all_to_all(weight.reshape(rows, SEQ_SIZE, block), "seq", 1, 0, tiled=True)
    return moved.reshape(rows * SEQ_SIZE, block)


def seq_total_and_squares(partial_value):
    groups = seq_groups()
    stride, size = groups[0]
    current = scatter_digit(partial_value, stride, size)
    for other_stride, other_size in groups[1:]:
        current = jnp.sum(exchange(current, "seq", SEQ_SIZE, other_stride, other_size), axis=0)
    half_squares = jnp.sum(current * current, axis=1)
    squares = jnp.sum(
        exchange(half_squares, ("seq", "mp"), SEQ_SIZE * MP_SIZE, 1, size * MP_SIZE), axis=0
    )
    return gather_digit(current, stride, size), squares


def merge_stack(stack):
    member_max = stack[..., HD]
    highest = jnp.max(member_max, axis=0)
    scale = jnp.exp(member_max - highest[None])
    totals = jnp.sum(stack[..., HD + 1] * scale, axis=0)
    running = jnp.sum(stack[..., :HD] * scale[..., None], axis=0)
    return jnp.concatenate([running, highest[..., None], totals[..., None]], axis=-1)


def feature_sums(squares):
    return jnp.sum(exchange(squares, "mp", MP_SIZE, 1, MP_SIZE), axis=0)


def inverse_rms(square_total):
    return lax.rsqrt(square_total / D + epsilon)[:, None]


def local(
    states,
    query_weight,
    key_weight,
    value_weight,
    output_weight,
    gate_weight,
    up_weight,
    down_weight,
    query_gain,
    key_gain,
    attention_gain,
    feedforward_gain,
    key_cache,
    value_cache,
    lengths,
    page_owner,
    page_index,
):
    local_width = query_weight.shape[1]
    local_heads = local_width // HD
    rows = STEPS * R
    score_scale = HD ** (-0.5)
    token_rows = states.reshape(rows, local_width)
    positions = (lengths[None, :] + jnp.arange(STEPS, dtype=jnp.int32)[:, None]).reshape(rows)

    sliced = seq_columns(token_rows, query_weight.shape[0])
    summed = seq_total(
        jnp.concatenate(
            [
                jnp.dot(sliced, query_weight, preferred_element_type=jnp.float32),
                jnp.dot(sliced, key_weight, preferred_element_type=jnp.float32),
                jnp.dot(sliced, value_weight, preferred_element_type=jnp.float32),
            ],
            axis=1,
        )
    )
    query_raw = summed[:, :local_width]
    key_raw = summed[:, local_width : 2 * local_width]
    value_raw = summed[:, 2 * local_width :]
    squares = feature_sums(
        jnp.stack([jnp.sum(query_raw * query_raw, axis=1), jnp.sum(key_raw * key_raw, axis=1)], axis=1)
    )
    queries = rotary(
        (query_raw * inverse_rms(squares[:, 0]) * query_gain).reshape(rows, local_heads, HD), positions
    ).astype(jnp.bfloat16)
    new_keys = rotary(
        (key_raw * inverse_rms(squares[:, 1]) * key_gain).reshape(rows, local_heads, HD), positions
    ).astype(jnp.bfloat16)
    new_values = value_raw.astype(jnp.bfloat16).reshape(rows, local_heads, HD)

    pages = key_cache.shape[0]
    tokens = pages * PAGE
    keys = key_cache.reshape(tokens, local_width)
    values = value_cache.reshape(tokens, local_width)
    token_owner = jnp.repeat(page_owner, PAGE)
    token_spot = (page_index[:, None] * PAGE + jnp.arange(PAGE, dtype=jnp.int32)[None, :]).reshape(tokens)
    validity = (token_owner[None, :] == jnp.arange(R, dtype=jnp.int32)[:, None]) & (
        token_spot[None, :] < lengths[:, None]
    )
    head_of_feature = jnp.arange(local_width, dtype=jnp.int32) // HD
    flat_queries = queries.reshape(rows, local_width)
    block_queries = jnp.where(
        head_of_feature[None, None, :] == jnp.arange(local_heads, dtype=jnp.int32)[:, None, None],
        flat_queries[None],
        jnp.zeros((), jnp.bfloat16),
    ).reshape(local_heads * rows, local_width)
    scores = lax.dot_general(
        block_queries, keys, (((1,), (1,)), ((), ())), preferred_element_type=jnp.float32
    ).reshape(local_heads, STEPS, R, tokens) * score_scale
    valid = validity[None, None]
    masked = jnp.where(valid, scores, very_low)
    maxima = jnp.max(masked, axis=3)
    weights = jnp.where(valid, jnp.exp(masked - maxima[..., None]), 0.0)
    totals = jnp.sum(weights, axis=3).reshape(local_heads, rows)
    maxima = maxima.reshape(local_heads, rows)
    all_heads = lax.dot_general(
        values,
        weights.astype(jnp.bfloat16).reshape(local_heads * rows, tokens),
        (((0,), (1,)), ((), ())),
        preferred_element_type=jnp.float32,
    ).reshape(local_heads, HD, local_heads, rows)
    running = jnp.stack([all_heads[h, :, h].T for h in range(local_heads)])

    seq = lax.axis_index("seq")
    slice_width = local_width // SEQ_SIZE
    per_head = HD // slice_width
    send = jnp.concatenate(
        [
            running.reshape(local_heads, rows, per_head, slice_width).transpose(0, 2, 1, 3),
            jnp.broadcast_to(maxima[:, None, :, None], (local_heads, per_head, rows, 1)),
            jnp.broadcast_to(totals[:, None, :, None], (local_heads, per_head, rows, 1)),
        ],
        axis=3,
    ).reshape(SEQ_SIZE, rows, slice_width + 2)
    sources = lax.all_to_all(send, "seq", 0, 0, tiled=True)
    source_max = sources[..., slice_width]
    cache_highest = jnp.max(source_max, axis=0)
    scale = jnp.exp(source_max - cache_highest[None])
    cache_totals = jnp.sum(sources[..., slice_width + 1] * scale, axis=0)
    cache_running = jnp.sum(sources[..., :slice_width] * scale[..., None], axis=0)

    head = seq // per_head
    offset = (seq % per_head) * slice_width
    q4 = lax.dynamic_index_in_dim(queries, head, 1, keepdims=False).reshape(STEPS, R, HD)
    k4 = lax.dynamic_index_in_dim(new_keys, head, 1, keepdims=False).reshape(STEPS, R, HD)
    v4 = lax.dynamic_slice_in_dim(
        lax.dynamic_index_in_dim(new_values, head, 1, keepdims=False), offset, slice_width, 1
    ).reshape(STEPS, R, slice_width)
    fresh_scores = jnp.einsum("srd,trd->srt", q4, k4, preferred_element_type=jnp.float32) * score_scale
    allowed = (jnp.arange(STEPS)[None, :] <= jnp.arange(STEPS)[:, None])[:, None, :]
    fresh_scores = jnp.where(allowed, fresh_scores, very_low)
    cache_highest = cache_highest.reshape(STEPS, R)
    highest = jnp.maximum(cache_highest, jnp.max(fresh_scores, axis=-1))
    fresh_weights = jnp.where(allowed, jnp.exp(fresh_scores - highest[..., None]), 0.0)
    factor = jnp.exp(cache_highest - highest)
    final_totals = cache_totals.reshape(STEPS, R) * factor + jnp.sum(fresh_weights, axis=-1)
    final_running = cache_running.reshape(STEPS, R, slice_width) * factor[..., None] + jnp.einsum(
        "srt,trd->srd", fresh_weights.astype(jnp.bfloat16), v4, preferred_element_type=jnp.float32
    )
    attended = (final_running / final_totals[..., None]).astype(jnp.bfloat16).reshape(rows, slice_width)

    sliced = deliver(attended, output_weight.shape[0], local_width)
    attention_out, attention_squares = seq_total_and_squares(
        jnp.dot(sliced, output_weight, preferred_element_type=jnp.float32)
    )
    hidden = (
        token_rows.astype(jnp.float32) + attention_out * inverse_rms(attention_squares) * attention_gain
    ).astype(jnp.bfloat16)

    hidden_all = jnp.transpose(exchange(hidden, "mp", MP_SIZE, 1, MP_SIZE), (1, 0, 2)).reshape(
        rows, MP_SIZE * local_width
    )
    units = gate_weight.shape[1] // SEQ_SIZE
    both = full_rows(
        jnp.concatenate(
            [
                gate_weight.reshape(-1, SEQ_SIZE, units),
                up_weight.reshape(-1, SEQ_SIZE, units),
            ],
            axis=2,
        ).reshape(gate_weight.shape[0], 2 * gate_weight.shape[1])
    )
    gate = jnp.dot(hidden_all, both[:, :units], preferred_element_type=jnp.float32)
    up_part = jnp.dot(hidden_all, both[:, units:], preferred_element_type=jnp.float32)
    active = (jax.nn.silu(gate) * up_part).astype(jnp.bfloat16)
    active_cols = deliver(active, down_weight.shape[0], gate_weight.shape[1])
    mlp_out, mlp_squares = seq_total_and_squares(
        jnp.dot(active_cols, down_weight, preferred_element_type=jnp.float32)
    )
    decoded = (
        hidden.astype(jnp.float32) + mlp_out * inverse_rms(mlp_squares) * feedforward_gain
    ).astype(jnp.bfloat16)
    return decoded.reshape(STEPS, R, local_width)


def solution(mesh):
    global SEQ_SIZE, MP_SIZE, SEQ_FACTORS
    SEQ_SIZE = mesh.shape["seq"]
    MP_SIZE = mesh.shape["mp"]
    factors = []
    left = SEQ_SIZE // MP_SIZE
    if left % 2 == 0:
        factors.append(2)
        left //= 2
    while left % 4 == 0:
        factors.append(4)
        left //= 4
    if left > 1:
        factors.append(left)
    factors.append(MP_SIZE)
    SEQ_FACTORS = tuple(factors)
    in_specs = (
        P(None, None, "mp"),
        P("seq", "mp"),
        P("seq", "mp"),
        P("seq", "mp"),
        P("seq", "mp"),
        P("seq", "mp"),
        P("seq", "mp"),
        P("seq", "mp"),
        P("mp"),
        P("mp"),
        P("mp"),
        P("mp"),
        P("seq", None, "mp"),
        P("seq", None, "mp"),
        P(),
        P("seq"),
        P("seq"),
    )
    out_specs = P(None, None, "mp")
    return jax.shard_map(local, mesh=mesh, in_specs=in_specs, out_specs=out_specs, check_vma=False)
```
